32 devices in a mesh: group: 2 (over x), blk: 16 (over z, y, core).
Axes of the slice: x: 2, y: 2, z: 4, core: 2. Of those that a mesh axis runs over, the one named last changes fastest.
Arguments:
- latents: bfloat16 [32, 32, 8, 512], P(('group', 'blk')), parts along dimension 0, may hold values from -6 to 6
- norm_gain: float32 [512], replicated, may hold values from 0.1 to 1.9
- metric: float32 [16, 9, 32, 8], P('blk'), may hold values from 0.1 to 1
- w_query: bfloat16 [512, 512], replicated, may hold values from -1 to 1
- w_key: bfloat16 [512, 512], replicated, may hold values from -1 to 1
- w_value: bfloat16 [512, 512], replicated, may hold values from -0.25 to 0.25
- w_output: bfloat16 [512, 512], replicated, may hold values from -0.25 to 0.25
- seam_table: int32 [16, 2, 3], P('blk'), may hold values from 0 to 15, as said below
Outputs:
- updated: bfloat16 [32, 32, 8, 512], P(('group', 'blk')), parts along dimension 0
The draws below stay inside these ranges and needn't reach their ends.
There are 2 independent parts, one for each index of `group`. The reference program is written for one: setup_inputs(seed, part) draws one part's arguments, and reference() takes and returns one part's arrays. A program takes and returns all parts, laid end to end along the dimension named above; an argument that names none is the same for every part. Nothing has to cross between parts.
Inputs may be any that keep to these rules, and one draw needn't show every extreme that they name: `seam_table`: entry [d, e] names the source tile, the source edge (0 or 1) and the orientation code (0 to 3) of the rim placed beyond edge e of tile d. The pairs (source tile, source edge) of all entries are distinct.
All inputs are finite; a program needn't handle non-finite values.
Results may differ from the reference program's by a relative error of at most 0.0094.
Values may be sent and summed in bfloat16 or wider, within the bound.
No kernel may reach another device: no remote copies, remote signals or barrier semaphores. Data moves between devices by JAX's collectives and lax.ppermute only.
A program may use at most 192 MiB of HBM per device.

```python
import math
import jax
import jax.numpy as jnp
from jax import lax

C = 512
HEADS = 8
RADIUS = 3
TH = 32
TW = 8
TILES = 16


def query_key_parts(key):
    base = jax.random.fold_in(key, 11)
    own_query = jax.random.truncated_normal(jax.random.fold_in(base, 2), -4.0, 4.0, (C, C), jnp.float32)
    own_key = jax.random.truncated_normal(jax.random.fold_in(base, 3), -4.0, 4.0, (C, C), jnp.float32)
    return (own_query, own_key)


def draw_w_query(key, part):
    own_query, own_key = query_key_parts(key)
    factor = C ** (-0.5)
    mixed = own_query
    return jnp.clip(mixed * factor, -1.0, 1.0).astype(jnp.bfloat16)


def draw_w_key(key, part):
    own_query, own_key = query_key_parts(key)
    factor = C ** (-0.5)
    mixed = own_key
    return jnp.clip(mixed * factor, -1.0, 1.0).astype(jnp.bfloat16)


def draw_seam_table(key, part):
    rim_order = jax.random.permutation(jax.random.fold_in(key, 21), 2 * TILES).astype(jnp.int32)
    rim_pairs = rim_order.reshape(TILES, 2)
    source_tile = rim_pairs // 2
    source_edge = rim_pairs % 2
    orient = jax.random.randint(jax.random.fold_in(key, 22), (TILES, 2), 0, 4, jnp.int32)
    return jnp.stack([source_tile, source_edge, orient], axis=-1).astype(jnp.int32)


def block_scale(key, shape, pieces, smallest, high):
    loudness = 1.0
    for position, shards_of in pieces:
        draws = jax.random.uniform(jax.random.fold_in(jax.random.fold_in(key, 6), position), (shards_of,), jnp.float32, smallest / len(pieces), high / len(pieces))
        loudness = loudness * jnp.repeat(jnp.exp(draws), shape[position] // shards_of).reshape((-1,) + (1,) * (len(shape) - 1 - position))
    return loudness


def scatter_about(key, shape, deviation, bound, cuts=(), kind=jnp.bfloat16):
    entries = deviation * jax.random.normal(key, shape, jnp.float32)
    if cuts:
        entries = entries * block_scale(key, shape, cuts, -0.22, 0.18)
    return jnp.clip(entries, -bound, bound).astype(kind)


def setup_inputs(seed: int = 0, part: int = 0) -> dict:
    arg_keys = jax.random.split(jax.random.key(seed), 9)
    own_keys = jax.random.split(jax.random.fold_in(arg_keys[8], part), 9)
    latents = scatter_about(own_keys[0], (TILES, TH, TW, C), 1.0, 6.0, ((0, 16),))
    norm_gain = jnp.clip(1.0 + 0.18 * jax.random.normal(arg_keys[1], (C,), jnp.float32), 0.1, 1.9)
    metric = jnp.clip(jnp.exp(math.log(1.0) - 2.3025851 * jax.random.uniform(arg_keys[2], (TILES, 9, TH, TW), jnp.float32) ** block_scale(arg_keys[2], (TILES, 9, TH, TW), ((0, 16),), -0.2, 0.2)), 0.1, 1.0)
    w_query = draw_w_query(jax.random.fold_in(arg_keys[8], 71), part)
    w_key = draw_w_key(jax.random.fold_in(arg_keys[8], 71), part)
    w_value = scatter_about(arg_keys[5], (C, C), C ** -0.5, 0.25)
    w_output = scatter_about(arg_keys[6], (C, C), C ** -0.5, 0.25)
    seam_table = draw_seam_table(jax.random.fold_in(arg_keys[8], 71), part)
    return dict(latents=latents, norm_gain=norm_gain, metric=metric, w_query=w_query, w_key=w_key, w_value=w_value, w_output=w_output, seam_table=seam_table)


def normalize(latents, norm_gain):
    values = latents.astype(jnp.float32)
    factor = lax.rsqrt(lax.optimization_barrier(jnp.mean(values * values, axis=-1, keepdims=True)) + 1e-05)
    return (values * factor * norm_gain).astype(jnp.bfloat16)

def extend_field(grid_field, seam_table, margin):
    west_side = jnp.roll(grid_field, 1, axis=0)[:, :, -margin:]
    east_side = jnp.roll(grid_field, -1, axis=0)[:, :, :margin]
    widened = jnp.concatenate([west_side, grid_field, east_side], axis=2)
    edge_rims = jnp.stack([widened[:, :margin], widened[:, -margin:]], axis=1)
    arrived = edge_rims[seam_table[:, :, 0], seam_table[:, :, 1]]
    orient = seam_table[:, :, 2]
    flip_along = (orient % 2 == 1)[:, :, None, None, None]
    arrived = jnp.where(flip_along, arrived[:, :, :, ::-1], arrived)
    flip_across = (orient // 2 == 1)[:, :, None, None, None]
    arrived = jnp.where(flip_across, arrived[:, :, ::-1], arrived)
    return jnp.concatenate([arrived[:, 0], widened, arrived[:, 1]], axis=1)

def smooth(padded, metric):
    rows, cols = (metric.shape[-2], metric.shape[-1])
    total = jnp.zeros(padded.shape[:-3] + (rows, cols, padded.shape[-1]), jnp.float32)
    for stencil in range(9):
        row_off = stencil // 3
        col_off = stencil % 3
        total = total + metric[..., stencil, :, :, None] * padded[..., row_off:row_off + rows, col_off:col_off + cols, :].astype(jnp.float32)
    return total.astype(jnp.bfloat16)

def project(values, weight):
    shape = values.shape
    flat = values.reshape(-1, shape[-1])
    return jnp.dot(flat, weight, preferred_element_type=jnp.float32).astype(jnp.bfloat16).reshape(shape[:-1] + (weight.shape[1],))

def window_attention(query, keys, vals):
    rows, cols, channels = query.shape
    head_size = channels // HEADS
    query_heads = query.reshape(rows, cols, HEADS, head_size).astype(jnp.float32)
    span = 2 * RADIUS + 1
    scores = []
    for row_off in range(span):
        for col_off in range(span):
            key_heads = keys[row_off:row_off + rows, col_off:col_off + cols].reshape(rows, cols, HEADS, head_size).astype(jnp.float32)
            scores.append(jnp.einsum('ijhd,ijhd->ijh', query_heads, key_heads) * head_size ** (-0.5))
    stacked = jnp.stack(scores)
    row_max = lax.optimization_barrier(jnp.max(stacked, axis=0, keepdims=True))
    exp_scores = jnp.exp(stacked - row_max)
    weights = (exp_scores / lax.optimization_barrier(jnp.sum(exp_scores, axis=0, keepdims=True))).astype(jnp.bfloat16)
    total = jnp.zeros((rows, cols, HEADS, head_size), jnp.float32)
    for row_off in range(span):
        for col_off in range(span):
            value_heads = vals[row_off:row_off + rows, col_off:col_off + cols].reshape(rows, cols, HEADS, head_size).astype(jnp.float32)
            total = total + weights[row_off * span + col_off].astype(jnp.float32)[..., None] * value_heads
    return total.reshape(rows, cols, channels).astype(jnp.bfloat16)

def attend_tile(triple):
    return window_attention(triple[0], triple[1], triple[2])

def reference(latents, norm_gain, metric, w_query, w_key, w_value, w_output, seam_table):
    normed = normalize(latents, norm_gain)
    padded = extend_field(normed, seam_table, 1)
    smoothed = smooth(padded, metric)
    query = project(smoothed, w_query)
    keys = project(smoothed, w_key)
    values = project(smoothed, w_value)
    key_pad = extend_field(keys, seam_table, RADIUS)
    value_pad = extend_field(values, seam_table, RADIUS)
    attended = lax.map(attend_tile, (query, key_pad, value_pad))
    mixed = jnp.dot(attended.reshape(-1, attended.shape[-1]), w_output, preferred_element_type=jnp.float32)
    return (latents.astype(jnp.float32) + mixed.reshape(latents.shape)).astype(jnp.bfloat16)
```

```python
import jax
import jax.numpy as jnp
from jax import lax
from jax.sharding import PartitionSpec as P
from jax.experimental import pallas as pl
from jax.experimental.pallas import tpu as pltpu

HEADS = 8
RADIUS = 3


def padded_2(array, sides, width):
    for axis, dim in sides:
        count, length = (lax.axis_size(axis), array.shape[dim])
        up = [(i, (i + 1) % count) for i in range(count)]
        down = [(j, i) for i, j in up]
        last = lax.slice_in_dim(array, length - width, length, axis=dim)
        first = lax.slice_in_dim(array, 0, width, axis=dim)
        before = lax.ppermute(last, axis, up)
        after = lax.ppermute(first, axis, down)
        array = jnp.concatenate([before, array, after], axis=dim)
    return array


def normalize(latents, norm_gain):
    values = latents.astype(jnp.float32)
    factor = lax.rsqrt(jnp.mean(values * values, axis=-1, keepdims=True) + 1e-05)
    return (values * factor * norm_gain).astype(jnp.bfloat16)


def pick_rims(seam_rows, piece):
    number = piece.shape[0]
    tile_ids = jnp.arange(number, dtype=jnp.int32)
    tile_hit = tile_ids[None, :] == seam_rows[:, 0:1]
    edge_hit = jnp.arange(2, dtype=jnp.int32)[None, :] == seam_rows[:, 1:2]
    chosen = (tile_hit[:, :, None] & edge_hit[:, None, :]).astype(piece.dtype)
    return jnp.einsum("enf,nfrwc->erwc", chosen, piece, preferred_element_type=jnp.float32)


def edge_rows(widened, margin):
    return jnp.stack([widened[:, :margin], widened[:, -margin:]], axis=1)


def orient_rims(received, seam_pair):
    arrived = received.astype(jnp.bfloat16)
    orient = seam_pair[:, 2]
    flip_along = (orient % 2 == 1)[:, None, None, None]
    arrived = jnp.where(flip_along, arrived[:, :, ::-1], arrived)
    flip_across = (orient // 2 == 1)[:, None, None, None]
    return jnp.where(flip_across, arrived[:, ::-1], arrived)


def place_rims(widened, received, seam_pair):
    arrived = orient_rims(received, seam_pair)
    return jnp.concatenate([arrived[0], widened, arrived[1]], axis=0)


def smooth(padded, metric):
    rows, cols = (metric.shape[-2], metric.shape[-1])
    total = jnp.zeros((rows, cols, padded.shape[-1]), jnp.float32)
    for stencil in range(9):
        row_off = stencil // 3
        col_off = stencil % 3
        total = (
            total
            + metric[stencil, :, :, None]
            * padded[row_off : row_off + rows, col_off : col_off + cols, :]
        )
    return total.astype(jnp.bfloat16)


def project(values, weight):
    shape = values.shape
    flat = values.reshape(-1, shape[-1])
    return (
        jnp.dot(flat, weight, preferred_element_type=jnp.float32)
        .astype(jnp.bfloat16)
        .reshape(shape[:-1] + (weight.shape[1],))
    )


def attention_kernel(q_ref, k_ref, v_ref, lat_ref, wo_ref, out_ref, s_ref):
    span = 2 * RADIUS + 1
    cells, channels = q_ref.shape
    rows = cells // k_ref.shape[2]
    head_size = channels // HEADS
    lanes = s_ref.shape[-1]
    c_ids = lax.broadcasted_iota(jnp.int32, (channels, lanes), 0) // head_size
    h_ids = lax.broadcasted_iota(jnp.int32, (channels, lanes), 1)
    head_sum = (c_ids == h_ids).astype(jnp.bfloat16)
    h_ids2 = lax.broadcasted_iota(jnp.int32, (lanes, channels), 0)
    c_ids2 = lax.broadcasted_iota(jnp.int32, (lanes, channels), 1) // head_size
    head_spread = (c_ids2 == h_ids2).astype(jnp.bfloat16)
    scale = head_size ** (-0.5)
    q = q_ref[...].astype(jnp.float32)

    def window(ref, o):
        a = o // span
        b = o % span
        return ref[b, pl.ds(a, rows)].reshape(cells, channels)

    def score_step(o, running):
        prod = q * window(k_ref, o)
        hi = prod.astype(jnp.bfloat16)
        lo = (prod - hi.astype(jnp.float32)).astype(jnp.bfloat16)
        s = (
            jnp.dot(hi, head_sum, preferred_element_type=jnp.float32)
            + jnp.dot(lo, head_sum, preferred_element_type=jnp.float32)
        ) * scale
        s_ref[o] = s
        return jnp.maximum(running, s)

    top = lax.fori_loop(
        0, span * span, score_step, jnp.full((cells, lanes), -jnp.inf, jnp.float32)
    )

    def exp_step(o, total):
        e = jnp.exp(s_ref[o] - top)
        s_ref[o] = e
        return total + e

    denom = lax.fori_loop(0, span * span, exp_step, jnp.zeros((cells, lanes), jnp.float32))

    def value_step(o, acc):
        w = (s_ref[o] / denom).astype(jnp.bfloat16)
        wide = jnp.dot(w, head_spread, preferred_element_type=jnp.float32)
        return acc + wide * window(v_ref, o)

    acc = lax.fori_loop(
        0, span * span, value_step, jnp.zeros((cells, channels), jnp.float32)
    )
    attended = acc.astype(jnp.bfloat16)
    mixed = jnp.dot(attended, wo_ref[...], preferred_element_type=jnp.float32)
    out_ref[...] = (lat_ref[...].astype(jnp.float32) + mixed).astype(out_ref.dtype)


def column_shifts(padded, cols):
    span = padded.shape[1] - cols + 1
    return jnp.stack([padded[:, b : b + cols] for b in range(span)]).astype(jnp.float32)


def attend_and_mix(query, key_pad, value_pad, own_tile, w_output):
    rows, cols, channels = own_tile.shape
    cells = rows * cols
    span = 2 * RADIUS + 1
    vmem = pl.BlockSpec(memory_space=pltpu.VMEM)
    out = pl.pallas_call(
        attention_kernel,
        out_shape=jax.ShapeDtypeStruct((cells, channels), own_tile.dtype),
        in_specs=[vmem] * 5,
        out_specs=vmem,
        scratch_shapes=[pltpu.VMEM((span * span, cells, 128), jnp.float32)],
        compiler_params=pltpu.CompilerParams(vmem_limit_bytes=60 * 1024 * 1024),
    )(
        query.reshape(cells, channels),
        column_shifts(key_pad, cols),
        column_shifts(value_pad, cols),
        own_tile.reshape(cells, channels),
        w_output,
    )
    return out.reshape(rows, cols, channels)


def local(latents, norm_gain, metric, w_query, w_key, w_value, w_output, seam_table):
    own_tile = latents[0]
    channels = own_tile.shape[-1]
    normed = normalize(own_tile, norm_gain)
    margin = 1
    seam_rows = seam_table[0]
    widened = padded_2(normed[None], (("blk", 2),), margin)
    received = pick_rims(
        seam_rows, lax.all_gather(edge_rows(widened, 1), "blk", axis=0, tiled=True)
    )
    padded = place_rims(widened[0], received, seam_rows)
    smoothed = smooth(padded, metric[0])
    query = project(smoothed, w_query)
    field_wide = padded_2(smoothed[None], (("blk", 2),), RADIUS)
    field_got = pick_rims(
        seam_rows, lax.all_gather(edge_rows(field_wide, RADIUS), "blk", axis=0, tiled=True)
    )
    field_pad = place_rims(field_wide[0], field_got, seam_rows)
    key_pad = project(field_pad, w_key)
    value_pad = project(field_pad, w_value)
    return attend_and_mix(query, key_pad, value_pad, own_tile, w_output)[None]


def solution(mesh):
    return jax.shard_map(
        local,
        mesh=mesh,
        in_specs=(
            P(("group", "blk"), None, None, None),
            P(),
            P("blk", None, None, None),
            P(),
            P(),
            P(),
            P(),
            P("blk", None, None),
        ),
        out_specs=P(("group", "blk"), None, None, None),
        check_vma=False,
    )
```

```python
import jax
import jax.numpy as jnp
from jax import lax
from jax.sharding import PartitionSpec as P
from jax.experimental import pallas as pl
from jax.experimental.pallas import tpu as pltpu

HEADS = 8
RADIUS = 3


def padded_2(array, sides, width):
    for axis, dim in sides:
        count, length = (lax.axis_size(axis), array.shape[dim])
        up = [(i, (i + 1) % count) for i in range(count)]
        down = [(j, i) for i, j in up]
        last = lax.slice_in_dim(array, length - width, length, axis=dim)
        first = lax.slice_in_dim(array, 0, width, axis=dim)
        before = lax.ppermute(last, axis, up)
        after = lax.ppermute(first, axis, down)
        array = jnp.concatenate([before, array, after], axis=dim)
    return array


def normalize(latents, norm_gain):
    values = latents.astype(jnp.float32)
    factor = lax.rsqrt(jnp.mean(values * values, axis=-1, keepdims=True) + 1e-05)
    return (values * factor * norm_gain).astype(jnp.bfloat16)


def pick_rims(seam_rows, piece):
    number = piece.shape[0]
    tile_ids = jnp.arange(number, dtype=jnp.int32)
    tile_hit = tile_ids[None, :] == seam_rows[:, 0:1]
    edge_hit = jnp.arange(2, dtype=jnp.int32)[None, :] == seam_rows[:, 1:2]
    chosen = (tile_hit[:, :, None] & edge_hit[:, None, :]).astype(piece.dtype)
    return jnp.einsum("enf,nfrwc->erwc", chosen, piece, preferred_element_type=jnp.float32)


def edge_rows(widened, margin):
    return jnp.stack([widened[:, :margin], widened[:, -margin:]], axis=1)


def orient_rims(received, seam_pair):
    arrived = received.astype(jnp.bfloat16)
    orient = seam_pair[:, 2]
    flip_along = (orient % 2 == 1)[:, None, None, None]
    arrived = jnp.where(flip_along, arrived[:, :, ::-1], arrived)
    flip_across = (orient // 2 == 1)[:, None, None, None]
    return jnp.where(flip_across, arrived[:, ::-1], arrived)


def place_rims(widened, received, seam_pair):
    arrived = orient_rims(received, seam_pair)
    return jnp.concatenate([arrived[0], widened, arrived[1]], axis=0)


def smooth(padded, metric):
    rows, cols = (metric.shape[-2], metric.shape[-1])
    total = jnp.zeros((rows, cols, padded.shape[-1]), jnp.float32)
    for stencil in range(9):
        row_off = stencil // 3
        col_off = stencil % 3
        total = (
            total
            + metric[stencil, :, :, None]
            * padded[row_off : row_off + rows, col_off : col_off + cols, :]
        )
    return total.astype(jnp.bfloat16)


def project(values, weight):
    shape = values.shape
    flat = values.reshape(-1, shape[-1])
    return (
        jnp.dot(flat, weight, preferred_element_type=jnp.float32)
        .astype(jnp.bfloat16)
        .reshape(shape[:-1] + (weight.shape[1],))
    )


def attention_kernel(q_ref, k_ref, v_ref, lat_ref, wo_ref, out_ref, s_ref):
    span = 2 * RADIUS + 1
    cells, channels = q_ref.shape
    rows = cells // k_ref.shape[2]
    head_size = channels // HEADS
    lanes = s_ref.shape[-1]
    c_ids = lax.broadcasted_iota(jnp.int32, (channels, lanes), 0) // head_size
    h_ids = lax.broadcasted_iota(jnp.int32, (channels, lanes), 1)
    head_sum = (c_ids == h_ids).astype(jnp.bfloat16)
    h_ids2 = lax.broadcasted_iota(jnp.int32, (lanes, channels), 0)
    c_ids2 = lax.broadcasted_iota(jnp.int32, (lanes, channels), 1) // head_size
    head_spread = (c_ids2 == h_ids2).astype(jnp.bfloat16)
    scale = head_size ** (-0.5)
    q = q_ref[...].astype(jnp.float32)

    def window(ref, o):
        a = o // span
        b = o % span
        return ref[b, pl.ds(a, rows)].reshape(cells, channels)

    def score_step(o, running):
        prod = q * window(k_ref, o)
        hi = prod.astype(jnp.bfloat16)
        lo = (prod - hi.astype(jnp.float32)).astype(jnp.bfloat16)
        s = (
            jnp.dot(hi, head_sum, preferred_element_type=jnp.float32)
            + jnp.dot(lo, head_sum, preferred_element_type=jnp.float32)
        ) * scale
        s_ref[o] = s
        return jnp.maximum(running, s)

    top = lax.fori_loop(
        0, span * span, score_step, jnp.full((cells, lanes), -jnp.inf, jnp.float32)
    )

    def exp_step(o, total):
        e = jnp.exp(s_ref[o] - top)
        s_ref[o] = e
        return total + e

    denom = lax.fori_loop(0, span * span, exp_step, jnp.zeros((cells, lanes), jnp.float32))

    def value_step(o, acc):
        w = (s_ref[o] / denom).astype(jnp.bfloat16)
        wide = jnp.dot(w, head_spread, preferred_element_type=jnp.float32)
        return acc + wide * window(v_ref, o)

    acc = lax.fori_loop(
        0, span * span, value_step, jnp.zeros((cells, channels), jnp.float32)
    )
    attended = acc.astype(jnp.bfloat16)
    mixed = jnp.dot(attended, wo_ref[...], preferred_element_type=jnp.float32)
    out_ref[...] = (lat_ref[...].astype(jnp.float32) + mixed).astype(out_ref.dtype)


def column_shifts(padded, cols):
    span = padded.shape[1] - cols + 1
    return jnp.stack([padded[:, b : b + cols] for b in range(span)]).astype(jnp.float32)


def attend_and_mix(query, key_pad, value_pad, own_tile, w_output):
    rows, cols, channels = own_tile.shape
    cells = rows * cols
    span = 2 * RADIUS + 1
    vmem = pl.BlockSpec(memory_space=pltpu.VMEM)
    out = pl.pallas_call(
        attention_kernel,
        out_shape=jax.ShapeDtypeStruct((cells, channels), own_tile.dtype),
        in_specs=[vmem] * 5,
        out_specs=vmem,
        scratch_shapes=[pltpu.VMEM((span * span, cells, 128), jnp.float32)],
        compiler_params=pltpu.CompilerParams(vmem_limit_bytes=60 * 1024 * 1024),
    )(
        query.reshape(cells, channels),
        column_shifts(key_pad, cols),
        column_shifts(value_pad, cols),
        own_tile.reshape(cells, channels),
        w_output,
    )
    return out.reshape(rows, cols, channels)


def smooth_batched(padded, metric):
    rows, cols = (metric.shape[-2], metric.shape[-1])
    total = jnp.zeros(padded.shape[:-3] + (rows, cols, padded.shape[-1]), jnp.float32)
    for stencil in range(9):
        row_off = stencil // 3
        col_off = stencil % 3
        total = (
            total
            + metric[..., stencil, :, :, None]
            * padded[..., row_off : row_off + rows, col_off : col_off + cols, :]
        )
    return total.astype(jnp.bfloat16)


def widen_tiles(field, margin):
    west = jnp.roll(field, 1, axis=0)[:, :, -margin:]
    east = jnp.roll(field, -1, axis=0)[:, :, :margin]
    return jnp.concatenate([west, field, east], axis=2)


def pick_all(table, edges):
    number = edges.shape[0]
    tile_hit = jnp.arange(number, dtype=jnp.int32) == table[..., 0:1]
    edge_hit = jnp.arange(2, dtype=jnp.int32) == table[..., 1:2]
    chosen = (tile_hit[..., :, None] & edge_hit[..., None, :]).astype(edges.dtype)
    got = jnp.einsum("...nf,nfrwc->...rwc", chosen, edges, preferred_element_type=jnp.float32)
    return got.astype(edges.dtype)


def local(latents, norm_gain, metric, w_query, w_key, w_value, w_output, seam_table):
    own_tile = latents[0]
    rows, cols, channels = own_tile.shape
    count = lax.axis_size("blk")
    me = lax.axis_index("blk")
    up = [(i, (i + 1) % count) for i in range(count)]
    down = [(j, i) for i, j in up]
    side = RADIUS + 1
    band = jnp.concatenate([own_tile[:side], own_tile[rows - side :]], axis=0)
    bands = lax.all_gather(band[None], "blk", axis=0, tiled=True)
    metric_all = lax.all_gather(metric, "blk", axis=0, tiled=True)
    table_all = lax.all_gather(seam_table, "blk", axis=0, tiled=True)
    west_cols = lax.ppermute(own_tile[:, cols - side :], "blk", up)
    east_cols = lax.ppermute(own_tile[:, :side], "blk", down)

    normed_bands = widen_tiles(normalize(bands, norm_gain), 1)
    edges1 = jnp.stack([normed_bands[:, 0], normed_bands[:, -1]], axis=1)[:, :, None]
    rims1 = pick_all(table_all, edges1)[:, :, 0]
    flip = (table_all[:, :, 2] % 2 == 1)[:, :, None, None]
    rims1 = jnp.where(flip, rims1[:, :, ::-1], rims1)

    top = jnp.concatenate([rims1[:, 0:1], normed_bands[:, :side]], axis=1)
    bottom = jnp.concatenate([normed_bands[:, side:], rims1[:, 1:2]], axis=1)
    sm_top = smooth_batched(top, metric_all[:, :, :RADIUS])
    sm_bottom = smooth_batched(bottom, metric_all[:, :, rows - RADIUS :])
    sm_bands = widen_tiles(jnp.concatenate([sm_top, sm_bottom], axis=1), RADIUS)
    edges3 = jnp.stack([sm_bands[:, :RADIUS], sm_bands[:, RADIUS:]], axis=1)

    normed = normalize(own_tile, norm_gain)
    west = normalize(west_cols, norm_gain)
    east = normalize(east_cols, norm_gain)
    prev = (me + count - 1) % count
    nxt = (me + 1) % count
    rims_prev = lax.dynamic_index_in_dim(rims1, prev, 0, keepdims=False)
    rims_me = lax.dynamic_index_in_dim(rims1, me, 0, keepdims=False)
    rims_next = lax.dynamic_index_in_dim(rims1, nxt, 0, keepdims=False)
    met_prev = lax.dynamic_index_in_dim(metric_all, prev, 0, keepdims=False)
    met_next = lax.dynamic_index_in_dim(metric_all, nxt, 0, keepdims=False)

    def pad_rows(body, rims, lo, hi):
        return jnp.concatenate([rims[0:1, lo:hi], body, rims[1:2, lo:hi]], axis=0)

    wide_me = jnp.concatenate([west[:, -1:], normed, east[:, :1]], axis=1)
    sm_me = smooth_batched(pad_rows(wide_me, rims_me, 0, cols + 2), metric[0])
    wide_prev = jnp.concatenate([west, normed[:, :1]], axis=1)
    sm_prev = smooth_batched(
        pad_rows(wide_prev, rims_prev, cols - RADIUS, cols + 2), met_prev[:, :, cols - RADIUS :]
    )
    wide_next = jnp.concatenate([normed[:, -1:], east], axis=1)
    sm_next = smooth_batched(pad_rows(wide_next, rims_next, 0, RADIUS + 2), met_next[:, :, :RADIUS])
    field_wide = jnp.concatenate([sm_prev, sm_me, sm_next], axis=1)

    seam_rows = seam_table[0]
    field_got = pick_all(seam_rows, edges3)
    field_pad = place_rims(field_wide, field_got, seam_rows)
    query = project(sm_me, w_query)
    key_pad = project(field_pad, w_key)
    value_pad = project(field_pad, w_value)
    return attend_and_mix(query, key_pad, value_pad, own_tile, w_output)[None]


def solution(mesh):
    return jax.shard_map(
        local,
        mesh=mesh,
        in_specs=(
            P(("group", "blk"), None, None, None),
            P(),
            P("blk", None, None, None),
            P(),
            P(),
            P(),
            P(),
            P("blk", None, None),
        ),
        out_specs=P(("group", "blk"), None, None, None),
        check_vma=False,
    )
```

```python
import jax
import jax.numpy as jnp
from jax import lax
from jax.sharding import PartitionSpec as P
from jax.experimental import pallas as pl
from jax.experimental.pallas import tpu as pltpu

HEADS = 8
RADIUS = 3


def padded_2(array, sides, width):
    for axis, dim in sides:
        count, length = (lax.axis_size(axis), array.shape[dim])
        up = [(i, (i + 1) % count) for i in range(count)]
        down = [(j, i) for i, j in up]
        last = lax.slice_in_dim(array, length - width, length, axis=dim)
        first = lax.slice_in_dim(array, 0, width, axis=dim)
        before = lax.ppermute(last, axis, up)
        after = lax.ppermute(first, axis, down)
        array = jnp.concatenate([before, array, after], axis=dim)
    return array


def normalize(latents, norm_gain):
    values = latents.astype(jnp.float32)
    factor = lax.rsqrt(jnp.mean(values * values, axis=-1, keepdims=True) + 1e-05)
    return (values * factor * norm_gain).astype(jnp.bfloat16)


def pick_rims(seam_rows, piece):
    number = piece.shape[0]
    tile_ids = jnp.arange(number, dtype=jnp.int32)
    tile_hit = tile_ids[None, :] == seam_rows[:, 0:1]
    edge_hit = jnp.arange(2, dtype=jnp.int32)[None, :] == seam_rows[:, 1:2]
    chosen = (tile_hit[:, :, None] & edge_hit[:, None, :]).astype(piece.dtype)
    return jnp.einsum("enf,nfrwc->erwc", chosen, piece, preferred_element_type=jnp.float32)


def edge_rows(widened, margin):
    return jnp.stack([widened[:, :margin], widened[:, -margin:]], axis=1)


def orient_rims(received, seam_pair):
    arrived = received.astype(jnp.bfloat16)
    orient = seam_pair[:, 2]
    flip_along = (orient % 2 == 1)[:, None, None, None]
    arrived = jnp.where(flip_along, arrived[:, :, ::-1], arrived)
    flip_across = (orient // 2 == 1)[:, None, None, None]
    return jnp.where(flip_across, arrived[:, ::-1], arrived)


def place_rims(widened, received, seam_pair):
    arrived = orient_rims(received, seam_pair)
    return jnp.concatenate([arrived[0], widened, arrived[1]], axis=0)


def smooth(padded, metric):
    rows, cols = (metric.shape[-2], metric.shape[-1])
    total = jnp.zeros((rows, cols, padded.shape[-1]), jnp.float32)
    for stencil in range(9):
        row_off = stencil // 3
        col_off = stencil % 3
        total = (
            total
            + metric[stencil, :, :, None]
            * padded[row_off : row_off + rows, col_off : col_off + cols, :]
        )
    return total.astype(jnp.bfloat16)


def project(values, weight):
    shape = values.shape
    flat = values.reshape(-1, shape[-1])
    return (
        jnp.dot(flat, weight, preferred_element_type=jnp.float32)
        .astype(jnp.bfloat16)
        .reshape(shape[:-1] + (weight.shape[1],))
    )


def attention_kernel(q_ref, k_ref, v_ref, lat_ref, wo_ref, out_ref, s_ref):
    span = 2 * RADIUS + 1
    cells, channels = q_ref.shape
    rows = cells // k_ref.shape[2]
    head_size = channels // HEADS
    lanes = s_ref.shape[-1]
    c_ids = lax.broadcasted_iota(jnp.int32, (channels, lanes), 0) // head_size
    h_ids = lax.broadcasted_iota(jnp.int32, (channels, lanes), 1)
    head_sum = (c_ids == h_ids).astype(jnp.bfloat16)
    h_ids2 = lax.broadcasted_iota(jnp.int32, (lanes, channels), 0)
    c_ids2 = lax.broadcasted_iota(jnp.int32, (lanes, channels), 1) // head_size
    head_spread = (c_ids2 == h_ids2).astype(jnp.bfloat16)
    scale = head_size ** (-0.5)
    q = q_ref[...].astype(jnp.float32)

    def window(ref, o):
        a = o // span
        b = o % span
        return ref[b, pl.ds(a, rows)].reshape(cells, channels)

    def score_step(o, running):
        prod = q * window(k_ref, o)
        hi = prod.astype(jnp.bfloat16)
        lo = (prod - hi.astype(jnp.float32)).astype(jnp.bfloat16)
        s = (
            jnp.dot(hi, head_sum, preferred_element_type=jnp.float32)
            + jnp.dot(lo, head_sum, preferred_element_type=jnp.float32)
        ) * scale
        s_ref[o] = s
        return jnp.maximum(running, s)

    top = lax.fori_loop(
        0, span * span, score_step, jnp.full((cells, lanes), -jnp.inf, jnp.float32)
    )

    def exp_step(o, total):
        e = jnp.exp(s_ref[o] - top)
        s_ref[o] = e
        return total + e

    denom = lax.fori_loop(0, span * span, exp_step, jnp.zeros((cells, lanes), jnp.float32))

    def value_step(o, acc):
        w = (s_ref[o] / denom).astype(jnp.bfloat16)
        wide = jnp.dot(w, head_spread, preferred_element_type=jnp.float32)
        return acc + wide * window(v_ref, o)

    acc = lax.fori_loop(
        0, span * span, value_step, jnp.zeros((cells, channels), jnp.float32)
    )
    attended = acc.astype(jnp.bfloat16)
    mixed = jnp.dot(attended, wo_ref[...], preferred_element_type=jnp.float32)
    out_ref[...] = (lat_ref[...].astype(jnp.float32) + mixed).astype(out_ref.dtype)


def column_shifts(padded, cols):
    span = padded.shape[1] - cols + 1
    return jnp.stack([padded[:, b : b + cols] for b in range(span)]).astype(jnp.float32)


def attend_and_mix(query, key_pad, value_pad, own_tile, w_output):
    rows, cols, channels = own_tile.shape
    cells = rows * cols
    span = 2 * RADIUS + 1
    vmem = pl.BlockSpec(memory_space=pltpu.VMEM)
    out = pl.pallas_call(
        attention_kernel,
        out_shape=jax.ShapeDtypeStruct((cells, channels), own_tile.dtype),
        in_specs=[vmem] * 5,
        out_specs=vmem,
        scratch_shapes=[pltpu.VMEM((span * span, cells, 128), jnp.float32)],
        compiler_params=pltpu.CompilerParams(vmem_limit_bytes=60 * 1024 * 1024),
    )(
        query.reshape(cells, channels),
        column_shifts(key_pad, cols),
        column_shifts(value_pad, cols),
        own_tile.reshape(cells, channels),
        w_output,
    )
    return out.reshape(rows, cols, channels)


def smooth_batched(padded, metric):
    rows, cols = (metric.shape[-2], metric.shape[-1])
    total = jnp.zeros(padded.shape[:-3] + (rows, cols, padded.shape[-1]), jnp.float32)
    for stencil in range(9):
        row_off = stencil // 3
        col_off = stencil % 3
        total = (
            total
            + metric[..., stencil, :, :, None]
            * padded[..., row_off : row_off + rows, col_off : col_off + cols, :]
        )
    return total.astype(jnp.bfloat16)


def widen_tiles(field, margin):
    west = jnp.roll(field, 1, axis=0)[:, :, -margin:]
    east = jnp.roll(field, -1, axis=0)[:, :, :margin]
    return jnp.concatenate([west, field, east], axis=2)


def pick_all(table, edges):
    number = edges.shape[0]
    tile_hit = jnp.arange(number, dtype=jnp.int32) == table[..., 0:1]
    edge_hit = jnp.arange(2, dtype=jnp.int32) == table[..., 1:2]
    chosen = (tile_hit[..., :, None] & edge_hit[..., None, :]).astype(edges.dtype)
    got = jnp.einsum("...nf,nfrwc->...rwc", chosen, edges, preferred_element_type=jnp.float32)
    return got.astype(edges.dtype)


def split_exact(values):
    hi = values.astype(jnp.bfloat16)
    rest = values - hi.astype(jnp.float32)
    mid = rest.astype(jnp.bfloat16)
    lo = (rest - mid.astype(jnp.float32)).astype(jnp.bfloat16)
    return jnp.stack([hi, mid, lo])


def gather_parts(band, metric, table, width):
    pieces = [band.reshape(-1), split_exact(metric).reshape(-1), table.astype(jnp.bfloat16).reshape(-1)]
    sizes = [p.size for p in pieces]
    flat = jnp.concatenate(pieces)
    total = -(-flat.size // width) * width
    flat = jnp.pad(flat, (0, total - flat.size)).reshape(1, total // width, width)
    got = lax.all_gather(flat, "blk", axis=0, tiled=True)
    count = got.shape[0]
    got = got.reshape(count, total)
    bands = got[:, : sizes[0]].reshape((count,) + band.shape)
    parts = got[:, sizes[0] : sizes[0] + sizes[1]].reshape((count, 3) + metric.shape)
    parts = parts.astype(jnp.float32)
    metric_all = parts[:, 0] + (parts[:, 1] + parts[:, 2])
    table_all = got[:, sizes[0] + sizes[1] : sum(sizes)].reshape((count,) + table.shape)
    return bands, metric_all, table_all.astype(jnp.int32)


def local(latents, norm_gain, metric, w_query, w_key, w_value, w_output, seam_table):
    own_tile = latents[0]
    rows, cols, channels = own_tile.shape
    count = lax.axis_size("blk")
    me = lax.axis_index("blk")
    up = [(i, (i + 1) % count) for i in range(count)]
    down = [(j, i) for i, j in up]
    side = RADIUS + 1
    band = jnp.concatenate([own_tile[:side], own_tile[rows - side :]], axis=0)
    bands, metric_all, table_all = gather_parts(band, metric[0], seam_table[0], channels)
    west_cols = lax.ppermute(own_tile[:, cols - side :], "blk", up)
    east_cols = lax.ppermute(own_tile[:, :side], "blk", down)

    normed_bands = widen_tiles(normalize(bands, norm_gain), 1)
    edges1 = jnp.stack([normed_bands[:, 0], normed_bands[:, -1]], axis=1)[:, :, None]
    rims1 = pick_all(table_all, edges1)[:, :, 0]
    flip = (table_all[:, :, 2] % 2 == 1)[:, :, None, None]
    rims1 = jnp.where(flip, rims1[:, :, ::-1], rims1)

    top = jnp.concatenate([rims1[:, 0:1], normed_bands[:, :side]], axis=1)
    bottom = jnp.concatenate([normed_bands[:, side:], rims1[:, 1:2]], axis=1)
    sm_top = smooth_batched(top, metric_all[:, :, :RADIUS])
    sm_bottom = smooth_batched(bottom, metric_all[:, :, rows - RADIUS :])
    sm_bands = widen_tiles(jnp.concatenate([sm_top, sm_bottom], axis=1), RADIUS)
    edges3 = jnp.stack([sm_bands[:, :RADIUS], sm_bands[:, RADIUS:]], axis=1)

    normed = normalize(own_tile, norm_gain)
    west = normalize(west_cols, norm_gain)
    east = normalize(east_cols, norm_gain)
    prev = (me + count - 1) % count
    nxt = (me + 1) % count
    rims_prev = lax.dynamic_index_in_dim(rims1, prev, 0, keepdims=False)
    rims_me = lax.dynamic_index_in_dim(rims1, me, 0, keepdims=False)
    rims_next = lax.dynamic_index_in_dim(rims1, nxt, 0, keepdims=False)
    met_prev = lax.dynamic_index_in_dim(metric_all, prev, 0, keepdims=False)
    met_next = lax.dynamic_index_in_dim(metric_all, nxt, 0, keepdims=False)

    def pad_rows(body, rims, lo, hi):
        return jnp.concatenate([rims[0:1, lo:hi], body, rims[1:2, lo:hi]], axis=0)

    wide_me = jnp.concatenate([west[:, -1:], normed, east[:, :1]], axis=1)
    sm_me = smooth_batched(pad_rows(wide_me, rims_me, 0, cols + 2), metric[0])
    wide_prev = jnp.concatenate([west, normed[:, :1]], axis=1)
    sm_prev = smooth_batched(
        pad_rows(wide_prev, rims_prev, cols - RADIUS, cols + 2), met_prev[:, :, cols - RADIUS :]
    )
    wide_next = jnp.concatenate([normed[:, -1:], east], axis=1)
    sm_next = smooth_batched(pad_rows(wide_next, rims_next, 0, RADIUS + 2), met_next[:, :, :RADIUS])
    field_wide = jnp.concatenate([sm_prev, sm_me, sm_next], axis=1)

    seam_rows = seam_table[0]
    field_got = pick_all(seam_rows, edges3)
    field_pad = place_rims(field_wide, field_got, seam_rows)
    query = project(sm_me, w_query)
    key_pad = project(field_pad, w_key)
    value_pad = project(field_pad, w_value)
    return attend_and_mix(query, key_pad, value_pad, own_tile, w_output)[None]


def solution(mesh):
    return jax.shard_map(
        local,
        mesh=mesh,
        in_specs=(
            P(("group", "blk"), None, None, None),
            P(),
            P("blk", None, None, None),
            P(),
            P(),
            P(),
            P(),
            P("blk", None, None),
        ),
        out_specs=P(("group", "blk"), None, None, None),
        check_vma=False,
    )
```

```python
import jax
import jax.numpy as jnp
from jax import lax
from jax.sharding import PartitionSpec as P
from jax.experimental import pallas as pl
from jax.experimental.pallas import tpu as pltpu

HEADS = 8
RADIUS = 3


def padded_2(array, sides, width):
    for axis, dim in sides:
        count, length = (lax.axis_size(axis), array.shape[dim])
        up = [(i, (i + 1) % count) for i in range(count)]
        down = [(j, i) for i, j in up]
        last = lax.slice_in_dim(array, length - width, length, axis=dim)
        first = lax.slice_in_dim(array, 0, width, axis=dim)
        before = lax.ppermute(last, axis, up)
        after = lax.ppermute(first, axis, down)
        array = jnp.concatenate([before, array, after], axis=dim)
    return array


def normalize(latents, norm_gain):
    values = latents.astype(jnp.float32)
    factor = lax.rsqrt(jnp.mean(values * values, axis=-1, keepdims=True) + 1e-05)
    return (values * factor * norm_gain).astype(jnp.bfloat16)


def pick_rims(seam_rows, piece):
    number = piece.shape[0]
    tile_ids = jnp.arange(number, dtype=jnp.int32)
    tile_hit = tile_ids[None, :] == seam_rows[:, 0:1]
    edge_hit = jnp.arange(2, dtype=jnp.int32)[None, :] == seam_rows[:, 1:2]
    chosen = (tile_hit[:, :, None] & edge_hit[:, None, :]).astype(piece.dtype)
    return jnp.einsum("enf,nfrwc->erwc", chosen, piece, preferred_element_type=jnp.float32)


def edge_rows(widened, margin):
    return jnp.stack([widened[:, :margin], widened[:, -margin:]], axis=1)


def orient_rims(received, seam_pair):
    arrived = received.astype(jnp.bfloat16)
    orient = seam_pair[:, 2]
    flip_along = (orient % 2 == 1)[:, None, None, None]
    arrived = jnp.where(flip_along, arrived[:, :, ::-1], arrived)
    flip_across = (orient // 2 == 1)[:, None, None, None]
    return jnp.where(flip_across, arrived[:, ::-1], arrived)


def place_rims(widened, received, seam_pair):
    arrived = orient_rims(received, seam_pair)
    return jnp.concatenate([arrived[0], widened, arrived[1]], axis=0)


def smooth(padded, metric):
    rows, cols = (metric.shape[-2], metric.shape[-1])
    total = jnp.zeros((rows, cols, padded.shape[-1]), jnp.float32)
    for stencil in range(9):
        row_off = stencil // 3
        col_off = stencil % 3
        total = (
            total
            + metric[stencil, :, :, None]
            * padded[row_off : row_off + rows, col_off : col_off + cols, :]
        )
    return total.astype(jnp.bfloat16)


def project(values, weight):
    shape = values.shape
    flat = values.reshape(-1, shape[-1])
    return (
        jnp.dot(flat, weight, preferred_element_type=jnp.float32)
        .astype(jnp.bfloat16)
        .reshape(shape[:-1] + (weight.shape[1],))
    )


def attention_kernel(q_ref, k_ref, v_ref, lat_ref, wo_ref, out_ref, att_ref):
    cells, channels = q_ref.shape
    positions = k_ref.shape[0]
    rows, cols = lat_ref.shape[0], lat_ref.shape[1]
    wide = cols + 2 * RADIUS
    span = 2 * RADIUS + 1
    head_size = channels // HEADS
    group = 128
    scale = head_size ** (-0.5)
    cell = lax.broadcasted_iota(jnp.int32, (cells, positions), 0)
    place = lax.broadcasted_iota(jnp.int32, (cells, positions), 1)
    row_gap = place // wide - cell // cols
    col_gap = place % wide - cell % cols
    valid = (row_gap >= 0) & (row_gap < span) & (col_gap >= 0) & (col_gap < span)
    lane = lax.broadcasted_iota(jnp.int32, (cells, group), 1) // head_size
    for g in range(channels // group):
        lanes = slice(g * group, (g + 1) * group)
        q_g = q_ref[:, lanes]
        k_g = k_ref[:, lanes]
        v_g = v_ref[:, lanes]
        acc = jnp.zeros((cells, group), jnp.float32)
        for part in range(group // head_size):
            q_h = jnp.where(lane == part, q_g, jnp.zeros_like(q_g))
            s = lax.dot_general(
                q_h, k_g, (((1,), (1,)), ((), ())), preferred_element_type=jnp.float32
            )
            s = jnp.where(valid, s * scale, -jnp.inf)
            top = jnp.max(s, axis=1, keepdims=True)
            e = jnp.exp(s - top)
            total = jnp.sum(e, axis=1, keepdims=True)
            w = (e / total).astype(jnp.bfloat16)
            o = jnp.dot(w, v_g, preferred_element_type=jnp.float32)
            acc = jnp.where(lane == part, o, acc)
        att_ref[:, lanes] = acc.astype(jnp.bfloat16)
    mixed = jnp.dot(att_ref[...], wo_ref[...], preferred_element_type=jnp.float32)
    lat = lat_ref[...].reshape(cells, channels)
    out_ref[...] = (lat.astype(jnp.float32) + mixed).astype(out_ref.dtype)


def attend_and_mix(query, field_pad, w_key, w_value, own_tile, w_output):
    rows, cols, channels = own_tile.shape
    cells = rows * cols
    flat = field_pad.reshape(-1, channels)
    positions = -(-flat.shape[0] // 128) * 128
    flat = jnp.pad(flat, ((0, positions - flat.shape[0]), (0, 0)))
    key_flat = project(flat, w_key)
    value_flat = project(flat, w_value)
    vmem = pl.BlockSpec(memory_space=pltpu.VMEM)
    out = pl.pallas_call(
        attention_kernel,
        out_shape=jax.ShapeDtypeStruct((cells, channels), own_tile.dtype),
        in_specs=[vmem] * 5,
        out_specs=vmem,
        scratch_shapes=[pltpu.VMEM((cells, channels), jnp.bfloat16)],
    )(query.reshape(cells, channels), key_flat, value_flat, own_tile, w_output)
    return out.reshape(rows, cols, channels)


def local(latents, norm_gain, metric, w_query, w_key, w_value, w_output, seam_table):
    own_tile = latents[0]
    channels = own_tile.shape[-1]
    normed = normalize(own_tile, norm_gain)
    margin = 1
    seam_rows = seam_table[0]
    widened = padded_2(normed[None], (("blk", 2),), margin)
    received = pick_rims(
        seam_rows, lax.all_gather(edge_rows(widened, 1), "blk", axis=0, tiled=True)
    )
    padded = place_rims(widened[0], received, seam_rows)
    smoothed = smooth(padded, metric[0])
    query = project(smoothed, w_query)
    field_wide = padded_2(smoothed[None], (("blk", 2),), RADIUS)
    field_got = pick_rims(
        seam_rows, lax.all_gather(edge_rows(field_wide, RADIUS), "blk", axis=0, tiled=True)
    )
    field_pad = place_rims(field_wide[0], field_got, seam_rows)
    return attend_and_mix(query, field_pad, w_key, w_value, own_tile, w_output)[None]


def solution(mesh):
    return jax.shard_map(
        local,
        mesh=mesh,
        in_specs=(
            P(("group", "blk"), None, None, None),
            P(),
            P("blk", None, None, None),
            P(),
            P(),
            P(),
            P(),
            P("blk", None, None),
        ),
        out_specs=P(("group", "blk"), None, None, None),
        check_vma=False,
    )
```

```python
import jax
import jax.numpy as jnp
from jax import lax
from jax.sharding import PartitionSpec as P
from jax.experimental import pallas as pl
from jax.experimental.pallas import tpu as pltpu

HEADS = 8
RADIUS = 3


def padded_2(array, sides, width):
    for axis, dim in sides:
        count, length = (lax.axis_size(axis), array.shape[dim])
        up = [(i, (i + 1) % count) for i in range(count)]
        down = [(j, i) for i, j in up]
        last = lax.slice_in_dim(array, length - width, length, axis=dim)
        first = lax.slice_in_dim(array, 0, width, axis=dim)
        before = lax.ppermute(last, axis, up)
        after = lax.ppermute(first, axis, down)
        array = jnp.concatenate([before, array, after], axis=dim)
    return array


def normalize(latents, norm_gain):
    values = latents.astype(jnp.float32)
    factor = lax.rsqrt(jnp.mean(values * values, axis=-1, keepdims=True) + 1e-05)
    return (values * factor * norm_gain).astype(jnp.bfloat16)


def pick_rims(seam_rows, piece):
    number = piece.shape[0]
    tile_ids = jnp.arange(number, dtype=jnp.int32)
    tile_hit = tile_ids[None, :] == seam_rows[:, 0:1]
    edge_hit = jnp.arange(2, dtype=jnp.int32)[None, :] == seam_rows[:, 1:2]
    chosen = (tile_hit[:, :, None] & edge_hit[:, None, :]).astype(piece.dtype)
    return jnp.einsum("enf,nfrwc->erwc", chosen, piece, preferred_element_type=jnp.float32)


def edge_rows(widened, margin):
    return jnp.stack([widened[:, :margin], widened[:, -margin:]], axis=1)


def orient_rims(received, seam_pair):
    arrived = received.astype(jnp.bfloat16)
    orient = seam_pair[:, 2]
    flip_along = (orient % 2 == 1)[:, None, None, None]
    arrived = jnp.where(flip_along, arrived[:, :, ::-1], arrived)
    flip_across = (orient // 2 == 1)[:, None, None, None]
    return jnp.where(flip_across, arrived[:, ::-1], arrived)


def place_rims(widened, received, seam_pair):
    arrived = orient_rims(received, seam_pair)
    return jnp.concatenate([arrived[0], widened, arrived[1]], axis=0)


def smooth(padded, metric):
    rows, cols = (metric.shape[-2], metric.shape[-1])
    total = jnp.zeros((rows, cols, padded.shape[-1]), jnp.float32)
    for stencil in range(9):
        row_off = stencil // 3
        col_off = stencil % 3
        total = (
            total
            + metric[stencil, :, :, None]
            * padded[row_off : row_off + rows, col_off : col_off + cols, :]
        )
    return total.astype(jnp.bfloat16)


def project(values, weight):
    shape = values.shape
    flat = values.reshape(-1, shape[-1])
    return (
        jnp.dot(flat, weight, preferred_element_type=jnp.float32)
        .astype(jnp.bfloat16)
        .reshape(shape[:-1] + (weight.shape[1],))
    )


def attention_kernel(q_ref, k_ref, v_ref, lat_ref, wo_ref, out_ref, att_ref):
    cells, channels = q_ref.shape
    positions = k_ref.shape[0]
    rows, cols = lat_ref.shape[0], lat_ref.shape[1]
    wide = cols + 2 * RADIUS
    span = 2 * RADIUS + 1
    head_size = channels // HEADS
    group = 128
    scale = head_size ** (-0.5)
    cell = lax.broadcasted_iota(jnp.int32, (cells, positions), 0)
    place = lax.broadcasted_iota(jnp.int32, (cells, positions), 1)
    row_gap = place // wide - cell // cols
    col_gap = place % wide - cell % cols
    valid = (row_gap >= 0) & (row_gap < span) & (col_gap >= 0) & (col_gap < span)
    lane = lax.broadcasted_iota(jnp.int32, (cells, group), 1) // head_size
    for g in range(channels // group):
        lanes = slice(g * group, (g + 1) * group)
        q_g = q_ref[:, lanes]
        k_g = k_ref[:, lanes]
        v_g = v_ref[:, lanes]
        acc = jnp.zeros((cells, group), jnp.float32)
        for part in range(group // head_size):
            q_h = jnp.where(lane == part, q_g, jnp.zeros_like(q_g))
            s = lax.dot_general(
                q_h, k_g, (((1,), (1,)), ((), ())), preferred_element_type=jnp.float32
            )
            s = jnp.where(valid, s * scale, -jnp.inf)
            top = jnp.max(s, axis=1, keepdims=True)
            e = jnp.exp(s - top)
            total = jnp.sum(e, axis=1, keepdims=True)
            w = (e / total).astype(jnp.bfloat16)
            o = jnp.dot(w, v_g, preferred_element_type=jnp.float32)
            acc = jnp.where(lane == part, o, acc)
        att_ref[:, lanes] = acc.astype(jnp.bfloat16)
    mixed = jnp.dot(att_ref[...], wo_ref[...], preferred_element_type=jnp.float32)
    lat = lat_ref[...].reshape(cells, channels)
    out_ref[...] = (lat.astype(jnp.float32) + mixed).astype(out_ref.dtype)


def attend_and_mix(query, field_pad, w_key, w_value, own_tile, w_output):
    rows, cols, channels = own_tile.shape
    cells = rows * cols
    flat = field_pad.reshape(-1, channels)
    positions = -(-flat.shape[0] // 128) * 128
    flat = jnp.pad(flat, ((0, positions - flat.shape[0]), (0, 0)))
    key_flat = project(flat, w_key)
    value_flat = project(flat, w_value)
    vmem = pl.BlockSpec(memory_space=pltpu.VMEM)
    out = pl.pallas_call(
        attention_kernel,
        out_shape=jax.ShapeDtypeStruct((cells, channels), own_tile.dtype),
        in_specs=[vmem] * 5,
        out_specs=vmem,
        scratch_shapes=[pltpu.VMEM((cells, channels), jnp.bfloat16)],
    )(query.reshape(cells, channels), key_flat, value_flat, own_tile, w_output)
    return out.reshape(rows, cols, channels)


def widen_tiles(field, margin):
    west = jnp.roll(field, 1, axis=0)[:, :, -margin:]
    east = jnp.roll(field, -1, axis=0)[:, :, :margin]
    return jnp.concatenate([west, field, east], axis=2)


def pick_all(table, edges):
    number = edges.shape[0]
    tile_hit = jnp.arange(number, dtype=jnp.int32) == table[..., 0:1]
    edge_hit = jnp.arange(2, dtype=jnp.int32) == table[..., 1:2]
    chosen = (tile_hit[..., :, None] & edge_hit[..., None, :]).astype(edges.dtype)
    got = jnp.einsum("...nf,nfrwc->...rwc", chosen, edges, preferred_element_type=jnp.float32)
    return got.astype(edges.dtype)


def local(latents, norm_gain, metric, w_query, w_key, w_value, w_output, seam_table):
    own_tile = latents[0]
    channels = own_tile.shape[-1]
    normed = normalize(own_tile, norm_gain)
    margin = 1
    seam_rows = seam_table[0]
    widened = padded_2(normed[None], (("blk", 2),), margin)
    rows1 = jnp.stack([normed[0], normed[-1]])
    got1 = widen_tiles(lax.all_gather(rows1[None], "blk", axis=0, tiled=True), 1)
    received = pick_all(seam_rows, got1[:, :, None])
    padded = place_rims(widened[0], received, seam_rows)
    smoothed = smooth(padded, metric[0])
    query = project(smoothed, w_query)
    field_wide = padded_2(smoothed[None], (("blk", 2),), RADIUS)
    rows3 = jnp.concatenate([smoothed[:RADIUS], smoothed[-RADIUS:]], axis=0)
    got3 = widen_tiles(lax.all_gather(rows3[None], "blk", axis=0, tiled=True), RADIUS)
    edges3 = jnp.stack([got3[:, :RADIUS], got3[:, RADIUS:]], axis=1)
    field_got = pick_all(seam_rows, edges3)
    field_pad = place_rims(field_wide[0], field_got, seam_rows)
    return attend_and_mix(query, field_pad, w_key, w_value, own_tile, w_output)[None]


def solution(mesh):
    return jax.shard_map(
        local,
        mesh=mesh,
        in_specs=(
            P(("group", "blk"), None, None, None),
            P(),
            P("blk", None, None, None),
            P(),
            P(),
            P(),
            P(),
            P("blk", None, None),
        ),
        out_specs=P(("group", "blk"), None, None, None),
        check_vma=False,
    )
```

```python
import jax
import jax.numpy as jnp
from jax import lax
from jax.sharding import PartitionSpec as P
from jax.experimental import pallas as pl
from jax.experimental.pallas import tpu as pltpu

HEADS = 8
RADIUS = 3


def padded_2(array, sides, width):
    for axis, dim in sides:
        count, length = (lax.axis_size(axis), array.shape[dim])
        up = [(i, (i + 1) % count) for i in range(count)]
        down = [(j, i) for i, j in up]
        last = lax.slice_in_dim(array, length - width, length, axis=dim)
        first = lax.slice_in_dim(array, 0, width, axis=dim)
        before = lax.ppermute(last, axis, up)
        after = lax.ppermute(first, axis, down)
        array = jnp.concatenate([before, array, after], axis=dim)
    return array


def normalize(latents, norm_gain):
    values = latents.astype(jnp.float32)
    factor = lax.rsqrt(jnp.mean(values * values, axis=-1, keepdims=True) + 1e-05)
    return (values * factor * norm_gain).astype(jnp.bfloat16)


def pick_rims(seam_rows, piece):
    number = piece.shape[0]
    tile_ids = jnp.arange(number, dtype=jnp.int32)
    tile_hit = tile_ids[None, :] == seam_rows[:, 0:1]
    edge_hit = jnp.arange(2, dtype=jnp.int32)[None, :] == seam_rows[:, 1:2]
    chosen = (tile_hit[:, :, None] & edge_hit[:, None, :]).astype(piece.dtype)
    return jnp.einsum("enf,nfrwc->erwc", chosen, piece, preferred_element_type=jnp.float32)


def edge_rows(widened, margin):
    return jnp.stack([widened[:, :margin], widened[:, -margin:]], axis=1)


def orient_rims(received, seam_pair):
    arrived = received.astype(jnp.bfloat16)
    orient = seam_pair[:, 2]
    flip_along = (orient % 2 == 1)[:, None, None, None]
    arrived = jnp.where(flip_along, arrived[:, :, ::-1], arrived)
    flip_across = (orient // 2 == 1)[:, None, None, None]
    return jnp.where(flip_across, arrived[:, ::-1], arrived)


def place_rims(widened, received, seam_pair):
    arrived = orient_rims(received, seam_pair)
    return jnp.concatenate([arrived[0], widened, arrived[1]], axis=0)


def smooth(padded, metric):
    rows, cols = (metric.shape[-2], metric.shape[-1])
    total = jnp.zeros((rows, cols, padded.shape[-1]), jnp.float32)
    for stencil in range(9):
        row_off = stencil // 3
        col_off = stencil % 3
        total = (
            total
            + metric[stencil, :, :, None]
            * padded[row_off : row_off + rows, col_off : col_off + cols, :]
        )
    return total.astype(jnp.bfloat16)


def project(values, weight):
    shape = values.shape
    flat = values.reshape(-1, shape[-1])
    return (
        jnp.dot(flat, weight, preferred_element_type=jnp.float32)
        .astype(jnp.bfloat16)
        .reshape(shape[:-1] + (weight.shape[1],))
    )


def attention_kernel(q_ref, k_ref, v_ref, lat_ref, wo_ref, out_ref, att_ref):
    cells, channels = q_ref.shape
    positions = k_ref.shape[0]
    rows, cols = lat_ref.shape[0], lat_ref.shape[1]
    wide = cols + 2 * RADIUS
    span = 2 * RADIUS + 1
    head_size = channels // HEADS
    group = 128
    scale = head_size ** (-0.5)
    cell = lax.broadcasted_iota(jnp.int32, (cells, positions), 0)
    place = lax.broadcasted_iota(jnp.int32, (cells, positions), 1)
    row_gap = place // wide - cell // cols
    col_gap = place % wide - cell % cols
    valid = (row_gap >= 0) & (row_gap < span) & (col_gap >= 0) & (col_gap < span)
    lane = lax.broadcasted_iota(jnp.int32, (cells, group), 1) // head_size
    for g in range(channels // group):
        lanes = slice(g * group, (g + 1) * group)
        q_g = q_ref[:, lanes]
        k_g = k_ref[:, lanes]
        v_g = v_ref[:, lanes]
        acc = jnp.zeros((cells, group), jnp.float32)
        for part in range(group // head_size):
            q_h = jnp.where(lane == part, q_g, jnp.zeros_like(q_g))
            s = lax.dot_general(
                q_h, k_g, (((1,), (1,)), ((), ())), preferred_element_type=jnp.float32
            )
            s = jnp.where(valid, s * scale, -jnp.inf)
            top = jnp.max(s, axis=1, keepdims=True)
            e = jnp.exp(s - top)
            total = jnp.sum(e, axis=1, keepdims=True)
            w = (e / total).astype(jnp.bfloat16)
            o = jnp.dot(w, v_g, preferred_element_type=jnp.float32)
            acc = jnp.where(lane == part, o, acc)
        att_ref[:, lanes] = acc.astype(jnp.bfloat16)
    mixed = jnp.dot(att_ref[...], wo_ref[...], preferred_element_type=jnp.float32)
    lat = lat_ref[...].reshape(cells, channels)
    out_ref[...] = (lat.astype(jnp.float32) + mixed).astype(out_ref.dtype)


def attend_and_mix(query, field_pad, w_key, w_value, own_tile, w_output):
    rows, cols, channels = own_tile.shape
    cells = rows * cols
    flat = field_pad.reshape(-1, channels)
    positions = -(-flat.shape[0] // 128) * 128
    flat = jnp.pad(flat, ((0, positions - flat.shape[0]), (0, 0)))
    key_flat = project(flat, w_key)
    value_flat = project(flat, w_value)
    vmem = pl.BlockSpec(memory_space=pltpu.VMEM)
    out = pl.pallas_call(
        attention_kernel,
        out_shape=jax.ShapeDtypeStruct((cells, channels), own_tile.dtype),
        in_specs=[vmem] * 5,
        out_specs=vmem,
        scratch_shapes=[pltpu.VMEM((cells, channels), jnp.bfloat16)],
    )(query.reshape(cells, channels), key_flat, value_flat, own_tile, w_output)
    return out.reshape(rows, cols, channels)


def widen_tiles(field, margin):
    west = jnp.roll(field, 1, axis=0)[:, :, -margin:]
    east = jnp.roll(field, -1, axis=0)[:, :, :margin]
    return jnp.concatenate([west, field, east], axis=2)


def pick_all(table, edges):
    number = edges.shape[0]
    tile_hit = jnp.arange(number, dtype=jnp.int32) == table[..., 0:1]
    edge_hit = jnp.arange(2, dtype=jnp.int32) == table[..., 1:2]
    chosen = (tile_hit[..., :, None] & edge_hit[..., None, :]).astype(edges.dtype)
    got = jnp.einsum("...nf,nfrwc->...rwc", chosen, edges, preferred_element_type=jnp.float32)
    return got.astype(edges.dtype)


def smooth_total(padded, metric):
    rows, cols = (metric.shape[-2], metric.shape[-1])
    total = jnp.zeros((rows, cols, padded.shape[-1]), jnp.float32)
    for stencil in range(9):
        row_off = stencil // 3
        col_off = stencil % 3
        total = (
            total
            + metric[stencil, :, :, None]
            * padded[row_off : row_off + rows, col_off : col_off + cols, :]
        )
    return total


def to_bf16_exact(values):
    return lax.reduce_precision(values, exponent_bits=8, mantissa_bits=7)


def split_parts(values, count):
    parts = []
    rest = values
    for _ in range(count - 1):
        head = to_bf16_exact(rest)
        parts.append(head.astype(jnp.bfloat16))
        rest = rest - head
    parts.append(rest.astype(jnp.bfloat16))
    return parts


def local(latents, norm_gain, metric, w_query, w_key, w_value, w_output, seam_table):
    own_tile = latents[0]
    rows, cols, channels = own_tile.shape
    count = lax.axis_size("blk")
    me = lax.axis_index("blk")
    seam_rows = seam_table[0]
    normed = normalize(own_tile, norm_gain)
    widened = padded_2(normed[None], (("blk", 2),), 1)[0]
    blank = jnp.zeros((1,) + widened.shape[1:], widened.dtype)
    partial = smooth_total(jnp.concatenate([blank, widened, blank], axis=0), metric[0])
    smoothed_p = partial.astype(jnp.bfloat16)
    field_wide = padded_2(smoothed_p[None], (("blk", 2),), RADIUS)[0]

    edge_partial = jnp.stack([partial[0], partial[-1]])
    taps = jnp.stack([metric[0, 0:3, 0], metric[0, 6:9, rows - 1]])
    pieces = [
        jnp.stack([normed[0], normed[-1]]).reshape(-1),
        *[p.reshape(-1) for p in split_parts(edge_partial, 2)],
        jnp.stack([smoothed_p[1], smoothed_p[2], smoothed_p[-3], smoothed_p[-2]]).reshape(-1),
        *[p.reshape(-1) for p in split_parts(taps, 3)],
        seam_rows.astype(jnp.bfloat16).reshape(-1),
    ]
    sizes = [p.size for p in pieces]
    flat = jnp.concatenate(pieces)
    total = -(-flat.size // channels) * channels
    flat = jnp.pad(flat, (0, total - flat.size)).reshape(1, total // channels, channels)
    got = lax.all_gather(flat, "blk", axis=0, tiled=True).reshape(count, total)
    offsets = [sum(sizes[:k]) for k in range(len(sizes) + 1)]

    def piece(k, shape):
        return got[:, offsets[k] : offsets[k + 1]].reshape((count,) + shape)

    edge_rows = piece(0, (2, cols, channels))
    part_all = piece(1, (2, cols, channels)).astype(jnp.float32) + piece(2, (2, cols, channels)).astype(jnp.float32)
    inner = piece(3, (4, cols, channels))
    tap_parts = [piece(4 + k, (2, 3, cols)).astype(jnp.float32) for k in range(3)]
    taps_all = tap_parts[0] + (tap_parts[1] + tap_parts[2])
    table_all = piece(7, (2, 3)).astype(jnp.int32)

    edges1 = widen_tiles(edge_rows, 1)
    rims1 = pick_all(table_all, edges1[:, :, None])[:, :, 0]
    flip = (table_all[:, :, 2] % 2 == 1)[:, :, None, None]
    rims1 = jnp.where(flip, rims1[:, :, ::-1], rims1)

    out_col = lax.broadcasted_iota(jnp.int32, (cols, cols + 2), 0)
    in_col = lax.broadcasted_iota(jnp.int32, (cols, cols + 2), 1)
    band = jnp.zeros((count, 2, cols, cols + 2), jnp.float32)
    for b in range(3):
        band = band + jnp.where(in_col == out_col + b, taps_all[:, :, b, :, None], 0.0)
    contrib = jnp.einsum(
        "uejp,uepc->uejc", band, rims1.astype(jnp.float32), precision=lax.Precision.HIGHEST
    )
    done = (part_all + contrib).astype(jnp.bfloat16)
    band6 = jnp.concatenate([done[:, 0:1], inner, done[:, 1:2]], axis=1)
    wide3 = widen_tiles(band6, RADIUS)
    mine = lax.dynamic_index_in_dim(wide3, me, 0, keepdims=False)
    field_wide = jnp.concatenate([mine[0:1], field_wide[1:-1], mine[-1:]], axis=0)

    edges3 = jnp.stack([wide3[:, :RADIUS], wide3[:, RADIUS:]], axis=1)
    field_got = pick_all(seam_rows, edges3)
    field_pad = place_rims(field_wide, field_got, seam_rows)
    query = project(field_wide[:, RADIUS : RADIUS + cols], w_query)
    return attend_and_mix(query, field_pad, w_key, w_value, own_tile, w_output)[None]


def solution(mesh):
    return jax.shard_map(
        local,
        mesh=mesh,
        in_specs=(
            P(("group", "blk"), None, None, None),
            P(),
            P("blk", None, None, None),
            P(),
            P(),
            P(),
            P(),
            P("blk", None, None),
        ),
        out_specs=P(("group", "blk"), None, None, None),
        check_vma=False,
    )
```

```python
import jax
import jax.numpy as jnp
from jax import lax
from jax.sharding import PartitionSpec as P
from jax.experimental import pallas as pl
from jax.experimental.pallas import tpu as pltpu

HEADS = 8
RADIUS = 3


def padded_2(array, sides, width):
    for axis, dim in sides:
        count, length = (lax.axis_size(axis), array.shape[dim])
        up = [(i, (i + 1) % count) for i in range(count)]
        down = [(j, i) for i, j in up]
        last = lax.slice_in_dim(array, length - width, length, axis=dim)
        first = lax.slice_in_dim(array, 0, width, axis=dim)
        before = lax.ppermute(last, axis, up)
        after = lax.ppermute(first, axis, down)
        array = jnp.concatenate([before, array, after], axis=dim)
    return array


def normalize(latents, norm_gain):
    values = latents.astype(jnp.float32)
    factor = lax.rsqrt(jnp.mean(values * values, axis=-1, keepdims=True) + 1e-05)
    return (values * factor * norm_gain).astype(jnp.bfloat16)


def pick_rims(seam_rows, piece):
    number = piece.shape[0]
    tile_ids = jnp.arange(number, dtype=jnp.int32)
    tile_hit = tile_ids[None, :] == seam_rows[:, 0:1]
    edge_hit = jnp.arange(2, dtype=jnp.int32)[None, :] == seam_rows[:, 1:2]
    chosen = (tile_hit[:, :, None] & edge_hit[:, None, :]).astype(piece.dtype)
    return jnp.einsum("enf,nfrwc->erwc", chosen, piece, preferred_element_type=jnp.float32)


def edge_rows(widened, margin):
    return jnp.stack([widened[:, :margin], widened[:, -margin:]], axis=1)


def orient_rims(received, seam_pair):
    arrived = received.astype(jnp.bfloat16)
    orient = seam_pair[:, 2]
    flip_along = (orient % 2 == 1)[:, None, None, None]
    arrived = jnp.where(flip_along, arrived[:, :, ::-1], arrived)
    flip_across = (orient // 2 == 1)[:, None, None, None]
    return jnp.where(flip_across, arrived[:, ::-1], arrived)


def place_rims(widened, received, seam_pair):
    arrived = orient_rims(received, seam_pair)
    return jnp.concatenate([arrived[0], widened, arrived[1]], axis=0)


def smooth(padded, metric):
    rows, cols = (metric.shape[-2], metric.shape[-1])
    total = jnp.zeros((rows, cols, padded.shape[-1]), jnp.float32)
    for stencil in range(9):
        row_off = stencil // 3
        col_off = stencil % 3
        total = (
            total
            + metric[stencil, :, :, None]
            * padded[row_off : row_off + rows, col_off : col_off + cols, :]
        )
    return total.astype(jnp.bfloat16)


def project(values, weight):
    shape = values.shape
    flat = values.reshape(-1, shape[-1])
    return (
        jnp.dot(flat, weight, preferred_element_type=jnp.float32)
        .astype(jnp.bfloat16)
        .reshape(shape[:-1] + (weight.shape[1],))
    )


def attention_kernel(
    sm_ref, field_ref, wq_ref, wk_ref, wv_ref, lat_ref, wo_ref, out_ref, att_ref, q_ref, k_ref, v_ref
):
    q_ref[...] = jnp.dot(sm_ref[...], wq_ref[...], preferred_element_type=jnp.float32).astype(q_ref.dtype)
    k_ref[...] = jnp.dot(field_ref[...], wk_ref[...], preferred_element_type=jnp.float32).astype(k_ref.dtype)
    v_ref[...] = jnp.dot(field_ref[...], wv_ref[...], preferred_element_type=jnp.float32).astype(v_ref.dtype)
    cells, channels = q_ref.shape
    positions = k_ref.shape[0]
    rows, cols = lat_ref.shape[0], lat_ref.shape[1]
    wide = cols + 2 * RADIUS
    span = 2 * RADIUS + 1
    head_size = channels // HEADS
    group = 128
    scale = head_size ** (-0.5)
    cell = lax.broadcasted_iota(jnp.int32, (cells, positions), 0)
    place = lax.broadcasted_iota(jnp.int32, (cells, positions), 1)
    row_gap = place // wide - cell // cols
    col_gap = place % wide - cell % cols
    valid = (row_gap >= 0) & (row_gap < span) & (col_gap >= 0) & (col_gap < span)
    lane = lax.broadcasted_iota(jnp.int32, (cells, group), 1) // head_size
    for g in range(channels // group):
        lanes = slice(g * group, (g + 1) * group)
        q_g = q_ref[:, lanes]
        k_g = k_ref[:, lanes]
        v_g = v_ref[:, lanes]
        acc = jnp.zeros((cells, group), jnp.float32)
        for part in range(group // head_size):
            q_h = jnp.where(lane == part, q_g, jnp.zeros_like(q_g))
            s = lax.dot_general(
                q_h, k_g, (((1,), (1,)), ((), ())), preferred_element_type=jnp.float32
            )
            s = jnp.where(valid, s * scale, -jnp.inf)
            top = jnp.max(s, axis=1, keepdims=True)
            e = jnp.exp(s - top)
            total = jnp.sum(e, axis=1, keepdims=True)
            w = (e / total).astype(jnp.bfloat16)
            o = jnp.dot(w, v_g, preferred_element_type=jnp.float32)
            acc = jnp.where(lane == part, o, acc)
        att_ref[:, lanes] = acc.astype(jnp.bfloat16)
    mixed = jnp.dot(att_ref[...], wo_ref[...], preferred_element_type=jnp.float32)
    lat = lat_ref[...].reshape(cells, channels)
    out_ref[...] = (lat.astype(jnp.float32) + mixed).astype(out_ref.dtype)


def attend_and_mix(smoothed, field_pad, w_query, w_key, w_value, own_tile, w_output):
    rows, cols, channels = own_tile.shape
    cells = rows * cols
    flat = field_pad.reshape(-1, channels)
    positions = -(-flat.shape[0] // 128) * 128
    flat = jnp.pad(flat, ((0, positions - flat.shape[0]), (0, 0)))
    vmem = pl.BlockSpec(memory_space=pltpu.VMEM)
    out = pl.pallas_call(
        attention_kernel,
        out_shape=jax.ShapeDtypeStruct((cells, channels), own_tile.dtype),
        in_specs=[vmem] * 7,
        out_specs=vmem,
        scratch_shapes=[
            pltpu.VMEM((cells, channels), jnp.bfloat16),
            pltpu.VMEM((cells, channels), jnp.bfloat16),
            pltpu.VMEM((positions, channels), jnp.bfloat16),
            pltpu.VMEM((positions, channels), jnp.bfloat16),
        ],
    )(smoothed.reshape(cells, channels), flat, w_query, w_key, w_value, own_tile, w_output)
    return out.reshape(rows, cols, channels)


def widen_tiles(field, margin):
    west = jnp.roll(field, 1, axis=0)[:, :, -margin:]
    east = jnp.roll(field, -1, axis=0)[:, :, :margin]
    return jnp.concatenate([west, field, east], axis=2)


def pick_all(table, edges):
    number = edges.shape[0]
    tile_hit = jnp.arange(number, dtype=jnp.int32) == table[..., 0:1]
    edge_hit = jnp.arange(2, dtype=jnp.int32) == table[..., 1:2]
    chosen = (tile_hit[..., :, None] & edge_hit[..., None, :]).astype(edges.dtype)
    got = jnp.einsum("...nf,nfrwc->...rwc", chosen, edges, preferred_element_type=jnp.float32)
    return got.astype(edges.dtype)


def local(latents, norm_gain, metric, w_query, w_key, w_value, w_output, seam_table):
    own_tile = latents[0]
    channels = own_tile.shape[-1]
    normed = normalize(own_tile, norm_gain)
    margin = 1
    seam_rows = seam_table[0]
    widened = padded_2(normed[None], (("blk", 2),), margin)
    rows1 = jnp.stack([normed[0], normed[-1]])
    got1 = widen_tiles(lax.all_gather(rows1[None], "blk", axis=0, tiled=True), 1)
    received = pick_all(seam_rows, got1[:, :, None])
    padded = place_rims(widened[0], received, seam_rows)
    smoothed = smooth(padded, metric[0])
    field_wide = padded_2(smoothed[None], (("blk", 2),), RADIUS)
    rows3 = jnp.concatenate([smoothed[:RADIUS], smoothed[-RADIUS:]], axis=0)
    got3 = widen_tiles(lax.all_gather(rows3[None], "blk", axis=0, tiled=True), RADIUS)
    edges3 = jnp.stack([got3[:, :RADIUS], got3[:, RADIUS:]], axis=1)
    field_got = pick_all(seam_rows, edges3)
    field_pad = place_rims(field_wide[0], field_got, seam_rows)
    return attend_and_mix(smoothed, field_pad, w_query, w_key, w_value, own_tile, w_output)[None]


def solution(mesh):
    return jax.shard_map(
        local,
        mesh=mesh,
        in_specs=(
            P(("group", "blk"), None, None, None),
            P(),
            P("blk", None, None, None),
            P(),
            P(),
            P(),
            P(),
            P("blk", None, None),
        ),
        out_specs=P(("group", "blk"), None, None, None),
        check_vma=False,
    )
```

```python
import jax
import jax.numpy as jnp
from jax import lax
from jax.sharding import PartitionSpec as P
from jax.experimental import pallas as pl
from jax.experimental.pallas import tpu as pltpu

HEADS = 8
RADIUS = 3


def padded_2(array, sides, width):
    for axis, dim in sides:
        count, length = (lax.axis_size(axis), array.shape[dim])
        up = [(i, (i + 1) % count) for i in range(count)]
        down = [(j, i) for i, j in up]
        last = lax.slice_in_dim(array, length - width, length, axis=dim)
        first = lax.slice_in_dim(array, 0, width, axis=dim)
        before = lax.ppermute(last, axis, up)
        after = lax.ppermute(first, axis, down)
        array = jnp.concatenate([before, array, after], axis=dim)
    return array


def normalize(latents, norm_gain):
    values = latents.astype(jnp.float32)
    factor = lax.rsqrt(jnp.mean(values * values, axis=-1, keepdims=True) + 1e-05)
    return (values * factor * norm_gain).astype(jnp.bfloat16)


def pick_rims(seam_rows, piece):
    number = piece.shape[0]
    tile_ids = jnp.arange(number, dtype=jnp.int32)
    tile_hit = tile_ids[None, :] == seam_rows[:, 0:1]
    edge_hit = jnp.arange(2, dtype=jnp.int32)[None, :] == seam_rows[:, 1:2]
    chosen = (tile_hit[:, :, None] & edge_hit[:, None, :]).astype(piece.dtype)
    return jnp.einsum("enf,nfrwc->erwc", chosen, piece, preferred_element_type=jnp.float32)


def edge_rows(widened, margin):
    return jnp.stack([widened[:, :margin], widened[:, -margin:]], axis=1)


def orient_rims(received, seam_pair):
    arrived = received.astype(jnp.bfloat16)
    orient = seam_pair[:, 2]
    flip_along = (orient % 2 == 1)[:, None, None, None]
    arrived = jnp.where(flip_along, arrived[:, :, ::-1], arrived)
    flip_across = (orient // 2 == 1)[:, None, None, None]
    return jnp.where(flip_across, arrived[:, ::-1], arrived)


def place_rims(widened, received, seam_pair):
    arrived = orient_rims(received, seam_pair)
    return jnp.concatenate([arrived[0], widened, arrived[1]], axis=0)


def smooth(padded, metric):
    rows, cols = (metric.shape[-2], metric.shape[-1])
    total = jnp.zeros((rows, cols, padded.shape[-1]), jnp.float32)
    for stencil in range(9):
        row_off = stencil // 3
        col_off = stencil % 3
        total = (
            total
            + metric[stencil, :, :, None]
            * padded[row_off : row_off + rows, col_off : col_off + cols, :]
        )
    return total.astype(jnp.bfloat16)


def project(values, weight):
    shape = values.shape
    flat = values.reshape(-1, shape[-1])
    return (
        jnp.dot(flat, weight, preferred_element_type=jnp.float32)
        .astype(jnp.bfloat16)
        .reshape(shape[:-1] + (weight.shape[1],))
    )


def attention_kernel(q_ref, k_ref, v_ref, lat_ref, wo_ref, out_ref, att_ref):
    cells, channels = q_ref.shape
    positions = k_ref.shape[0]
    rows, cols = lat_ref.shape[0], lat_ref.shape[1]
    wide = cols + 2 * RADIUS
    span = 2 * RADIUS + 1
    head_size = channels // HEADS
    group = 128
    scale = head_size ** (-0.5)
    cell = lax.broadcasted_iota(jnp.int32, (cells, positions), 0)
    place = lax.broadcasted_iota(jnp.int32, (cells, positions), 1)
    row_gap = place // wide - cell // cols
    col_gap = place % wide - cell % cols
    valid = (row_gap >= 0) & (row_gap < span) & (col_gap >= 0) & (col_gap < span)
    lane = lax.broadcasted_iota(jnp.int32, (cells, group), 1) // head_size
    for g in range(channels // group):
        lanes = slice(g * group, (g + 1) * group)
        q_g = q_ref[:, lanes]
        k_g = k_ref[:, lanes]
        v_g = v_ref[:, lanes]
        acc = jnp.zeros((cells, group), jnp.float32)
        for part in range(group // head_size):
            q_h = jnp.where(lane == part, q_g, jnp.zeros_like(q_g))
            s = lax.dot_general(
                q_h, k_g, (((1,), (1,)), ((), ())), preferred_element_type=jnp.float32
            )
            s = jnp.where(valid, s * scale, -jnp.inf)
            top = jnp.max(s, axis=1, keepdims=True)
            e = jnp.exp(s - top)
            total = jnp.sum(e, axis=1, keepdims=True)
            w = (e / total).astype(jnp.bfloat16)
            o = jnp.dot(w, v_g, preferred_element_type=jnp.float32)
            acc = jnp.where(lane == part, o, acc)
        att_ref[:, lanes] = acc.astype(jnp.bfloat16)
    mixed = jnp.dot(att_ref[...], wo_ref[...], preferred_element_type=jnp.float32)
    lat = lat_ref[...].reshape(cells, channels)
    out_ref[...] = (lat.astype(jnp.float32) + mixed).astype(out_ref.dtype)


def attend_and_mix(query, field_pad, w_key, w_value, own_tile, w_output):
    rows, cols, channels = own_tile.shape
    cells = rows * cols
    flat = field_pad.reshape(-1, channels)
    positions = -(-flat.shape[0] // 128) * 128
    flat = jnp.pad(flat, ((0, positions - flat.shape[0]), (0, 0)))
    key_flat = project(flat, w_key)
    value_flat = project(flat, w_value)
    vmem = pl.BlockSpec(memory_space=pltpu.VMEM)
    out = pl.pallas_call(
        attention_kernel,
        out_shape=jax.ShapeDtypeStruct((cells, channels), own_tile.dtype),
        in_specs=[vmem] * 5,
        out_specs=vmem,
        scratch_shapes=[pltpu.VMEM((cells, channels), jnp.bfloat16)],
    )(query.reshape(cells, channels), key_flat, value_flat, own_tile, w_output)
    return out.reshape(rows, cols, channels)


def widen_tiles(field, margin):
    west = jnp.roll(field, 1, axis=0)[:, :, -margin:]
    east = jnp.roll(field, -1, axis=0)[:, :, :margin]
    return jnp.concatenate([west, field, east], axis=2)


def pick_all(table, edges):
    number = edges.shape[0]
    tile_hit = jnp.arange(number, dtype=jnp.int32) == table[..., 0:1]
    edge_hit = jnp.arange(2, dtype=jnp.int32) == table[..., 1:2]
    chosen = (tile_hit[..., :, None] & edge_hit[..., None, :]).astype(edges.dtype)
    got = jnp.einsum("...nf,nfrwc->...rwc", chosen, edges, preferred_element_type=jnp.float32)
    return got.astype(edges.dtype)


def doubling_gather(block, axis):
    count = lax.axis_size(axis)
    if count & (count - 1):
        return lax.all_gather(block, axis, axis=0, tiled=True)
    me = lax.axis_index(axis)
    held = block
    step = 1
    while step < count:
        other = lax.ppermute(held, axis, [(i, i ^ step) for i in range(count)])
        low = (me & step) == 0
        held = jnp.where(
            low, jnp.concatenate([held, other], axis=0), jnp.concatenate([other, held], axis=0)
        )
        step *= 2
    return held


def local(latents, norm_gain, metric, w_query, w_key, w_value, w_output, seam_table):
    own_tile = latents[0]
    channels = own_tile.shape[-1]
    normed = normalize(own_tile, norm_gain)
    margin = 1
    seam_rows = seam_table[0]
    widened = padded_2(normed[None], (("blk", 2),), margin)
    rows1 = jnp.stack([normed[0], normed[-1]])
    got1 = widen_tiles(doubling_gather(rows1[None], "blk"), 1)
    received = pick_all(seam_rows, got1[:, :, None])
    padded = place_rims(widened[0], received, seam_rows)
    smoothed = smooth(padded, metric[0])
    query = project(smoothed, w_query)
    field_wide = padded_2(smoothed[None], (("blk", 2),), RADIUS)
    rows3 = jnp.concatenate([smoothed[:RADIUS], smoothed[-RADIUS:]], axis=0)
    got3 = widen_tiles(doubling_gather(rows3[None], "blk"), RADIUS)
    edges3 = jnp.stack([got3[:, :RADIUS], got3[:, RADIUS:]], axis=1)
    field_got = pick_all(seam_rows, edges3)
    field_pad = place_rims(field_wide[0], field_got, seam_rows)
    return attend_and_mix(query, field_pad, w_key, w_value, own_tile, w_output)[None]


def solution(mesh):
    return jax.shard_map(
        local,
        mesh=mesh,
        in_specs=(
            P(("group", "blk"), None, None, None),
            P(),
            P("blk", None, None, None),
            P(),
            P(),
            P(),
            P(),
            P("blk", None, None),
        ),
        out_specs=P(("group", "blk"), None, None, None),
        check_vma=False,
    )
```

```python
import jax
import jax.numpy as jnp
from jax import lax
from jax.sharding import PartitionSpec as P
from jax.experimental import pallas as pl
from jax.experimental.pallas import tpu as pltpu

HEADS = 8
RADIUS = 3


def padded_2(array, sides, width):
    for axis, dim in sides:
        count, length = (lax.axis_size(axis), array.shape[dim])
        up = [(i, (i + 1) % count) for i in range(count)]
        down = [(j, i) for i, j in up]
        last = lax.slice_in_dim(array, length - width, length, axis=dim)
        first = lax.slice_in_dim(array, 0, width, axis=dim)
        before = lax.ppermute(last, axis, up)
        after = lax.ppermute(first, axis, down)
        array = jnp.concatenate([before, array, after], axis=dim)
    return array


def normalize(latents, norm_gain):
    values = latents.astype(jnp.float32)
    factor = lax.rsqrt(jnp.mean(values * values, axis=-1, keepdims=True) + 1e-05)
    return (values * factor * norm_gain).astype(jnp.bfloat16)


def pick_rims(seam_rows, piece):
    number = piece.shape[0]
    tile_ids = jnp.arange(number, dtype=jnp.int32)
    tile_hit = tile_ids[None, :] == seam_rows[:, 0:1]
    edge_hit = jnp.arange(2, dtype=jnp.int32)[None, :] == seam_rows[:, 1:2]
    chosen = (tile_hit[:, :, None] & edge_hit[:, None, :]).astype(piece.dtype)
    return jnp.einsum("enf,nfrwc->erwc", chosen, piece, preferred_element_type=jnp.float32)


def edge_rows(widened, margin):
    return jnp.stack([widened[:, :margin], widened[:, -margin:]], axis=1)


def orient_rims(received, seam_pair):
    arrived = received.astype(jnp.bfloat16)
    orient = seam_pair[:, 2]
    flip_along = (orient % 2 == 1)[:, None, None, None]
    arrived = jnp.where(flip_along, arrived[:, :, ::-1], arrived)
    flip_across = (orient // 2 == 1)[:, None, None, None]
    return jnp.where(flip_across, arrived[:, ::-1], arrived)


def place_rims(widened, received, seam_pair):
    arrived = orient_rims(received, seam_pair)
    return jnp.concatenate([arrived[0], widened, arrived[1]], axis=0)


def smooth(padded, metric):
    rows, cols = (metric.shape[-2], metric.shape[-1])
    total = jnp.zeros((rows, cols, padded.shape[-1]), jnp.float32)
    for stencil in range(9):
        row_off = stencil // 3
        col_off = stencil % 3
        total = (
            total
            + metric[stencil, :, :, None]
            * padded[row_off : row_off + rows, col_off : col_off + cols, :]
        )
    return total.astype(jnp.bfloat16)


def project(values, weight):
    shape = values.shape
    flat = values.reshape(-1, shape[-1])
    return (
        jnp.dot(flat, weight, preferred_element_type=jnp.float32)
        .astype(jnp.bfloat16)
        .reshape(shape[:-1] + (weight.shape[1],))
    )


def attention_kernel(q_ref, k_ref, v_ref, lat_ref, wo_ref, out_ref, att_ref):
    cells, channels = q_ref.shape
    positions = k_ref.shape[0]
    rows, cols = lat_ref.shape[0], lat_ref.shape[1]
    wide = cols + 2 * RADIUS
    span = 2 * RADIUS + 1
    head_size = channels // HEADS
    group = 128
    scale = head_size ** (-0.5)
    cell = lax.broadcasted_iota(jnp.int32, (cells, positions), 0)
    place = lax.broadcasted_iota(jnp.int32, (cells, positions), 1)
    row_gap = place // wide - cell // cols
    col_gap = place % wide - cell % cols
    valid = (row_gap >= 0) & (row_gap < span) & (col_gap >= 0) & (col_gap < span)
    lane = lax.broadcasted_iota(jnp.int32, (cells, group), 1) // head_size
    for g in range(channels // group):
        lanes = slice(g * group, (g + 1) * group)
        q_g = q_ref[:, lanes]
        k_g = k_ref[:, lanes]
        v_g = v_ref[:, lanes]
        acc = jnp.zeros((cells, group), jnp.float32)
        for part in range(group // head_size):
            q_h = jnp.where(lane == part, q_g, jnp.zeros_like(q_g))
            s = lax.dot_general(
                q_h, k_g, (((1,), (1,)), ((), ())), preferred_element_type=jnp.float32
            )
            s = jnp.where(valid, s * scale, -jnp.inf)
            top = jnp.max(s, axis=1, keepdims=True)
            e = jnp.exp(s - top)
            total = jnp.sum(e, axis=1, keepdims=True)
            w = (e / total).astype(jnp.bfloat16)
            o = jnp.dot(w, v_g, preferred_element_type=jnp.float32)
            acc = jnp.where(lane == part, o, acc)
        att_ref[:, lanes] = acc.astype(jnp.bfloat16)
    mixed = jnp.dot(att_ref[...], wo_ref[...], preferred_element_type=jnp.float32)
    lat = lat_ref[...].reshape(cells, channels)
    out_ref[...] = (lat.astype(jnp.float32) + mixed).astype(out_ref.dtype)


def attend_and_mix(query, field_pad, w_key, w_value, own_tile, w_output):
    rows, cols, channels = own_tile.shape
    cells = rows * cols
    flat = field_pad.reshape(-1, channels)
    positions = -(-flat.shape[0] // 128) * 128
    flat = jnp.pad(flat, ((0, positions - flat.shape[0]), (0, 0)))
    key_flat = project(flat, w_key)
    value_flat = project(flat, w_value)
    vmem = pl.BlockSpec(memory_space=pltpu.VMEM)
    out = pl.pallas_call(
        attention_kernel,
        out_shape=jax.ShapeDtypeStruct((cells, channels), own_tile.dtype),
        in_specs=[vmem] * 5,
        out_specs=vmem,
        scratch_shapes=[pltpu.VMEM((cells, channels), jnp.bfloat16)],
    )(query.reshape(cells, channels), key_flat, value_flat, own_tile, w_output)
    return out.reshape(rows, cols, channels)


def widen_tiles(field, margin):
    west = jnp.roll(field, 1, axis=0)[:, :, -margin:]
    east = jnp.roll(field, -1, axis=0)[:, :, :margin]
    return jnp.concatenate([west, field, east], axis=2)


def pick_all(table, edges):
    number = edges.shape[0]
    tile_hit = jnp.arange(number, dtype=jnp.int32) == table[..., 0:1]
    edge_hit = jnp.arange(2, dtype=jnp.int32) == table[..., 1:2]
    chosen = (tile_hit[..., :, None] & edge_hit[..., None, :]).astype(edges.dtype)
    got = jnp.einsum("...nf,nfrwc->...rwc", chosen, edges, preferred_element_type=jnp.float32)
    return got.astype(edges.dtype)


def radix_gather(block, axis, radix=16):
    count = lax.axis_size(axis)
    if count & (count - 1):
        return lax.all_gather(block, axis, axis=0, tiled=True)
    me = lax.axis_index(axis)
    held = block
    stride = 1
    while stride < count:
        r = min(radix, count // stride)
        got = [held]
        for d in range(1, r):
            got.append(lax.ppermute(held, axis, [(i, i ^ (d * stride)) for i in range(count)]))
        digit = (me // stride) % r
        order = digit ^ jnp.arange(r, dtype=jnp.int32)
        held = jnp.take(jnp.stack(got), order, axis=0)
        held = held.reshape((r * held.shape[1],) + held.shape[2:])
        stride *= r
    return held


def local(latents, norm_gain, metric, w_query, w_key, w_value, w_output, seam_table):
    own_tile = latents[0]
    channels = own_tile.shape[-1]
    normed = normalize(own_tile, norm_gain)
    margin = 1
    seam_rows = seam_table[0]
    widened = padded_2(normed[None], (("blk", 2),), margin)
    rows1 = jnp.stack([normed[0], normed[-1]])
    got1 = widen_tiles(radix_gather(rows1[None], "blk"), 1)
    received = pick_all(seam_rows, got1[:, :, None])
    padded = place_rims(widened[0], received, seam_rows)
    smoothed = smooth(padded, metric[0])
    query = project(smoothed, w_query)
    field_wide = padded_2(smoothed[None], (("blk", 2),), RADIUS)
    rows3 = jnp.concatenate([smoothed[:RADIUS], smoothed[-RADIUS:]], axis=0)
    got3 = widen_tiles(radix_gather(rows3[None], "blk"), RADIUS)
    edges3 = jnp.stack([got3[:, :RADIUS], got3[:, RADIUS:]], axis=1)
    field_got = pick_all(seam_rows, edges3)
    field_pad = place_rims(field_wide[0], field_got, seam_rows)
    return attend_and_mix(query, field_pad, w_key, w_value, own_tile, w_output)[None]


def solution(mesh):
    return jax.shard_map(
        local,
        mesh=mesh,
        in_specs=(
            P(("group", "blk"), None, None, None),
            P(),
            P("blk", None, None, None),
            P(),
            P(),
            P(),
            P(),
            P("blk", None, None),
        ),
        out_specs=P(("group", "blk"), None, None, None),
        check_vma=False,
    )
```

```python
import functools

import jax
import jax.numpy as jnp
from jax import lax
from jax.sharding import PartitionSpec as P
from jax.experimental import pallas as pl
from jax.experimental.pallas import tpu as pltpu

HEADS = 8
RADIUS = 3


def padded_2(array, sides, width):
    for axis, dim in sides:
        count, length = (lax.axis_size(axis), array.shape[dim])
        up = [(i, (i + 1) % count) for i in range(count)]
        down = [(j, i) for i, j in up]
        last = lax.slice_in_dim(array, length - width, length, axis=dim)
        first = lax.slice_in_dim(array, 0, width, axis=dim)
        before = lax.ppermute(last, axis, up)
        after = lax.ppermute(first, axis, down)
        array = jnp.concatenate([before, array, after], axis=dim)
    return array


def normalize(latents, norm_gain):
    values = latents.astype(jnp.float32)
    factor = lax.rsqrt(jnp.mean(values * values, axis=-1, keepdims=True) + 1e-05)
    return (values * factor * norm_gain).astype(jnp.bfloat16)


def pick_rims(seam_rows, piece):
    number = piece.shape[0]
    tile_ids = jnp.arange(number, dtype=jnp.int32)
    tile_hit = tile_ids[None, :] == seam_rows[:, 0:1]
    edge_hit = jnp.arange(2, dtype=jnp.int32)[None, :] == seam_rows[:, 1:2]
    chosen = (tile_hit[:, :, None] & edge_hit[:, None, :]).astype(piece.dtype)
    return jnp.einsum("enf,nfrwc->erwc", chosen, piece, preferred_element_type=jnp.float32)


def edge_rows(widened, margin):
    return jnp.stack([widened[:, :margin], widened[:, -margin:]], axis=1)


def orient_rims(received, seam_pair):
    arrived = received.astype(jnp.bfloat16)
    orient = seam_pair[:, 2]
    flip_along = (orient % 2 == 1)[:, None, None, None]
    arrived = jnp.where(flip_along, arrived[:, :, ::-1], arrived)
    flip_across = (orient // 2 == 1)[:, None, None, None]
    return jnp.where(flip_across, arrived[:, ::-1], arrived)


def place_rims(widened, received, seam_pair):
    arrived = orient_rims(received, seam_pair)
    return jnp.concatenate([arrived[0], widened, arrived[1]], axis=0)


def smooth(padded, metric):
    rows, cols = (metric.shape[-2], metric.shape[-1])
    total = jnp.zeros((rows, cols, padded.shape[-1]), jnp.float32)
    for stencil in range(9):
        row_off = stencil // 3
        col_off = stencil % 3
        total = (
            total
            + metric[stencil, :, :, None]
            * padded[row_off : row_off + rows, col_off : col_off + cols, :]
        )
    return total.astype(jnp.bfloat16)


def project(values, weight):
    shape = values.shape
    flat = values.reshape(-1, shape[-1])
    return (
        jnp.dot(flat, weight, preferred_element_type=jnp.float32)
        .astype(jnp.bfloat16)
        .reshape(shape[:-1] + (weight.shape[1],))
    )


def attention_kernel(cols, q_ref, k_ref, v_ref, lat_ref, wo_ref, out_ref, att_ref):
    cells, channels = q_ref.shape
    positions = k_ref.shape[0]
    wide = cols + 2 * RADIUS
    span = 2 * RADIUS + 1
    head_size = channels // HEADS
    group = 128
    scale = head_size ** (-0.5)
    cell = lax.broadcasted_iota(jnp.int32, (cells, positions), 0)
    place = lax.broadcasted_iota(jnp.int32, (cells, positions), 1)
    row_gap = place // wide - cell // cols
    col_gap = place % wide - cell % cols
    valid = (row_gap >= 0) & (row_gap < span) & (col_gap >= 0) & (col_gap < span)
    lane = lax.broadcasted_iota(jnp.int32, (cells, group), 1) // head_size
    for g in range(channels // group):
        lanes = slice(g * group, (g + 1) * group)
        q_g = q_ref[:, lanes]
        k_g = k_ref[:, lanes]
        v_g = v_ref[:, lanes]
        acc = jnp.zeros((cells, group), jnp.float32)
        for part in range(group // head_size):
            q_h = jnp.where(lane == part, q_g, jnp.zeros_like(q_g))
            s = lax.dot_general(
                q_h, k_g, (((1,), (1,)), ((), ())), preferred_element_type=jnp.float32
            )
            s = jnp.where(valid, s * scale, -jnp.inf)
            top = jnp.max(s, axis=1, keepdims=True)
            e = jnp.exp(s - top)
            total = jnp.sum(e, axis=1, keepdims=True)
            w = (e / total).astype(jnp.bfloat16)
            o = jnp.dot(w, v_g, preferred_element_type=jnp.float32)
            acc = jnp.where(lane == part, o, acc)
        att_ref[:, lanes] = acc.astype(jnp.bfloat16)
    mixed = jnp.dot(att_ref[...], wo_ref[...], preferred_element_type=jnp.float32)
    lat = lat_ref[...]
    out_ref[...] = (lat.astype(jnp.float32) + mixed).astype(out_ref.dtype)


def attend_rows(query, keys_field, w_key, w_value, lat, w_output):
    q_rows, cols, channels = query.shape
    cells = q_rows * cols
    flat = keys_field.reshape(-1, channels)
    positions = -(-flat.shape[0] // 128) * 128
    flat = jnp.pad(flat, ((0, positions - flat.shape[0]), (0, 0)))
    key_flat = project(flat, w_key)
    value_flat = project(flat, w_value)
    vmem = pl.BlockSpec(memory_space=pltpu.VMEM)
    out = pl.pallas_call(
        functools.partial(attention_kernel, cols),
        out_shape=jax.ShapeDtypeStruct((cells, channels), lat.dtype),
        in_specs=[vmem] * 5,
        out_specs=vmem,
        scratch_shapes=[pltpu.VMEM((cells, channels), jnp.bfloat16)],
    )(query.reshape(cells, channels), key_flat, value_flat, lat.reshape(cells, channels), w_output)
    return out.reshape(q_rows, cols, channels)


def widen_tiles(field, margin):
    west = jnp.roll(field, 1, axis=0)[:, :, -margin:]
    east = jnp.roll(field, -1, axis=0)[:, :, :margin]
    return jnp.concatenate([west, field, east], axis=2)


def pick_all(table, edges):
    number = edges.shape[0]
    tile_hit = jnp.arange(number, dtype=jnp.int32) == table[..., 0:1]
    edge_hit = jnp.arange(2, dtype=jnp.int32) == table[..., 1:2]
    chosen = (tile_hit[..., :, None] & edge_hit[..., None, :]).astype(edges.dtype)
    got = jnp.einsum("...nf,nfrwc->...rwc", chosen, edges, preferred_element_type=jnp.float32)
    return got.astype(edges.dtype)


def doubling_gather(block, axis):
    count = lax.axis_size(axis)
    if count & (count - 1):
        return lax.all_gather(block, axis, axis=0, tiled=True)
    me = lax.axis_index(axis)
    held = block
    step = 1
    while step < count:
        other = lax.ppermute(held, axis, [(i, i ^ step) for i in range(count)])
        low = (me & step) == 0
        held = jnp.where(
            low, jnp.concatenate([held, other], axis=0), jnp.concatenate([other, held], axis=0)
        )
        step *= 2
    return held


def local(latents, norm_gain, metric, w_query, w_key, w_value, w_output, seam_table):
    own_tile = latents[0]
    channels = own_tile.shape[-1]
    normed = normalize(own_tile, norm_gain)
    margin = 1
    seam_rows = seam_table[0]
    widened = padded_2(normed[None], (("blk", 2),), margin)
    rows1 = jnp.stack([normed[0], normed[-1]])
    got1 = widen_tiles(doubling_gather(rows1[None], "blk"), 1)
    received = pick_all(seam_rows, got1[:, :, None])
    padded = place_rims(widened[0], received, seam_rows)
    smoothed = smooth(padded, metric[0])
    query = project(smoothed, w_query)
    field_wide = padded_2(smoothed[None], (("blk", 2),), RADIUS)
    rows = own_tile.shape[0]
    span = 2 * RADIUS + 1
    inner = attend_rows(
        query[RADIUS : rows - RADIUS], field_wide[0], w_key, w_value,
        own_tile[RADIUS : rows - RADIUS], w_output,
    )
    rows3 = jnp.concatenate([smoothed[:RADIUS], smoothed[-RADIUS:]], axis=0)
    got3 = widen_tiles(doubling_gather(rows3[None], "blk"), RADIUS)
    edges3 = jnp.stack([got3[:, :RADIUS], got3[:, RADIUS:]], axis=1)
    field_got = pick_all(seam_rows, edges3)
    field_pad = place_rims(field_wide[0], field_got, seam_rows)
    top = attend_rows(
        query[:RADIUS], field_pad[: RADIUS + span - 1], w_key, w_value, own_tile[:RADIUS], w_output
    )
    bottom = attend_rows(
        query[rows - RADIUS :], field_pad[rows - RADIUS :], w_key, w_value,
        own_tile[rows - RADIUS :], w_output,
    )
    return jnp.concatenate([top, inner, bottom], axis=0)[None]


def solution(mesh):
    return jax.shard_map(
        local,
        mesh=mesh,
        in_specs=(
            P(("group", "blk"), None, None, None),
            P(),
            P("blk", None, None, None),
            P(),
            P(),
            P(),
            P(),
            P("blk", None, None),
        ),
        out_specs=P(("group", "blk"), None, None, None),
        check_vma=False,
    )
```

```python
import jax
import jax.numpy as jnp
from jax import lax
from jax.sharding import PartitionSpec as P
from jax.experimental import pallas as pl
from jax.experimental.pallas import tpu as pltpu

HEADS = 8
RADIUS = 3


def padded_2(array, sides, width):
    for axis, dim in sides:
        count, length = (lax.axis_size(axis), array.shape[dim])
        up = [(i, (i + 1) % count) for i in range(count)]
        down = [(j, i) for i, j in up]
        last = lax.slice_in_dim(array, length - width, length, axis=dim)
        first = lax.slice_in_dim(array, 0, width, axis=dim)
        before = lax.ppermute(last, axis, up)
        after = lax.ppermute(first, axis, down)
        array = jnp.concatenate([before, array, after], axis=dim)
    return array


def normalize(latents, norm_gain):
    values = latents.astype(jnp.float32)
    factor = lax.rsqrt(jnp.mean(values * values, axis=-1, keepdims=True) + 1e-05)
    return (values * factor * norm_gain).astype(jnp.bfloat16)


def pick_rims(seam_rows, piece):
    number = piece.shape[0]
    tile_ids = jnp.arange(number, dtype=jnp.int32)
    tile_hit = tile_ids[None, :] == seam_rows[:, 0:1]
    edge_hit = jnp.arange(2, dtype=jnp.int32)[None, :] == seam_rows[:, 1:2]
    chosen = (tile_hit[:, :, None] & edge_hit[:, None, :]).astype(piece.dtype)
    return jnp.einsum("enf,nfrwc->erwc", chosen, piece, preferred_element_type=jnp.float32)


def edge_rows(widened, margin):
    return jnp.stack([widened[:, :margin], widened[:, -margin:]], axis=1)


def orient_rims(received, seam_pair):
    arrived = received.astype(jnp.bfloat16)
    orient = seam_pair[:, 2]
    flip_along = (orient % 2 == 1)[:, None, None, None]
    arrived = jnp.where(flip_along, arrived[:, :, ::-1], arrived)
    flip_across = (orient // 2 == 1)[:, None, None, None]
    return jnp.where(flip_across, arrived[:, ::-1], arrived)


def place_rims(widened, received, seam_pair):
    arrived = orient_rims(received, seam_pair)
    return jnp.concatenate([arrived[0], widened, arrived[1]], axis=0)


def smooth(padded, metric):
    rows, cols = (metric.shape[-2], metric.shape[-1])
    total = jnp.zeros((rows, cols, padded.shape[-1]), jnp.float32)
    for stencil in range(9):
        row_off = stencil // 3
        col_off = stencil % 3
        total = (
            total
            + metric[stencil, :, :, None]
            * padded[row_off : row_off + rows, col_off : col_off + cols, :]
        )
    return total.astype(jnp.bfloat16)


def project(values, weight):
    shape = values.shape
    flat = values.reshape(-1, shape[-1])
    return (
        jnp.dot(flat, weight, preferred_element_type=jnp.float32)
        .astype(jnp.bfloat16)
        .reshape(shape[:-1] + (weight.shape[1],))
    )


def attention_kernel(q_ref, k_ref, v_ref, lat_ref, wo_ref, out_ref, att_ref):
    cells, channels = q_ref.shape
    positions = k_ref.shape[0]
    rows, cols = lat_ref.shape[0], lat_ref.shape[1]
    wide = cols + 2 * RADIUS
    span = 2 * RADIUS + 1
    head_size = channels // HEADS
    group = 128
    scale = head_size ** (-0.5)
    cell = lax.broadcasted_iota(jnp.int32, (cells, positions), 0)
    place = lax.broadcasted_iota(jnp.int32, (cells, positions), 1)
    row_gap = place // wide - cell // cols
    col_gap = place % wide - cell % cols
    valid = (row_gap >= 0) & (row_gap < span) & (col_gap >= 0) & (col_gap < span)
    lane = lax.broadcasted_iota(jnp.int32, (cells, group), 1) // head_size
    for g in range(channels // group):
        lanes = slice(g * group, (g + 1) * group)
        q_g = q_ref[:, lanes]
        k_g = k_ref[:, lanes]
        v_g = v_ref[:, lanes]
        acc = jnp.zeros((cells, group), jnp.float32)
        for part in range(group // head_size):
            q_h = jnp.where(lane == part, q_g, jnp.zeros_like(q_g))
            s = lax.dot_general(
                q_h, k_g, (((1,), (1,)), ((), ())), preferred_element_type=jnp.float32
            )
            s = jnp.where(valid, s * scale, -jnp.inf)
            top = jnp.max(s, axis=1, keepdims=True)
            e = jnp.exp(s - top)
            total = jnp.sum(e, axis=1, keepdims=True)
            w = (e / total).astype(jnp.bfloat16)
            o = jnp.dot(w, v_g, preferred_element_type=jnp.float32)
            acc = jnp.where(lane == part, o, acc)
        att_ref[:, lanes] = acc.astype(jnp.bfloat16)
    mixed = jnp.dot(att_ref[...], wo_ref[...], preferred_element_type=jnp.float32)
    lat = lat_ref[...].reshape(cells, channels)
    out_ref[...] = (lat.astype(jnp.float32) + mixed).astype(out_ref.dtype)


def attend_and_mix(query, field_pad, w_key, w_value, own_tile, w_output):
    rows, cols, channels = own_tile.shape
    cells = rows * cols
    flat = field_pad.reshape(-1, channels)
    positions = -(-flat.shape[0] // 128) * 128
    flat = jnp.pad(flat, ((0, positions - flat.shape[0]), (0, 0)))
    key_flat = project(flat, w_key)
    value_flat = project(flat, w_value)
    vmem = pl.BlockSpec(memory_space=pltpu.VMEM)
    out = pl.pallas_call(
        attention_kernel,
        out_shape=jax.ShapeDtypeStruct((cells, channels), own_tile.dtype),
        in_specs=[vmem] * 5,
        out_specs=vmem,
        scratch_shapes=[pltpu.VMEM((cells, channels), jnp.bfloat16)],
    )(query.reshape(cells, channels), key_flat, value_flat, own_tile, w_output)
    return out.reshape(rows, cols, channels)


def widen_tiles(field, margin):
    west = jnp.roll(field, 1, axis=0)[:, :, -margin:]
    east = jnp.roll(field, -1, axis=0)[:, :, :margin]
    return jnp.concatenate([west, field, east], axis=2)


def pick_all(table, edges):
    number = edges.shape[0]
    tile_hit = jnp.arange(number, dtype=jnp.int32) == table[..., 0:1]
    edge_hit = jnp.arange(2, dtype=jnp.int32) == table[..., 1:2]
    chosen = (tile_hit[..., :, None] & edge_hit[..., None, :]).astype(edges.dtype)
    got = jnp.einsum("...nf,nfrwc->...rwc", chosen, edges, preferred_element_type=jnp.float32)
    return got.astype(edges.dtype)


def doubling_gather(block, axis):
    count = lax.axis_size(axis)
    if count & (count - 1):
        return lax.all_gather(block, axis, axis=0, tiled=True)
    me = lax.axis_index(axis)
    bits = count.bit_length() - 1
    held = block
    for k in reversed(range(bits)):
        step = 1 << k
        other = lax.ppermute(held, axis, [(i, i ^ step) for i in range(count)])
        low = (me & step) == 0
        held = jnp.where(
            low, jnp.concatenate([held, other], axis=0), jnp.concatenate([other, held], axis=0)
        )
    reverse = [int(format(j, "0%db" % bits)[::-1], 2) for j in range(count)] if bits else [0]
    return jnp.take(held, jnp.array(reverse, dtype=jnp.int32), axis=0)


def local(latents, norm_gain, metric, w_query, w_key, w_value, w_output, seam_table):
    own_tile = latents[0]
    channels = own_tile.shape[-1]
    normed = normalize(own_tile, norm_gain)
    margin = 1
    seam_rows = seam_table[0]
    widened = padded_2(normed[None], (("blk", 2),), margin)
    rows1 = jnp.stack([normed[0], normed[-1]])
    got1 = widen_tiles(doubling_gather(rows1[None], "blk"), 1)
    received = pick_all(seam_rows, got1[:, :, None])
    padded = place_rims(widened[0], received, seam_rows)
    smoothed = smooth(padded, metric[0])
    query = project(smoothed, w_query)
    field_wide = padded_2(smoothed[None], (("blk", 2),), RADIUS)
    rows3 = jnp.concatenate([smoothed[:RADIUS], smoothed[-RADIUS:]], axis=0)
    got3 = widen_tiles(doubling_gather(rows3[None], "blk"), RADIUS)
    edges3 = jnp.stack([got3[:, :RADIUS], got3[:, RADIUS:]], axis=1)
    field_got = pick_all(seam_rows, edges3)
    field_pad = place_rims(field_wide[0], field_got, seam_rows)
    return attend_and_mix(query, field_pad, w_key, w_value, own_tile, w_output)[None]


def solution(mesh):
    return jax.shard_map(
        local,
        mesh=mesh,
        in_specs=(
            P(("group", "blk"), None, None, None),
            P(),
            P("blk", None, None, None),
            P(),
            P(),
            P(),
            P(),
            P("blk", None, None),
        ),
        out_specs=P(("group", "blk"), None, None, None),
        check_vma=False,
    )
```

```python
import jax
import jax.numpy as jnp
from jax import lax
from jax.sharding import PartitionSpec as P
from jax.experimental import pallas as pl
from jax.experimental.pallas import tpu as pltpu

HEADS = 8
RADIUS = 3


def padded_2(array, sides, width):
    for axis, dim in sides:
        count, length = (lax.axis_size(axis), array.shape[dim])
        up = [(i, (i + 1) % count) for i in range(count)]
        down = [(j, i) for i, j in up]
        last = lax.slice_in_dim(array, length - width, length, axis=dim)
        first = lax.slice_in_dim(array, 0, width, axis=dim)
        before = lax.ppermute(last, axis, up)
        after = lax.ppermute(first, axis, down)
        array = jnp.concatenate([before, array, after], axis=dim)
    return array


def normalize(latents, norm_gain):
    values = latents.astype(jnp.float32)
    factor = lax.rsqrt(jnp.mean(values * values, axis=-1, keepdims=True) + 1e-05)
    return (values * factor * norm_gain).astype(jnp.bfloat16)


def pick_rims(seam_rows, piece):
    number = piece.shape[0]
    tile_ids = jnp.arange(number, dtype=jnp.int32)
    tile_hit = tile_ids[None, :] == seam_rows[:, 0:1]
    edge_hit = jnp.arange(2, dtype=jnp.int32)[None, :] == seam_rows[:, 1:2]
    chosen = (tile_hit[:, :, None] & edge_hit[:, None, :]).astype(piece.dtype)
    return jnp.einsum("enf,nfrwc->erwc", chosen, piece, preferred_element_type=jnp.float32)


def edge_rows(widened, margin):
    return jnp.stack([widened[:, :margin], widened[:, -margin:]], axis=1)


def orient_rims(received, seam_pair):
    arrived = received.astype(jnp.bfloat16)
    orient = seam_pair[:, 2]
    flip_along = (orient % 2 == 1)[:, None, None, None]
    arrived = jnp.where(flip_along, arrived[:, :, ::-1], arrived)
    flip_across = (orient // 2 == 1)[:, None, None, None]
    return jnp.where(flip_across, arrived[:, ::-1], arrived)


def place_rims(widened, received, seam_pair):
    arrived = orient_rims(received, seam_pair)
    return jnp.concatenate([arrived[0], widened, arrived[1]], axis=0)


def smooth(padded, metric):
    rows, cols = (metric.shape[-2], metric.shape[-1])
    total = jnp.zeros((rows, cols, padded.shape[-1]), jnp.float32)
    for stencil in range(9):
        row_off = stencil // 3
        col_off = stencil % 3
        total = (
            total
            + metric[stencil, :, :, None]
            * padded[row_off : row_off + rows, col_off : col_off + cols, :]
        )
    return total.astype(jnp.bfloat16)


def project(values, weight):
    shape = values.shape
    flat = values.reshape(-1, shape[-1])
    return (
        jnp.dot(flat, weight, preferred_element_type=jnp.float32)
        .astype(jnp.bfloat16)
        .reshape(shape[:-1] + (weight.shape[1],))
    )


def attention_kernel(q_ref, k_ref, v_ref, lat_ref, wo_ref, out_ref, att_ref):
    cells, channels = q_ref.shape
    positions = k_ref.shape[0]
    rows, cols = lat_ref.shape[0], lat_ref.shape[1]
    wide = cols + 2 * RADIUS
    span = 2 * RADIUS + 1
    head_size = channels // HEADS
    group = 128
    scale = head_size ** (-0.5)
    cell = lax.broadcasted_iota(jnp.int32, (cells, positions), 0)
    place = lax.broadcasted_iota(jnp.int32, (cells, positions), 1)
    row_gap = place // wide - cell // cols
    col_gap = place % wide - cell % cols
    valid = (row_gap >= 0) & (row_gap < span) & (col_gap >= 0) & (col_gap < span)
    lane = lax.broadcasted_iota(jnp.int32, (cells, group), 1) // head_size
    for g in range(channels // group):
        lanes = slice(g * group, (g + 1) * group)
        q_g = q_ref[:, lanes]
        k_g = k_ref[:, lanes]
        v_g = v_ref[:, lanes]
        acc = jnp.zeros((cells, group), jnp.float32)
        for part in range(group // head_size):
            q_h = jnp.where(lane == part, q_g, jnp.zeros_like(q_g))
            s = lax.dot_general(
                q_h, k_g, (((1,), (1,)), ((), ())), preferred_element_type=jnp.float32
            )
            s = jnp.where(valid, s * scale, -jnp.inf)
            top = jnp.max(s, axis=1, keepdims=True)
            e = jnp.exp(s - top)
            total = jnp.sum(e, axis=1, keepdims=True)
            w = (e / total).astype(jnp.bfloat16)
            o = jnp.dot(w, v_g, preferred_element_type=jnp.float32)
            acc = jnp.where(lane == part, o, acc)
        att_ref[:, lanes] = acc.astype(jnp.bfloat16)
    mixed = jnp.dot(att_ref[...], wo_ref[...], preferred_element_type=jnp.float32)
    lat = lat_ref[...].reshape(cells, channels)
    out_ref[...] = (lat.astype(jnp.float32) + mixed).astype(out_ref.dtype)


def attend_and_mix(query, field_pad, w_key, w_value, own_tile, w_output):
    rows, cols, channels = own_tile.shape
    cells = rows * cols
    flat = field_pad.reshape(-1, channels)
    positions = -(-flat.shape[0] // 128) * 128
    flat = jnp.pad(flat, ((0, positions - flat.shape[0]), (0, 0)))
    key_flat = project(flat, w_key)
    value_flat = project(flat, w_value)
    vmem = pl.BlockSpec(memory_space=pltpu.VMEM)
    out = pl.pallas_call(
        attention_kernel,
        out_shape=jax.ShapeDtypeStruct((cells, channels), own_tile.dtype),
        in_specs=[vmem] * 5,
        out_specs=vmem,
        scratch_shapes=[pltpu.VMEM((cells, channels), jnp.bfloat16)],
    )(query.reshape(cells, channels), key_flat, value_flat, own_tile, w_output)
    return out.reshape(rows, cols, channels)


def widen_tiles(field, margin):
    west = jnp.roll(field, 1, axis=0)[:, :, -margin:]
    east = jnp.roll(field, -1, axis=0)[:, :, :margin]
    return jnp.concatenate([west, field, east], axis=2)


def pick_all(table, edges):
    number = edges.shape[0]
    tile_hit = jnp.arange(number, dtype=jnp.int32) == table[..., 0:1]
    edge_hit = jnp.arange(2, dtype=jnp.int32) == table[..., 1:2]
    chosen = (tile_hit[..., :, None] & edge_hit[..., None, :]).astype(edges.dtype)
    got = jnp.einsum("...nf,nfrwc->...rwc", chosen, edges, preferred_element_type=jnp.float32)
    return got.astype(edges.dtype)


def doubling_gather(block, axis, radix=4):
    count = lax.axis_size(axis)
    if count & (count - 1):
        return lax.all_gather(block, axis, axis=0, tiled=True)
    me = lax.axis_index(axis)
    levels = []
    stride = 1
    while stride < count:
        r = min(radix, count // stride)
        levels.append((stride, r))
        stride *= r
    held = block
    for stride, r in reversed(levels):
        got = [held]
        for d in range(1, r):
            got.append(lax.ppermute(held, axis, [(i, i ^ (d * stride)) for i in range(count)]))
        digit = (me // stride) % r
        held = jnp.take(jnp.stack(got), digit ^ jnp.arange(r, dtype=jnp.int32), axis=0)
    depth = len(levels)
    held = jnp.transpose(held, tuple(reversed(range(depth))) + tuple(range(depth, held.ndim)))
    return held.reshape((count * block.shape[0],) + block.shape[1:])


def local(latents, norm_gain, metric, w_query, w_key, w_value, w_output, seam_table):
    own_tile = latents[0]
    channels = own_tile.shape[-1]
    normed = normalize(own_tile, norm_gain)
    margin = 1
    seam_rows = seam_table[0]
    widened = padded_2(normed[None], (("blk", 2),), margin)
    rows1 = jnp.stack([normed[0], normed[-1]])
    got1 = widen_tiles(doubling_gather(rows1[None], "blk"), 1)
    received = pick_all(seam_rows, got1[:, :, None])
    padded = place_rims(widened[0], received, seam_rows)
    smoothed = smooth(padded, metric[0])
    query = project(smoothed, w_query)
    field_wide = padded_2(smoothed[None], (("blk", 2),), RADIUS)
    rows3 = jnp.concatenate([smoothed[:RADIUS], smoothed[-RADIUS:]], axis=0)
    got3 = widen_tiles(doubling_gather(rows3[None], "blk"), RADIUS)
    edges3 = jnp.stack([got3[:, :RADIUS], got3[:, RADIUS:]], axis=1)
    field_got = pick_all(seam_rows, edges3)
    field_pad = place_rims(field_wide[0], field_got, seam_rows)
    return attend_and_mix(query, field_pad, w_key, w_value, own_tile, w_output)[None]


def solution(mesh):
    return jax.shard_map(
        local,
        mesh=mesh,
        in_specs=(
            P(("group", "blk"), None, None, None),
            P(),
            P("blk", None, None, None),
            P(),
            P(),
            P(),
            P(),
            P("blk", None, None),
        ),
        out_specs=P(("group", "blk"), None, None, None),
        check_vma=False,
    )
```

```python
import jax
import jax.numpy as jnp
from jax import lax
from jax.sharding import PartitionSpec as P
from jax.experimental import pallas as pl
from jax.experimental.pallas import tpu as pltpu

HEADS = 8
RADIUS = 3


def padded_2(array, sides, width):
    for axis, dim in sides:
        count, length = (lax.axis_size(axis), array.shape[dim])
        up = [(i, (i + 1) % count) for i in range(count)]
        down = [(j, i) for i, j in up]
        last = lax.slice_in_dim(array, length - width, length, axis=dim)
        first = lax.slice_in_dim(array, 0, width, axis=dim)
        before = lax.ppermute(last, axis, up)
        after = lax.ppermute(first, axis, down)
        array = jnp.concatenate([before, array, after], axis=dim)
    return array


def normalize(latents, norm_gain):
    values = latents.astype(jnp.float32)
    factor = lax.rsqrt(jnp.mean(values * values, axis=-1, keepdims=True) + 1e-05)
    return (values * factor * norm_gain).astype(jnp.bfloat16)


def pick_rims(seam_rows, piece):
    number = piece.shape[0]
    tile_ids = jnp.arange(number, dtype=jnp.int32)
    tile_hit = tile_ids[None, :] == seam_rows[:, 0:1]
    edge_hit = jnp.arange(2, dtype=jnp.int32)[None, :] == seam_rows[:, 1:2]
    chosen = (tile_hit[:, :, None] & edge_hit[:, None, :]).astype(piece.dtype)
    return jnp.einsum("enf,nfrwc->erwc", chosen, piece, preferred_element_type=jnp.float32)


def edge_rows(widened, margin):
    return jnp.stack([widened[:, :margin], widened[:, -margin:]], axis=1)


def orient_rims(received, seam_pair):
    arrived = received.astype(jnp.bfloat16)
    orient = seam_pair[:, 2]
    flip_along = (orient % 2 == 1)[:, None, None, None]
    arrived = jnp.where(flip_along, arrived[:, :, ::-1], arrived)
    flip_across = (orient // 2 == 1)[:, None, None, None]
    return jnp.where(flip_across, arrived[:, ::-1], arrived)


def place_rims(widened, received, seam_pair):
    arrived = orient_rims(received, seam_pair)
    return jnp.concatenate([arrived[0], widened, arrived[1]], axis=0)


def smooth(padded, metric):
    rows, cols = (metric.shape[-2], metric.shape[-1])
    total = jnp.zeros((rows, cols, padded.shape[-1]), jnp.float32)
    for stencil in range(9):
        row_off = stencil // 3
        col_off = stencil % 3
        total = (
            total
            + metric[stencil, :, :, None]
            * padded[row_off : row_off + rows, col_off : col_off + cols, :]
        )
    return total.astype(jnp.bfloat16)


def project(values, weight):
    shape = values.shape
    flat = values.reshape(-1, shape[-1])
    return (
        jnp.dot(flat, weight, preferred_element_type=jnp.float32)
        .astype(jnp.bfloat16)
        .reshape(shape[:-1] + (weight.shape[1],))
    )


def attention_kernel(q_ref, k_ref, v_ref, lat_ref, wo_ref, out_ref, att_ref):
    cells, channels = q_ref.shape
    rows, cols = lat_ref.shape[0], lat_ref.shape[1]
    wide = cols + 2 * RADIUS
    span = 2 * RADIUS + 1
    head_size = channels // HEADS
    group = 128
    scale = head_size ** (-0.5)
    band_rows = 8
    band_cells = band_rows * cols
    band_keys = -(-(band_rows + span - 1) * wide // group) * group
    cell = lax.broadcasted_iota(jnp.int32, (band_cells, band_keys), 0)
    place = lax.broadcasted_iota(jnp.int32, (band_cells, band_keys), 1)
    row_gap = place // wide - cell // cols
    col_gap = place % wide - cell % cols
    valid = (row_gap >= 0) & (row_gap < span) & (col_gap >= 0) & (col_gap < span)
    lane = lax.broadcasted_iota(jnp.int32, (band_cells, group), 1) // head_size
    for g in range(channels // group):
        lanes = slice(g * group, (g + 1) * group)
        for band in range(rows // band_rows):
            q_g = q_ref[pl.ds(band * band_cells, band_cells), lanes]
            first = band * band_rows * wide
            k_g = k_ref[pl.ds(first, band_keys), lanes]
            v_g = v_ref[pl.ds(first, band_keys), lanes]
            acc = jnp.zeros((band_cells, group), jnp.float32)
            for part in range(group // head_size):
                q_h = jnp.where(lane == part, q_g, jnp.zeros_like(q_g))
                s = lax.dot_general(
                    q_h, k_g, (((1,), (1,)), ((), ())), preferred_element_type=jnp.float32
                )
                s = jnp.where(valid, s * scale, -jnp.inf)
                top = jnp.max(s, axis=1, keepdims=True)
                e = jnp.exp(s - top)
                total = jnp.sum(e, axis=1, keepdims=True)
                w = (e / total).astype(jnp.bfloat16)
                o = jnp.dot(w, v_g, preferred_element_type=jnp.float32)
                acc = jnp.where(lane == part, o, acc)
            att_ref[pl.ds(band * band_cells, band_cells), lanes] = acc.astype(jnp.bfloat16)
    mixed = jnp.dot(att_ref[...], wo_ref[...], preferred_element_type=jnp.float32)
    lat = lat_ref[...].reshape(cells, channels)
    out_ref[...] = (lat.astype(jnp.float32) + mixed).astype(out_ref.dtype)


def attend_and_mix(query, field_pad, w_key, w_value, own_tile, w_output):
    rows, cols, channels = own_tile.shape
    cells = rows * cols
    flat = field_pad.reshape(-1, channels)
    wide = cols + 2 * RADIUS
    band_keys = -(-(8 + 2 * RADIUS) * wide // 128) * 128
    positions = max(-(-flat.shape[0] // 128) * 128, (rows - 8) * wide + band_keys)
    flat = jnp.pad(flat, ((0, positions - flat.shape[0]), (0, 0)))
    key_flat = project(flat, w_key)
    value_flat = project(flat, w_value)
    vmem = pl.BlockSpec(memory_space=pltpu.VMEM)
    out = pl.pallas_call(
        attention_kernel,
        out_shape=jax.ShapeDtypeStruct((cells, channels), own_tile.dtype),
        in_specs=[vmem] * 5,
        out_specs=vmem,
        scratch_shapes=[pltpu.VMEM((cells, channels), jnp.bfloat16)],
    )(query.reshape(cells, channels), key_flat, value_flat, own_tile, w_output)
    return out.reshape(rows, cols, channels)


def widen_tiles(field, margin):
    west = jnp.roll(field, 1, axis=0)[:, :, -margin:]
    east = jnp.roll(field, -1, axis=0)[:, :, :margin]
    return jnp.concatenate([west, field, east], axis=2)


def pick_all(table, edges):
    number = edges.shape[0]
    tile_hit = jnp.arange(number, dtype=jnp.int32) == table[..., 0:1]
    edge_hit = jnp.arange(2, dtype=jnp.int32) == table[..., 1:2]
    chosen = (tile_hit[..., :, None] & edge_hit[..., None, :]).astype(edges.dtype)
    got = jnp.einsum("...nf,nfrwc->...rwc", chosen, edges, preferred_element_type=jnp.float32)
    return got.astype(edges.dtype)


def doubling_gather(block, axis, radix=4):
    count = lax.axis_size(axis)
    if count & (count - 1):
        return lax.all_gather(block, axis, axis=0, tiled=True)
    me = lax.axis_index(axis)
    levels = []
    stride = 1
    while stride < count:
        r = min(radix, count // stride)
        levels.append((stride, r))
        stride *= r
    held = block
    for stride, r in reversed(levels):
        got = [held]
        for d in range(1, r):
            got.append(lax.ppermute(held, axis, [(i, i ^ (d * stride)) for i in range(count)]))
        digit = (me // stride) % r
        held = jnp.take(jnp.stack(got), digit ^ jnp.arange(r, dtype=jnp.int32), axis=0)
    depth = len(levels)
    held = jnp.transpose(held, tuple(reversed(range(depth))) + tuple(range(depth, held.ndim)))
    return held.reshape((count * block.shape[0],) + block.shape[1:])


def local(latents, norm_gain, metric, w_query, w_key, w_value, w_output, seam_table):
    own_tile = latents[0]
    channels = own_tile.shape[-1]
    normed = normalize(own_tile, norm_gain)
    margin = 1
    seam_rows = seam_table[0]
    widened = padded_2(normed[None], (("blk", 2),), margin)
    rows1 = jnp.stack([normed[0], normed[-1]])
    got1 = widen_tiles(doubling_gather(rows1[None], "blk"), 1)
    received = pick_all(seam_rows, got1[:, :, None])
    padded = place_rims(widened[0], received, seam_rows)
    smoothed = smooth(padded, metric[0])
    query = project(smoothed, w_query)
    field_wide = padded_2(smoothed[None], (("blk", 2),), RADIUS)
    rows3 = jnp.concatenate([smoothed[:RADIUS], smoothed[-RADIUS:]], axis=0)
    got3 = widen_tiles(doubling_gather(rows3[None], "blk"), RADIUS)
    edges3 = jnp.stack([got3[:, :RADIUS], got3[:, RADIUS:]], axis=1)
    field_got = pick_all(seam_rows, edges3)
    field_pad = place_rims(field_wide[0], field_got, seam_rows)
    return attend_and_mix(query, field_pad, w_key, w_value, own_tile, w_output)[None]


def solution(mesh):
    return jax.shard_map(
        local,
        mesh=mesh,
        in_specs=(
            P(("group", "blk"), None, None, None),
            P(),
            P("blk", None, None, None),
            P(),
            P(),
            P(),
            P(),
            P("blk", None, None),
        ),
        out_specs=P(("group", "blk"), None, None, None),
        check_vma=False,
    )
```

```python
import jax
import jax.numpy as jnp
from jax import lax
from jax.sharding import PartitionSpec as P
from jax.experimental import pallas as pl
from jax.experimental.pallas import tpu as pltpu

HEADS = 8
RADIUS = 3


def padded_2(array, sides, width):
    for axis, dim in sides:
        count, length = (lax.axis_size(axis), array.shape[dim])
        up = [(i, (i + 1) % count) for i in range(count)]
        down = [(j, i) for i, j in up]
        last = lax.slice_in_dim(array, length - width, length, axis=dim)
        first = lax.slice_in_dim(array, 0, width, axis=dim)
        before = lax.ppermute(last, axis, up)
        after = lax.ppermute(first, axis, down)
        array = jnp.concatenate([before, array, after], axis=dim)
    return array


def normalize(latents, norm_gain):
    values = latents.astype(jnp.float32)
    factor = lax.rsqrt(jnp.mean(values * values, axis=-1, keepdims=True) + 1e-05)
    return (values * factor * norm_gain).astype(jnp.bfloat16)


def pick_rims(seam_rows, piece):
    number = piece.shape[0]
    tile_ids = jnp.arange(number, dtype=jnp.int32)
    tile_hit = tile_ids[None, :] == seam_rows[:, 0:1]
    edge_hit = jnp.arange(2, dtype=jnp.int32)[None, :] == seam_rows[:, 1:2]
    chosen = (tile_hit[:, :, None] & edge_hit[:, None, :]).astype(piece.dtype)
    return jnp.einsum("enf,nfrwc->erwc", chosen, piece, preferred_element_type=jnp.float32)


def edge_rows(widened, margin):
    return jnp.stack([widened[:, :margin], widened[:, -margin:]], axis=1)


def orient_rims(received, seam_pair):
    arrived = received.astype(jnp.bfloat16)
    orient = seam_pair[:, 2]
    flip_along = (orient % 2 == 1)[:, None, None, None]
    arrived = jnp.where(flip_along, arrived[:, :, ::-1], arrived)
    flip_across = (orient // 2 == 1)[:, None, None, None]
    return jnp.where(flip_across, arrived[:, ::-1], arrived)


def place_rims(widened, received, seam_pair):
    arrived = orient_rims(received, seam_pair)
    return jnp.concatenate([arrived[0], widened, arrived[1]], axis=0)


def smooth(padded, metric):
    rows, cols = (metric.shape[-2], metric.shape[-1])
    total = jnp.zeros((rows, cols, padded.shape[-1]), jnp.float32)
    for stencil in range(9):
        row_off = stencil // 3
        col_off = stencil % 3
        total = (
            total
            + metric[stencil, :, :, None]
            * padded[row_off : row_off + rows, col_off : col_off + cols, :]
        )
    return total.astype(jnp.bfloat16)


def project(values, weight):
    shape = values.shape
    flat = values.reshape(-1, shape[-1])
    return (
        jnp.dot(flat, weight, preferred_element_type=jnp.float32)
        .astype(jnp.bfloat16)
        .reshape(shape[:-1] + (weight.shape[1],))
    )


def attention_kernel(q_ref, k_ref, v_ref, lat_ref, wo_ref, out_ref, att_ref):
    cells, channels = q_ref.shape
    positions = k_ref.shape[0]
    rows, cols = lat_ref.shape[0], lat_ref.shape[1]
    wide = cols + 2 * RADIUS
    span = 2 * RADIUS + 1
    head_size = channels // HEADS
    group = 128
    scale = head_size ** (-0.5)
    cell = lax.broadcasted_iota(jnp.int32, (cells, positions), 0)
    place = lax.broadcasted_iota(jnp.int32, (cells, positions), 1)
    row_gap = place // wide - cell // cols
    col_gap = place % wide - cell % cols
    valid = (row_gap >= 0) & (row_gap < span) & (col_gap >= 0) & (col_gap < span)
    lane = lax.broadcasted_iota(jnp.int32, (cells, group), 1) // head_size
    for g in range(channels // group):
        lanes = slice(g * group, (g + 1) * group)
        q_g = q_ref[:, lanes]
        k_g = k_ref[:, lanes]
        v_g = v_ref[:, lanes]
        acc = jnp.zeros((cells, group), jnp.float32)
        for part in range(group // head_size):
            q_h = jnp.where(lane == part, q_g, jnp.zeros_like(q_g))
            s = lax.dot_general(
                q_h, k_g, (((1,), (1,)), ((), ())), preferred_element_type=jnp.float32
            )
            s = jnp.where(valid, s * scale, -jnp.inf)
            top = jnp.max(s, axis=1, keepdims=True)
            e = jnp.exp(s - top)
            total = jnp.sum(e, axis=1, keepdims=True)
            w = (e / total).astype(jnp.bfloat16)
            o = jnp.dot(w, v_g, preferred_element_type=jnp.float32)
            acc = jnp.where(lane == part, o, acc)
        att_ref[:, lanes] = acc.astype(jnp.bfloat16)
    mixed = jnp.dot(att_ref[...], wo_ref[...], preferred_element_type=jnp.float32)
    lat = lat_ref[...].reshape(cells, channels)
    out_ref[...] = (lat.astype(jnp.float32) + mixed).astype(out_ref.dtype)


def attend_and_mix(query, center, rims, w_key, w_value, own_tile, w_output):
    rows, cols, channels = own_tile.shape
    cells = rows * cols
    center_flat = center.reshape(-1, channels)
    rim_flat = rims.reshape(2, -1, channels)
    count = center_flat.shape[0] + 2 * rim_flat.shape[1]
    positions = -(-count // 128) * 128
    tail = jnp.zeros((positions - count, channels), jnp.bfloat16)

    def both(weight):
        mid = project(center_flat, weight)
        edge = project(rim_flat.reshape(-1, channels), weight).reshape(rim_flat.shape)
        return jnp.concatenate([edge[0], mid, edge[1], tail], axis=0)

    key_flat = both(w_key)
    value_flat = both(w_value)
    vmem = pl.BlockSpec(memory_space=pltpu.VMEM)
    out = pl.pallas_call(
        attention_kernel,
        out_shape=jax.ShapeDtypeStruct((cells, channels), own_tile.dtype),
        in_specs=[vmem] * 5,
        out_specs=vmem,
        scratch_shapes=[pltpu.VMEM((cells, channels), jnp.bfloat16)],
    )(query.reshape(cells, channels), key_flat, value_flat, own_tile, w_output)
    return out.reshape(rows, cols, channels)


def widen_tiles(field, margin):
    west = jnp.roll(field, 1, axis=0)[:, :, -margin:]
    east = jnp.roll(field, -1, axis=0)[:, :, :margin]
    return jnp.concatenate([west, field, east], axis=2)


def pick_all(table, edges):
    number = edges.shape[0]
    tile_hit = jnp.arange(number, dtype=jnp.int32) == table[..., 0:1]
    edge_hit = jnp.arange(2, dtype=jnp.int32) == table[..., 1:2]
    chosen = (tile_hit[..., :, None] & edge_hit[..., None, :]).astype(edges.dtype)
    got = jnp.einsum("...nf,nfrwc->...rwc", chosen, edges, preferred_element_type=jnp.float32)
    return got.astype(edges.dtype)


def doubling_gather(block, axis, radix=4):
    count = lax.axis_size(axis)
    if count & (count - 1):
        return lax.all_gather(block, axis, axis=0, tiled=True)
    me = lax.axis_index(axis)
    levels = []
    stride = 1
    while stride < count:
        r = min(radix, count // stride)
        levels.append((stride, r))
        stride *= r
    held = block
    for stride, r in reversed(levels):
        got = [held]
        for d in range(1, r):
            got.append(lax.ppermute(held, axis, [(i, i ^ (d * stride)) for i in range(count)]))
        digit = (me // stride) % r
        held = jnp.take(jnp.stack(got), digit ^ jnp.arange(r, dtype=jnp.int32), axis=0)
    depth = len(levels)
    held = jnp.transpose(held, tuple(reversed(range(depth))) + tuple(range(depth, held.ndim)))
    return held.reshape((count * block.shape[0],) + block.shape[1:])


def local(latents, norm_gain, metric, w_query, w_key, w_value, w_output, seam_table):
    own_tile = latents[0]
    channels = own_tile.shape[-1]
    normed = normalize(own_tile, norm_gain)
    margin = 1
    seam_rows = seam_table[0]
    widened = padded_2(normed[None], (("blk", 2),), margin)
    rows1 = jnp.stack([normed[0], normed[-1]])
    got1 = widen_tiles(doubling_gather(rows1[None], "blk"), 1)
    received = pick_all(seam_rows, got1[:, :, None])
    padded = place_rims(widened[0], received, seam_rows)
    smoothed = smooth(padded, metric[0])
    query = project(smoothed, w_query)
    field_wide = padded_2(smoothed[None], (("blk", 2),), RADIUS)
    rows3 = jnp.concatenate([smoothed[:RADIUS], smoothed[-RADIUS:]], axis=0)
    got3 = widen_tiles(doubling_gather(rows3[None], "blk"), RADIUS)
    edges3 = jnp.stack([got3[:, :RADIUS], got3[:, RADIUS:]], axis=1)
    field_got = pick_all(seam_rows, edges3)
    arrived = orient_rims(field_got, seam_rows)
    return attend_and_mix(query, field_wide[0], arrived, w_key, w_value, own_tile, w_output)[None]


def solution(mesh):
    return jax.shard_map(
        local,
        mesh=mesh,
        in_specs=(
            P(("group", "blk"), None, None, None),
            P(),
            P("blk", None, None, None),
            P(),
            P(),
            P(),
            P(),
            P("blk", None, None),
        ),
        out_specs=P(("group", "blk"), None, None, None),
        check_vma=False,
    )
```

```python
import jax
import jax.numpy as jnp
from jax import lax
from jax.sharding import PartitionSpec as P
from jax.experimental import pallas as pl
from jax.experimental.pallas import tpu as pltpu

HEADS = 8
RADIUS = 3


def padded_2(array, sides, width):
    for axis, dim in sides:
        count, length = (lax.axis_size(axis), array.shape[dim])
        up = [(i, (i + 1) % count) for i in range(count)]
        down = [(j, i) for i, j in up]
        last = lax.slice_in_dim(array, length - width, length, axis=dim)
        first = lax.slice_in_dim(array, 0, width, axis=dim)
        before = lax.ppermute(last, axis, up)
        after = lax.ppermute(first, axis, down)
        array = jnp.concatenate([before, array, after], axis=dim)
    return array


def normalize(latents, norm_gain):
    values = latents.astype(jnp.float32)
    factor = lax.rsqrt(jnp.mean(values * values, axis=-1, keepdims=True) + 1e-05)
    return (values * factor * norm_gain).astype(jnp.bfloat16)


def pick_rims(seam_rows, piece):
    number = piece.shape[0]
    tile_ids = jnp.arange(number, dtype=jnp.int32)
    tile_hit = tile_ids[None, :] == seam_rows[:, 0:1]
    edge_hit = jnp.arange(2, dtype=jnp.int32)[None, :] == seam_rows[:, 1:2]
    chosen = (tile_hit[:, :, None] & edge_hit[:, None, :]).astype(piece.dtype)
    return jnp.einsum("enf,nfrwc->erwc", chosen, piece, preferred_element_type=jnp.float32)


def edge_rows(widened, margin):
    return jnp.stack([widened[:, :margin], widened[:, -margin:]], axis=1)


def orient_rims(received, seam_pair):
    arrived = received.astype(jnp.bfloat16)
    orient = seam_pair[:, 2]
    flip_along = (orient % 2 == 1)[:, None, None, None]
    arrived = jnp.where(flip_along, arrived[:, :, ::-1], arrived)
    flip_across = (orient // 2 == 1)[:, None, None, None]
    return jnp.where(flip_across, arrived[:, ::-1], arrived)


def place_rims(widened, received, seam_pair):
    arrived = orient_rims(received, seam_pair)
    return jnp.concatenate([arrived[0], widened, arrived[1]], axis=0)


def smooth(padded, metric):
    rows, cols = (metric.shape[-2], metric.shape[-1])
    total = jnp.zeros((rows, cols, padded.shape[-1]), jnp.float32)
    for stencil in range(9):
        row_off = stencil // 3
        col_off = stencil % 3
        total = (
            total
            + metric[stencil, :, :, None]
            * padded[row_off : row_off + rows, col_off : col_off + cols, :]
        )
    return total.astype(jnp.bfloat16)


def project(values, weight):
    shape = values.shape
    flat = values.reshape(-1, shape[-1])
    return (
        jnp.dot(flat, weight, preferred_element_type=jnp.float32)
        .astype(jnp.bfloat16)
        .reshape(shape[:-1] + (weight.shape[1],))
    )


def attention_kernel(q_ref, k_ref, v_ref, lat_ref, wo_ref, out_ref, att_ref):
    cells, channels = q_ref.shape
    positions = k_ref.shape[0]
    rows, cols = lat_ref.shape[0], lat_ref.shape[1]
    wide = cols + 2 * RADIUS
    span = 2 * RADIUS + 1
    head_size = channels // HEADS
    group = 128
    scale = head_size ** (-0.5)
    cell = lax.broadcasted_iota(jnp.int32, (cells, positions), 0)
    place = lax.broadcasted_iota(jnp.int32, (cells, positions), 1)
    row_gap = place // wide - cell // cols
    col_gap = place % wide - cell % cols
    valid = (row_gap >= 0) & (row_gap < span) & (col_gap >= 0) & (col_gap < span)
    lane = lax.broadcasted_iota(jnp.int32, (cells, group), 1) // head_size
    for g in range(channels // group):
        lanes = slice(g * group, (g + 1) * group)
        q_g = q_ref[:, lanes]
        k_g = k_ref[:, lanes]
        v_g = v_ref[:, lanes]
        acc = jnp.zeros((cells, group), jnp.float32)
        for part in range(group // head_size):
            q_h = jnp.where(lane == part, q_g, jnp.zeros_like(q_g))
            s = lax.dot_general(
                q_h, k_g, (((1,), (1,)), ((), ())), preferred_element_type=jnp.float32
            )
            s = jnp.where(valid, s * scale, -jnp.inf)
            top = jnp.max(s, axis=1, keepdims=True)
            e = jnp.exp(s - top)
            total = jnp.sum(e, axis=1, keepdims=True)
            w = (e / total).astype(jnp.bfloat16)
            o = jnp.dot(w, v_g, preferred_element_type=jnp.float32)
            acc = jnp.where(lane == part, o, acc)
        att_ref[:, lanes] = acc.astype(jnp.bfloat16)
    mixed = jnp.dot(att_ref[...], wo_ref[...], preferred_element_type=jnp.float32)
    lat = lat_ref[...].reshape(cells, channels)
    out_ref[...] = (lat.astype(jnp.float32) + mixed).astype(out_ref.dtype)


def attend_and_mix(query, center, rims, w_key, w_value, own_tile, w_output):
    rows, cols, channels = own_tile.shape
    cells = rows * cols
    center_flat = center.reshape(-1, channels)
    rim_flat = rims.reshape(2, -1, channels)
    count = center_flat.shape[0] + 2 * rim_flat.shape[1]
    positions = -(-count // 128) * 128
    tail = jnp.zeros((positions - count, channels), jnp.bfloat16)

    def both(weight):
        mid = project(center_flat, weight)
        edge = project(rim_flat.reshape(-1, channels), weight).reshape(rim_flat.shape)
        return jnp.concatenate([edge[0], mid, edge[1], tail], axis=0)

    key_flat = both(w_key)
    value_flat = both(w_value)
    vmem = pl.BlockSpec(memory_space=pltpu.VMEM)
    out = pl.pallas_call(
        attention_kernel,
        out_shape=jax.ShapeDtypeStruct((cells, channels), own_tile.dtype),
        in_specs=[vmem] * 5,
        out_specs=vmem,
        scratch_shapes=[pltpu.VMEM((cells, channels), jnp.bfloat16)],
    )(query.reshape(cells, channels), key_flat, value_flat, own_tile, w_output)
    return out.reshape(rows, cols, channels)


def widen_tiles(field, margin):
    west = jnp.roll(field, 1, axis=0)[:, :, -margin:]
    east = jnp.roll(field, -1, axis=0)[:, :, :margin]
    return jnp.concatenate([west, field, east], axis=2)


def pick_all(table, edges):
    number = edges.shape[0]
    tile_hit = jnp.arange(number, dtype=jnp.int32) == table[..., 0:1]
    edge_hit = jnp.arange(2, dtype=jnp.int32) == table[..., 1:2]
    chosen = (tile_hit[..., :, None] & edge_hit[..., None, :]).astype(edges.dtype)
    got = jnp.einsum("...nf,nfrwc->...rwc", chosen, edges, preferred_element_type=jnp.float32)
    return got.astype(edges.dtype)


def raw_gather(block, axis, radix=4):
    count = lax.axis_size(axis)
    me = lax.axis_index(axis)
    if count & (count - 1):
        return lax.all_gather(block[None], axis, axis=0, tiled=True), (lambda j: j)
    levels = []
    stride = 1
    while stride < count:
        r = min(radix, count // stride)
        levels.append((stride, r))
        stride *= r
    held = block
    for stride, r in reversed(levels):
        got = [held]
        for d in range(1, r):
            got.append(lax.ppermute(held, axis, [(i, i ^ (d * stride)) for i in range(count)]))
        held = jnp.stack(got)

    def locate(j):
        gap = j ^ me
        flat = 0
        for stride, r in levels:
            flat = flat * r + (gap // stride) % r
        return flat

    return held.reshape((count,) + block.shape), locate


def fetch_rim(raw, locate, seam_pair, depth):
    count = raw.shape[0]
    src, edge, orient = seam_pair[0], seam_pair[1], seam_pair[2]

    def rows_of(j):
        tile = lax.dynamic_index_in_dim(raw, locate(j), 0, keepdims=False)
        return lax.dynamic_slice_in_dim(tile, edge * depth, depth, 0)

    rim = jnp.concatenate(
        [rows_of((src + count - 1) % count)[:, -depth:], rows_of(src), rows_of((src + 1) % count)[:, :depth]],
        axis=1,
    )
    rim = jnp.where(orient % 2 == 1, rim[:, ::-1], rim)
    return jnp.where(orient // 2 == 1, rim[::-1], rim)


def local(latents, norm_gain, metric, w_query, w_key, w_value, w_output, seam_table):
    own_tile = latents[0]
    channels = own_tile.shape[-1]
    normed = normalize(own_tile, norm_gain)
    margin = 1
    seam_rows = seam_table[0]
    widened = padded_2(normed[None], (("blk", 2),), margin)
    rows1 = jnp.stack([normed[0], normed[-1]])
    raw1, locate1 = raw_gather(rows1, "blk")
    padded = jnp.concatenate(
        [fetch_rim(raw1, locate1, seam_rows[0], 1), widened[0], fetch_rim(raw1, locate1, seam_rows[1], 1)],
        axis=0,
    )
    smoothed = smooth(padded, metric[0])
    query = project(smoothed, w_query)
    field_wide = padded_2(smoothed[None], (("blk", 2),), RADIUS)
    rows3 = jnp.concatenate([smoothed[:RADIUS], smoothed[-RADIUS:]], axis=0)
    raw3, locate3 = raw_gather(rows3, "blk")
    arrived = jnp.stack([fetch_rim(raw3, locate3, seam_rows[e], RADIUS) for e in range(2)])
    return attend_and_mix(query, field_wide[0], arrived, w_key, w_value, own_tile, w_output)[None]


def solution(mesh):
    return jax.shard_map(
        local,
        mesh=mesh,
        in_specs=(
            P(("group", "blk"), None, None, None),
            P(),
            P("blk", None, None, None),
            P(),
            P(),
            P(),
            P(),
            P("blk", None, None),
        ),
        out_specs=P(("group", "blk"), None, None, None),
        check_vma=False,
    )
```

```python
import jax
import jax.numpy as jnp
from jax import lax
from jax.sharding import PartitionSpec as P
from jax.experimental import pallas as pl
from jax.experimental.pallas import tpu as pltpu

HEADS = 8
RADIUS = 3


def padded_2(array, sides, width):
    for axis, dim in sides:
        count, length = (lax.axis_size(axis), array.shape[dim])
        up = [(i, (i + 1) % count) for i in range(count)]
        down = [(j, i) for i, j in up]
        last = lax.slice_in_dim(array, length - width, length, axis=dim)
        first = lax.slice_in_dim(array, 0, width, axis=dim)
        before = lax.ppermute(last, axis, up)
        after = lax.ppermute(first, axis, down)
        array = jnp.concatenate([before, array, after], axis=dim)
    return array


def normalize(latents, norm_gain):
    values = latents.astype(jnp.float32)
    factor = lax.rsqrt(jnp.mean(values * values, axis=-1, keepdims=True) + 1e-05)
    return (values * factor * norm_gain).astype(jnp.bfloat16)


def pick_rims(seam_rows, piece):
    number = piece.shape[0]
    tile_ids = jnp.arange(number, dtype=jnp.int32)
    tile_hit = tile_ids[None, :] == seam_rows[:, 0:1]
    edge_hit = jnp.arange(2, dtype=jnp.int32)[None, :] == seam_rows[:, 1:2]
    chosen = (tile_hit[:, :, None] & edge_hit[:, None, :]).astype(piece.dtype)
    return jnp.einsum("enf,nfrwc->erwc", chosen, piece, preferred_element_type=jnp.float32)


def edge_rows(widened, margin):
    return jnp.stack([widened[:, :margin], widened[:, -margin:]], axis=1)


def orient_rims(received, seam_pair):
    arrived = received.astype(jnp.bfloat16)
    orient = seam_pair[:, 2]
    flip_along = (orient % 2 == 1)[:, None, None, None]
    arrived = jnp.where(flip_along, arrived[:, :, ::-1], arrived)
    flip_across = (orient // 2 == 1)[:, None, None, None]
    return jnp.where(flip_across, arrived[:, ::-1], arrived)


def place_rims(widened, received, seam_pair):
    arrived = orient_rims(received, seam_pair)
    return jnp.concatenate([arrived[0], widened, arrived[1]], axis=0)


def smooth(padded, metric):
    rows, cols = (metric.shape[-2], metric.shape[-1])
    total = jnp.zeros((rows, cols, padded.shape[-1]), jnp.float32)
    for stencil in range(9):
        row_off = stencil // 3
        col_off = stencil % 3
        total = (
            total
            + metric[stencil, :, :, None]
            * padded[row_off : row_off + rows, col_off : col_off + cols, :]
        )
    return total.astype(jnp.bfloat16)


def project(values, weight):
    shape = values.shape
    flat = values.reshape(-1, shape[-1])
    return (
        jnp.dot(flat, weight, preferred_element_type=jnp.float32)
        .astype(jnp.bfloat16)
        .reshape(shape[:-1] + (weight.shape[1],))
    )


def attention_kernel(q_ref, k_ref, v_ref, lat_ref, wo_ref, out_ref, att_ref):
    cells, channels = q_ref.shape
    positions = k_ref.shape[0]
    rows, cols = lat_ref.shape[0], lat_ref.shape[1]
    wide = cols + 2 * RADIUS
    span = 2 * RADIUS + 1
    head_size = channels // HEADS
    group = 128
    scale = head_size ** (-0.5)
    cell = lax.broadcasted_iota(jnp.int32, (cells, positions), 0)
    place = lax.broadcasted_iota(jnp.int32, (cells, positions), 1)
    row_gap = place // wide - cell // cols
    col_gap = place % wide - cell % cols
    valid = (row_gap >= 0) & (row_gap < span) & (col_gap >= 0) & (col_gap < span)
    lane = lax.broadcasted_iota(jnp.int32, (cells, group), 1) // head_size
    for g in range(channels // group):
        lanes = slice(g * group, (g + 1) * group)
        q_g = q_ref[:, lanes]
        k_g = k_ref[:, lanes]
        v_g = v_ref[:, lanes]
        acc = jnp.zeros((cells, group), jnp.float32)
        for part in range(group // head_size):
            q_h = jnp.where(lane == part, q_g, jnp.zeros_like(q_g))
            s = lax.dot_general(
                q_h, k_g, (((1,), (1,)), ((), ())), preferred_element_type=jnp.float32
            )
            s = jnp.where(valid, s * scale, -jnp.inf)
            top = jnp.max(s, axis=1, keepdims=True)
            e = jnp.exp(s - top)
            total = jnp.sum(e, axis=1, keepdims=True)
            w = (e / total).astype(jnp.bfloat16)
            o = jnp.dot(w, v_g, preferred_element_type=jnp.float32)
            acc = jnp.where(lane == part, o, acc)
        att_ref[:, lanes] = acc.astype(jnp.bfloat16)
    mixed = jnp.dot(att_ref[...], wo_ref[...], preferred_element_type=jnp.float32)
    lat = lat_ref[...].reshape(cells, channels)
    out_ref[...] = (lat.astype(jnp.float32) + mixed).astype(out_ref.dtype)


def attend_and_mix(query, center, rims, w_key, w_value, own_tile, w_output):
    rows, cols, channels = own_tile.shape
    cells = rows * cols
    center_flat = center.reshape(-1, channels)
    rim_flat = rims.reshape(2, -1, channels)
    count = center_flat.shape[0] + 2 * rim_flat.shape[1]
    positions = -(-count // 128) * 128
    tail = jnp.zeros((positions - count, channels), jnp.bfloat16)

    def both(weight):
        mid = project(center_flat, weight)
        edge = project(rim_flat.reshape(-1, channels), weight).reshape(rim_flat.shape)
        return jnp.concatenate([edge[0], mid, edge[1], tail], axis=0)

    key_flat = both(w_key)
    value_flat = both(w_value)
    vmem = pl.BlockSpec(memory_space=pltpu.VMEM)
    out = pl.pallas_call(
        attention_kernel,
        out_shape=jax.ShapeDtypeStruct((cells, channels), own_tile.dtype),
        in_specs=[vmem] * 5,
        out_specs=vmem,
        scratch_shapes=[pltpu.VMEM((cells, channels), jnp.bfloat16)],
    )(query.reshape(cells, channels), key_flat, value_flat, own_tile, w_output)
    return out.reshape(rows, cols, channels)


def widen_tiles(field, margin):
    west = jnp.roll(field, 1, axis=0)[:, :, -margin:]
    east = jnp.roll(field, -1, axis=0)[:, :, :margin]
    return jnp.concatenate([west, field, east], axis=2)


def pick_all(table, edges):
    number = edges.shape[0]
    tile_hit = jnp.arange(number, dtype=jnp.int32) == table[..., 0:1]
    edge_hit = jnp.arange(2, dtype=jnp.int32) == table[..., 1:2]
    chosen = (tile_hit[..., :, None] & edge_hit[..., None, :]).astype(edges.dtype)
    got = jnp.einsum("...nf,nfrwc->...rwc", chosen, edges, preferred_element_type=jnp.float32)
    return got.astype(edges.dtype)


def doubling_gather(block, axis, radix=4):
    count = lax.axis_size(axis)
    if count & (count - 1):
        return lax.all_gather(block, axis, axis=0, tiled=True)
    me = lax.axis_index(axis)
    levels = []
    stride = 1
    while stride < count:
        r = min(radix, count // stride)
        levels.append((stride, r))
        stride *= r
    held = block
    for stride, r in reversed(levels):
        got = [held]
        for d in range(1, r):
            got.append(lax.ppermute(held, axis, [(i, i ^ (d * stride)) for i in range(count)]))
        digit = (me // stride) % r
        held = jnp.take(jnp.stack(got), digit ^ jnp.arange(r, dtype=jnp.int32), axis=0)
    depth = len(levels)
    held = jnp.transpose(held, tuple(reversed(range(depth))) + tuple(range(depth, held.ndim)))
    return held.reshape((count * block.shape[0],) + block.shape[1:])


def raw_gather(block, axis, radix=4):
    count = lax.axis_size(axis)
    me = lax.axis_index(axis)
    if count & (count - 1):
        return lax.all_gather(block[None], axis, axis=0, tiled=True), (lambda j: j)
    levels = []
    stride = 1
    while stride < count:
        r = min(radix, count // stride)
        levels.append((stride, r))
        stride *= r
    held = block
    for stride, r in reversed(levels):
        got = [held]
        for d in range(1, r):
            got.append(lax.ppermute(held, axis, [(i, i ^ (d * stride)) for i in range(count)]))
        held = jnp.stack(got)

    def locate(j):
        gap = j ^ me
        flat = 0
        for stride, r in levels:
            flat = flat * r + (gap // stride) % r
        return flat

    return held.reshape((count,) + block.shape), locate


def fetch_rim(raw, locate, seam_pair, depth):
    count = raw.shape[0]
    src, edge, orient = seam_pair[0], seam_pair[1], seam_pair[2]

    def rows_of(j):
        tile = lax.dynamic_index_in_dim(raw, locate(j), 0, keepdims=False)
        return lax.dynamic_slice_in_dim(tile, edge * depth, depth, 0)

    rim = jnp.concatenate(
        [rows_of((src + count - 1) % count)[:, -depth:], rows_of(src), rows_of((src + 1) % count)[:, :depth]],
        axis=1,
    )
    rim = jnp.where(orient % 2 == 1, rim[:, ::-1], rim)
    return jnp.where(orient // 2 == 1, rim[::-1], rim)


def local(latents, norm_gain, metric, w_query, w_key, w_value, w_output, seam_table):
    own_tile = latents[0]
    channels = own_tile.shape[-1]
    normed = normalize(own_tile, norm_gain)
    margin = 1
    seam_rows = seam_table[0]
    widened = padded_2(normed[None], (("blk", 2),), margin)
    rows1 = jnp.stack([normed[0], normed[-1]])
    got1 = widen_tiles(doubling_gather(rows1[None], "blk"), 1)
    received = pick_all(seam_rows, got1[:, :, None])
    padded = place_rims(widened[0], received, seam_rows)
    smoothed = smooth(padded, metric[0])
    query = project(smoothed, w_query)
    field_wide = padded_2(smoothed[None], (("blk", 2),), RADIUS)
    rows3 = jnp.concatenate([smoothed[:RADIUS], smoothed[-RADIUS:]], axis=0)
    raw3, locate3 = raw_gather(rows3, "blk")
    arrived = jnp.stack([fetch_rim(raw3, locate3, seam_rows[e], RADIUS) for e in range(2)])
    return attend_and_mix(query, field_wide[0], arrived, w_key, w_value, own_tile, w_output)[None]


def solution(mesh):
    return jax.shard_map(
        local,
        mesh=mesh,
        in_specs=(
            P(("group", "blk"), None, None, None),
            P(),
            P("blk", None, None, None),
            P(),
            P(),
            P(),
            P(),
            P("blk", None, None),
        ),
        out_specs=P(("group", "blk"), None, None, None),
        check_vma=False,
    )
```

```python
import jax
import jax.numpy as jnp
from jax import lax
from jax.sharding import PartitionSpec as P
from jax.experimental import pallas as pl
from jax.experimental.pallas import tpu as pltpu

HEADS = 8
RADIUS = 3


def padded_2(array, sides, width):
    for axis, dim in sides:
        count, length = (lax.axis_size(axis), array.shape[dim])
        up = [(i, (i + 1) % count) for i in range(count)]
        down = [(j, i) for i, j in up]
        last = lax.slice_in_dim(array, length - width, length, axis=dim)
        first = lax.slice_in_dim(array, 0, width, axis=dim)
        before = lax.ppermute(last, axis, up)
        after = lax.ppermute(first, axis, down)
        array = jnp.concatenate([before, array, after], axis=dim)
    return array


def normalize(latents, norm_gain):
    values = latents.astype(jnp.float32)
    factor = lax.rsqrt(jnp.mean(values * values, axis=-1, keepdims=True) + 1e-05)
    return (values * factor * norm_gain).astype(jnp.bfloat16)


def pick_rims(seam_rows, piece):
    number = piece.shape[0]
    tile_ids = jnp.arange(number, dtype=jnp.int32)
    tile_hit = tile_ids[None, :] == seam_rows[:, 0:1]
    edge_hit = jnp.arange(2, dtype=jnp.int32)[None, :] == seam_rows[:, 1:2]
    chosen = (tile_hit[:, :, None] & edge_hit[:, None, :]).astype(piece.dtype)
    return jnp.einsum("enf,nfrwc->erwc", chosen, piece, preferred_element_type=jnp.float32)


def edge_rows(widened, margin):
    return jnp.stack([widened[:, :margin], widened[:, -margin:]], axis=1)


def orient_rims(received, seam_pair):
    arrived = received.astype(jnp.bfloat16)
    orient = seam_pair[:, 2]
    flip_along = (orient % 2 == 1)[:, None, None, None]
    arrived = jnp.where(flip_along, arrived[:, :, ::-1], arrived)
    flip_across = (orient // 2 == 1)[:, None, None, None]
    return jnp.where(flip_across, arrived[:, ::-1], arrived)


def place_rims(widened, received, seam_pair):
    arrived = orient_rims(received, seam_pair)
    return jnp.concatenate([arrived[0], widened, arrived[1]], axis=0)


def smooth(padded, metric):
    rows, cols = (metric.shape[-2], metric.shape[-1])
    total = jnp.zeros((rows, cols, padded.shape[-1]), jnp.float32)
    for stencil in range(9):
        row_off = stencil // 3
        col_off = stencil % 3
        total = (
            total
            + metric[stencil, :, :, None]
            * padded[row_off : row_off + rows, col_off : col_off + cols, :]
        )
    return total.astype(jnp.bfloat16)


def project(values, weight):
    shape = values.shape
    flat = values.reshape(-1, shape[-1])
    return (
        jnp.dot(flat, weight, preferred_element_type=jnp.float32)
        .astype(jnp.bfloat16)
        .reshape(shape[:-1] + (weight.shape[1],))
    )


def attention_kernel(
    q_ref, kc_ref, kr_ref, vc_ref, vr_ref, lat_ref, wo_ref, out_ref, att_ref, k_ref, v_ref
):
    middle = kc_ref.shape[0]
    k_ref[pl.ds(0, middle)] = kc_ref[...]
    k_ref[pl.ds(middle, kr_ref.shape[0])] = kr_ref[...]
    v_ref[pl.ds(0, middle)] = vc_ref[...]
    v_ref[pl.ds(middle, vr_ref.shape[0])] = vr_ref[...]
    cells, channels = q_ref.shape
    positions = k_ref.shape[0]
    rows, cols = lat_ref.shape[0], lat_ref.shape[1]
    wide = cols + 2 * RADIUS
    span = 2 * RADIUS + 1
    head_size = channels // HEADS
    group = 128
    scale = head_size ** (-0.5)
    cell = lax.broadcasted_iota(jnp.int32, (cells, positions), 0)
    place = lax.broadcasted_iota(jnp.int32, (cells, positions), 1)
    rim_rows = RADIUS * wide
    rows_total = lat_ref.shape[0] + 2 * RADIUS
    key_row = jnp.where(
        place < middle,
        place // wide + RADIUS,
        jnp.where(
            place < middle + rim_rows,
            (place - middle) // wide,
            (place - middle - rim_rows) // wide + rows_total - RADIUS,
        ),
    )
    key_row = jnp.where(place < middle + 2 * rim_rows, key_row, rows_total + span)
    key_col = jnp.where(place < middle, place % wide, (place - middle) % wide)
    row_gap = key_row - cell // cols
    col_gap = key_col - cell % cols
    valid = (row_gap >= 0) & (row_gap < span) & (col_gap >= 0) & (col_gap < span)
    lane = lax.broadcasted_iota(jnp.int32, (cells, group), 1) // head_size
    for g in range(channels // group):
        lanes = slice(g * group, (g + 1) * group)
        q_g = q_ref[:, lanes]
        k_g = k_ref[:, lanes]
        v_g = v_ref[:, lanes]
        acc = jnp.zeros((cells, group), jnp.float32)
        for part in range(group // head_size):
            q_h = jnp.where(lane == part, q_g, jnp.zeros_like(q_g))
            s = lax.dot_general(
                q_h, k_g, (((1,), (1,)), ((), ())), preferred_element_type=jnp.float32
            )
            s = jnp.where(valid, s * scale, -jnp.inf)
            top = jnp.max(s, axis=1, keepdims=True)
            e = jnp.exp(s - top)
            total = jnp.sum(e, axis=1, keepdims=True)
            w = (e / total).astype(jnp.bfloat16)
            o = jnp.dot(w, v_g, preferred_element_type=jnp.float32)
            acc = jnp.where(lane == part, o, acc)
        att_ref[:, lanes] = acc.astype(jnp.bfloat16)
    mixed = jnp.dot(att_ref[...], wo_ref[...], preferred_element_type=jnp.float32)
    lat = lat_ref[...].reshape(cells, channels)
    out_ref[...] = (lat.astype(jnp.float32) + mixed).astype(out_ref.dtype)


def attend_and_mix(query, center, rims, w_key, w_value, own_tile, w_output):
    rows, cols, channels = own_tile.shape
    cells = rows * cols
    center_flat = center.reshape(-1, channels)
    rim_flat = rims.reshape(-1, channels)
    count = center_flat.shape[0] + rim_flat.shape[0]
    positions = -(-count // 128) * 128
    rim_flat = jnp.pad(rim_flat, ((0, positions - count), (0, 0)))
    vmem = pl.BlockSpec(memory_space=pltpu.VMEM)
    out = pl.pallas_call(
        attention_kernel,
        out_shape=jax.ShapeDtypeStruct((cells, channels), own_tile.dtype),
        in_specs=[vmem] * 7,
        out_specs=vmem,
        scratch_shapes=[
            pltpu.VMEM((cells, channels), jnp.bfloat16),
            pltpu.VMEM((positions, channels), jnp.bfloat16),
            pltpu.VMEM((positions, channels), jnp.bfloat16),
        ],
    )(
        query.reshape(cells, channels),
        project(center_flat, w_key),
        project(rim_flat, w_key),
        project(center_flat, w_value),
        project(rim_flat, w_value),
        own_tile,
        w_output,
    )
    return out.reshape(rows, cols, channels)


def widen_tiles(field, margin):
    west = jnp.roll(field, 1, axis=0)[:, :, -margin:]
    east = jnp.roll(field, -1, axis=0)[:, :, :margin]
    return jnp.concatenate([west, field, east], axis=2)


def pick_all(table, edges):
    number = edges.shape[0]
    tile_hit = jnp.arange(number, dtype=jnp.int32) == table[..., 0:1]
    edge_hit = jnp.arange(2, dtype=jnp.int32) == table[..., 1:2]
    chosen = (tile_hit[..., :, None] & edge_hit[..., None, :]).astype(edges.dtype)
    got = jnp.einsum("...nf,nfrwc->...rwc", chosen, edges, preferred_element_type=jnp.float32)
    return got.astype(edges.dtype)


def doubling_gather(block, axis, radix=4):
    count = lax.axis_size(axis)
    if count & (count - 1):
        return lax.all_gather(block, axis, axis=0, tiled=True)
    me = lax.axis_index(axis)
    levels = []
    stride = 1
    while stride < count:
        r = min(radix, count // stride)
        levels.append((stride, r))
        stride *= r
    held = block
    for stride, r in reversed(levels):
        got = [held]
        for d in range(1, r):
            got.append(lax.ppermute(held, axis, [(i, i ^ (d * stride)) for i in range(count)]))
        digit = (me // stride) % r
        held = jnp.take(jnp.stack(got), digit ^ jnp.arange(r, dtype=jnp.int32), axis=0)
    depth = len(levels)
    held = jnp.transpose(held, tuple(reversed(range(depth))) + tuple(range(depth, held.ndim)))
    return held.reshape((count * block.shape[0],) + block.shape[1:])


def local(latents, norm_gain, metric, w_query, w_key, w_value, w_output, seam_table):
    own_tile = latents[0]
    channels = own_tile.shape[-1]
    normed = normalize(own_tile, norm_gain)
    margin = 1
    seam_rows = seam_table[0]
    widened = padded_2(normed[None], (("blk", 2),), margin)
    rows1 = jnp.stack([normed[0], normed[-1]])
    got1 = widen_tiles(doubling_gather(rows1[None], "blk"), 1)
    received = pick_all(seam_rows, got1[:, :, None])
    padded = place_rims(widened[0], received, seam_rows)
    smoothed = smooth(padded, metric[0])
    query = project(smoothed, w_query)
    field_wide = padded_2(smoothed[None], (("blk", 2),), RADIUS)
    rows3 = jnp.concatenate([smoothed[:RADIUS], smoothed[-RADIUS:]], axis=0)
    got3 = widen_tiles(doubling_gather(rows3[None], "blk"), RADIUS)
    edges3 = jnp.stack([got3[:, :RADIUS], got3[:, RADIUS:]], axis=1)
    field_got = pick_all(seam_rows, edges3)
    arrived = orient_rims(field_got, seam_rows)
    return attend_and_mix(query, field_wide[0], arrived, w_key, w_value, own_tile, w_output)[None]


def solution(mesh):
    return jax.shard_map(
        local,
        mesh=mesh,
        in_specs=(
            P(("group", "blk"), None, None, None),
            P(),
            P("blk", None, None, None),
            P(),
            P(),
            P(),
            P(),
            P("blk", None, None),
        ),
        out_specs=P(("group", "blk"), None, None, None),
        check_vma=False,
    )
```

```python
import jax
import jax.numpy as jnp
from jax import lax
from jax.sharding import PartitionSpec as P
from jax.experimental import pallas as pl
from jax.experimental.pallas import tpu as pltpu

HEADS = 8
RADIUS = 3


def padded_2(array, sides, width):
    for axis, dim in sides:
        count, length = (lax.axis_size(axis), array.shape[dim])
        up = [(i, (i + 1) % count) for i in range(count)]
        down = [(j, i) for i, j in up]
        last = lax.slice_in_dim(array, length - width, length, axis=dim)
        first = lax.slice_in_dim(array, 0, width, axis=dim)
        before = lax.ppermute(last, axis, up)
        after = lax.ppermute(first, axis, down)
        array = jnp.concatenate([before, array, after], axis=dim)
    return array


def normalize(latents, norm_gain):
    values = latents.astype(jnp.float32)
    factor = lax.rsqrt(jnp.mean(values * values, axis=-1, keepdims=True) + 1e-05)
    return (values * factor * norm_gain).astype(jnp.bfloat16)


def pick_rims(seam_rows, piece):
    number = piece.shape[0]
    tile_ids = jnp.arange(number, dtype=jnp.int32)
    tile_hit = tile_ids[None, :] == seam_rows[:, 0:1]
    edge_hit = jnp.arange(2, dtype=jnp.int32)[None, :] == seam_rows[:, 1:2]
    chosen = (tile_hit[:, :, None] & edge_hit[:, None, :]).astype(piece.dtype)
    return jnp.einsum("enf,nfrwc->erwc", chosen, piece, preferred_element_type=jnp.float32)


def edge_rows(widened, margin):
    return jnp.stack([widened[:, :margin], widened[:, -margin:]], axis=1)


def orient_rims(received, seam_pair):
    arrived = received.astype(jnp.bfloat16)
    orient = seam_pair[:, 2]
    flip_along = (orient % 2 == 1)[:, None, None, None]
    arrived = jnp.where(flip_along, arrived[:, :, ::-1], arrived)
    flip_across = (orient // 2 == 1)[:, None, None, None]
    return jnp.where(flip_across, arrived[:, ::-1], arrived)


def place_rims(widened, received, seam_pair):
    arrived = orient_rims(received, seam_pair)
    return jnp.concatenate([arrived[0], widened, arrived[1]], axis=0)


def smooth(padded, metric):
    rows, cols = (metric.shape[-2], metric.shape[-1])
    total = jnp.zeros((rows, cols, padded.shape[-1]), jnp.float32)
    for stencil in range(9):
        row_off = stencil // 3
        col_off = stencil % 3
        total = (
            total
            + metric[stencil, :, :, None]
            * padded[row_off : row_off + rows, col_off : col_off + cols, :]
        )
    return total.astype(jnp.bfloat16)


def project(values, weight):
    shape = values.shape
    flat = values.reshape(-1, shape[-1])
    return (
        jnp.dot(flat, weight, preferred_element_type=jnp.float32)
        .astype(jnp.bfloat16)
        .reshape(shape[:-1] + (weight.shape[1],))
    )


def attention_kernel(
    q_ref, kc_ref, vc_ref, rim_ref, wk_ref, wv_ref, lat_ref, wo_ref, out_ref, att_ref, k_ref, v_ref
):
    middle = kc_ref.shape[0]
    extra = rim_ref.shape[0]
    rim = rim_ref[...]
    k_ref[pl.ds(0, middle)] = kc_ref[...]
    k_ref[pl.ds(middle, extra)] = jnp.dot(
        rim, wk_ref[...], preferred_element_type=jnp.float32
    ).astype(k_ref.dtype)
    v_ref[pl.ds(0, middle)] = vc_ref[...]
    v_ref[pl.ds(middle, extra)] = jnp.dot(
        rim, wv_ref[...], preferred_element_type=jnp.float32
    ).astype(v_ref.dtype)
    cells, channels = q_ref.shape
    positions = k_ref.shape[0]
    rows, cols = lat_ref.shape[0], lat_ref.shape[1]
    wide = cols + 2 * RADIUS
    span = 2 * RADIUS + 1
    head_size = channels // HEADS
    group = 128
    scale = head_size ** (-0.5)
    cell = lax.broadcasted_iota(jnp.int32, (cells, positions), 0)
    place = lax.broadcasted_iota(jnp.int32, (cells, positions), 1)
    rim_rows = RADIUS * wide
    rows_total = lat_ref.shape[0] + 2 * RADIUS
    key_row = jnp.where(
        place < middle,
        place // wide + RADIUS,
        jnp.where(
            place < middle + rim_rows,
            (place - middle) // wide,
            (place - middle - rim_rows) // wide + rows_total - RADIUS,
        ),
    )
    key_row = jnp.where(place < middle + 2 * rim_rows, key_row, rows_total + span)
    key_col = jnp.where(place < middle, place % wide, (place - middle) % wide)
    row_gap = key_row - cell // cols
    col_gap = key_col - cell % cols
    valid = (row_gap >= 0) & (row_gap < span) & (col_gap >= 0) & (col_gap < span)
    lane = lax.broadcasted_iota(jnp.int32, (cells, group), 1) // head_size
    for g in range(channels // group):
        lanes = slice(g * group, (g + 1) * group)
        q_g = q_ref[:, lanes]
        k_g = k_ref[:, lanes]
        v_g = v_ref[:, lanes]
        acc = jnp.zeros((cells, group), jnp.float32)
        for part in range(group // head_size):
            q_h = jnp.where(lane == part, q_g, jnp.zeros_like(q_g))
            s = lax.dot_general(
                q_h, k_g, (((1,), (1,)), ((), ())), preferred_element_type=jnp.float32
            )
            s = jnp.where(valid, s * scale, -jnp.inf)
            top = jnp.max(s, axis=1, keepdims=True)
            e = jnp.exp(s - top)
            total = jnp.sum(e, axis=1, keepdims=True)
            w = (e / total).astype(jnp.bfloat16)
            o = jnp.dot(w, v_g, preferred_element_type=jnp.float32)
            acc = jnp.where(lane == part, o, acc)
        att_ref[:, lanes] = acc.astype(jnp.bfloat16)
    mixed = jnp.dot(att_ref[...], wo_ref[...], preferred_element_type=jnp.float32)
    lat = lat_ref[...].reshape(cells, channels)
    out_ref[...] = (lat.astype(jnp.float32) + mixed).astype(out_ref.dtype)


def attend_and_mix(query, center, rims, w_key, w_value, own_tile, w_output):
    rows, cols, channels = own_tile.shape
    cells = rows * cols
    center_flat = center.reshape(-1, channels)
    rim_flat = rims.reshape(-1, channels)
    count = center_flat.shape[0] + rim_flat.shape[0]
    positions = -(-count // 128) * 128
    rim_flat = jnp.pad(rim_flat, ((0, positions - count), (0, 0)))
    vmem = pl.BlockSpec(memory_space=pltpu.VMEM)
    out = pl.pallas_call(
        attention_kernel,
        out_shape=jax.ShapeDtypeStruct((cells, channels), own_tile.dtype),
        in_specs=[vmem] * 8,
        out_specs=vmem,
        scratch_shapes=[
            pltpu.VMEM((cells, channels), jnp.bfloat16),
            pltpu.VMEM((positions, channels), jnp.bfloat16),
            pltpu.VMEM((positions, channels), jnp.bfloat16),
        ],
    )(
        query.reshape(cells, channels),
        project(center_flat, w_key),
        project(center_flat, w_value),
        rim_flat,
        w_key,
        w_value,
        own_tile,
        w_output,
    )
    return out.reshape(rows, cols, channels)


def widen_tiles(field, margin):
    west = jnp.roll(field, 1, axis=0)[:, :, -margin:]
    east = jnp.roll(field, -1, axis=0)[:, :, :margin]
    return jnp.concatenate([west, field, east], axis=2)


def pick_all(table, edges):
    number = edges.shape[0]
    tile_hit = jnp.arange(number, dtype=jnp.int32) == table[..., 0:1]
    edge_hit = jnp.arange(2, dtype=jnp.int32) == table[..., 1:2]
    chosen = (tile_hit[..., :, None] & edge_hit[..., None, :]).astype(edges.dtype)
    got = jnp.einsum("...nf,nfrwc->...rwc", chosen, edges, preferred_element_type=jnp.float32)
    return got.astype(edges.dtype)


def doubling_gather(block, axis, radix=4):
    count = lax.axis_size(axis)
    if count & (count - 1):
        return lax.all_gather(block, axis, axis=0, tiled=True)
    me = lax.axis_index(axis)
    levels = []
    stride = 1
    while stride < count:
        r = min(radix, count // stride)
        levels.append((stride, r))
        stride *= r
    held = block
    for stride, r in reversed(levels):
        got = [held]
        for d in range(1, r):
            got.append(lax.ppermute(held, axis, [(i, i ^ (d * stride)) for i in range(count)]))
        digit = (me // stride) % r
        held = jnp.take(jnp.stack(got), digit ^ jnp.arange(r, dtype=jnp.int32), axis=0)
    depth = len(levels)
    held = jnp.transpose(held, tuple(reversed(range(depth))) + tuple(range(depth, held.ndim)))
    return held.reshape((count * block.shape[0],) + block.shape[1:])


def local(latents, norm_gain, metric, w_query, w_key, w_value, w_output, seam_table):
    own_tile = latents[0]
    channels = own_tile.shape[-1]
    normed = normalize(own_tile, norm_gain)
    margin = 1
    seam_rows = seam_table[0]
    widened = padded_2(normed[None], (("blk", 2),), margin)
    rows1 = jnp.stack([normed[0], normed[-1]])
    got1 = widen_tiles(doubling_gather(rows1[None], "blk"), 1)
    received = pick_all(seam_rows, got1[:, :, None])
    padded = place_rims(widened[0], received, seam_rows)
    smoothed = smooth(padded, metric[0])
    query = project(smoothed, w_query)
    field_wide = padded_2(smoothed[None], (("blk", 2),), RADIUS)
    rows3 = jnp.concatenate([smoothed[:RADIUS], smoothed[-RADIUS:]], axis=0)
    got3 = widen_tiles(doubling_gather(rows3[None], "blk"), RADIUS)
    edges3 = jnp.stack([got3[:, :RADIUS], got3[:, RADIUS:]], axis=1)
    field_got = pick_all(seam_rows, edges3)
    arrived = orient_rims(field_got, seam_rows)
    return attend_and_mix(query, field_wide[0], arrived, w_key, w_value, own_tile, w_output)[None]


def solution(mesh):
    return jax.shard_map(
        local,
        mesh=mesh,
        in_specs=(
            P(("group", "blk"), None, None, None),
            P(),
            P("blk", None, None, None),
            P(),
            P(),
            P(),
            P(),
            P("blk", None, None),
        ),
        out_specs=P(("group", "blk"), None, None, None),
        check_vma=False,
    )
```

```python
import jax
import jax.numpy as jnp
from jax import lax
from jax.sharding import PartitionSpec as P
from jax.experimental import pallas as pl
from jax.experimental.pallas import tpu as pltpu

HEADS = 8
RADIUS = 3


def padded_2(array, sides, width):
    for axis, dim in sides:
        count, length = (lax.axis_size(axis), array.shape[dim])
        up = [(i, (i + 1) % count) for i in range(count)]
        down = [(j, i) for i, j in up]
        last = lax.slice_in_dim(array, length - width, length, axis=dim)
        first = lax.slice_in_dim(array, 0, width, axis=dim)
        before = lax.ppermute(last, axis, up)
        after = lax.ppermute(first, axis, down)
        array = jnp.concatenate([before, array, after], axis=dim)
    return array


def normalize(latents, norm_gain):
    values = latents.astype(jnp.float32)
    factor = lax.rsqrt(jnp.mean(values * values, axis=-1, keepdims=True) + 1e-05)
    return (values * factor * norm_gain).astype(jnp.bfloat16)


def pick_rims(seam_rows, piece):
    number = piece.shape[0]
    tile_ids = jnp.arange(number, dtype=jnp.int32)
    tile_hit = tile_ids[None, :] == seam_rows[:, 0:1]
    edge_hit = jnp.arange(2, dtype=jnp.int32)[None, :] == seam_rows[:, 1:2]
    chosen = (tile_hit[:, :, None] & edge_hit[:, None, :]).astype(piece.dtype)
    return jnp.einsum("enf,nfrwc->erwc", chosen, piece, preferred_element_type=jnp.float32)


def edge_rows(widened, margin):
    return jnp.stack([widened[:, :margin], widened[:, -margin:]], axis=1)


def orient_rims(received, seam_pair):
    arrived = received.astype(jnp.bfloat16)
    orient = seam_pair[:, 2]
    flip_along = (orient % 2 == 1)[:, None, None, None]
    arrived = jnp.where(flip_along, arrived[:, :, ::-1], arrived)
    flip_across = (orient // 2 == 1)[:, None, None, None]
    return jnp.where(flip_across, arrived[:, ::-1], arrived)


def place_rims(widened, received, seam_pair):
    arrived = orient_rims(received, seam_pair)
    return jnp.concatenate([arrived[0], widened, arrived[1]], axis=0)


def smooth(padded, metric):
    rows, cols = (metric.shape[-2], metric.shape[-1])
    total = jnp.zeros((rows, cols, padded.shape[-1]), jnp.float32)
    for stencil in range(9):
        row_off = stencil // 3
        col_off = stencil % 3
        total = (
            total
            + metric[stencil, :, :, None]
            * padded[row_off : row_off + rows, col_off : col_off + cols, :]
        )
    return total.astype(jnp.bfloat16)


def project(values, weight):
    shape = values.shape
    flat = values.reshape(-1, shape[-1])
    return (
        jnp.dot(flat, weight, preferred_element_type=jnp.float32)
        .astype(jnp.bfloat16)
        .reshape(shape[:-1] + (weight.shape[1],))
    )


def attention_kernel(
    q_ref, kc_ref, kr_ref, vc_ref, vr_ref, lat_ref, wo_ref, out_ref, att_ref, k_ref, v_ref
):
    middle = kc_ref.shape[0]
    k_ref[pl.ds(0, middle)] = kc_ref[...]
    k_ref[pl.ds(middle, kr_ref.shape[0])] = kr_ref[...]
    v_ref[pl.ds(0, middle)] = vc_ref[...]
    v_ref[pl.ds(middle, vr_ref.shape[0])] = vr_ref[...]
    cells, channels = q_ref.shape
    positions = k_ref.shape[0]
    rows, cols = lat_ref.shape[0], lat_ref.shape[1]
    wide = cols + 2 * RADIUS
    span = 2 * RADIUS + 1
    head_size = channels // HEADS
    group = 128
    scale = head_size ** (-0.5)
    cell = lax.broadcasted_iota(jnp.int32, (cells, positions), 0)
    place = lax.broadcasted_iota(jnp.int32, (cells, positions), 1)
    rim_rows = RADIUS * wide
    rows_total = lat_ref.shape[0] + 2 * RADIUS
    key_row = jnp.where(
        place < middle,
        place // wide + RADIUS,
        jnp.where(
            place < middle + rim_rows,
            (place - middle) // wide,
            (place - middle - rim_rows) // wide + rows_total - RADIUS,
        ),
    )
    key_row = jnp.where(place < middle + 2 * rim_rows, key_row, rows_total + span)
    key_col = jnp.where(place < middle, place % wide, (place - middle) % wide)
    row_gap = key_row - cell // cols
    col_gap = key_col - cell % cols
    valid = (row_gap >= 0) & (row_gap < span) & (col_gap >= 0) & (col_gap < span)
    lane = lax.broadcasted_iota(jnp.int32, (cells, group), 1) // head_size
    for g in range(channels // group):
        lanes = slice(g * group, (g + 1) * group)
        q_g = q_ref[:, lanes]
        k_g = k_ref[:, lanes]
        v_g = v_ref[:, lanes]
        acc = jnp.zeros((cells, group), jnp.float32)
        for part in range(group // head_size):
            q_h = jnp.where(lane == part, q_g, jnp.zeros_like(q_g))
            s = lax.dot_general(
                q_h, k_g, (((1,), (1,)), ((), ())), preferred_element_type=jnp.float32
            )
            s = jnp.where(valid, s * scale, -jnp.inf)
            top = jnp.max(s, axis=1, keepdims=True)
            e = jnp.exp(s - top)
            total = jnp.sum(e, axis=1, keepdims=True)
            w = (e / total).astype(jnp.bfloat16)
            o = jnp.dot(w, v_g, preferred_element_type=jnp.float32)
            acc = jnp.where(lane == part, o, acc)
        att_ref[:, lanes] = acc.astype(jnp.bfloat16)
    mixed = jnp.dot(att_ref[...], wo_ref[...], preferred_element_type=jnp.float32)
    lat = lat_ref[...].reshape(cells, channels)
    out_ref[...] = (lat.astype(jnp.float32) + mixed).astype(out_ref.dtype)


def attend_and_mix(query, center, rims, w_key, w_value, own_tile, w_output):
    rows, cols, channels = own_tile.shape
    cells = rows * cols
    center_flat = center.reshape(-1, channels)
    rim_flat = rims.reshape(-1, channels)
    count = center_flat.shape[0] + rim_flat.shape[0]
    positions = -(-count // 128) * 128
    rim_flat = jnp.pad(rim_flat, ((0, positions - count), (0, 0)))
    vmem = pl.BlockSpec(memory_space=pltpu.VMEM)
    out = pl.pallas_call(
        attention_kernel,
        out_shape=jax.ShapeDtypeStruct((cells, channels), own_tile.dtype),
        in_specs=[vmem] * 7,
        out_specs=vmem,
        scratch_shapes=[
            pltpu.VMEM((cells, channels), jnp.bfloat16),
            pltpu.VMEM((positions, channels), jnp.bfloat16),
            pltpu.VMEM((positions, channels), jnp.bfloat16),
        ],
    )(
        query.reshape(cells, channels),
        project(center_flat, w_key),
        project(rim_flat, w_key),
        project(center_flat, w_value),
        project(rim_flat, w_value),
        own_tile,
        w_output,
    )
    return out.reshape(rows, cols, channels)


def widen_tiles(field, margin):
    west = jnp.roll(field, 1, axis=0)[:, :, -margin:]
    east = jnp.roll(field, -1, axis=0)[:, :, :margin]
    return jnp.concatenate([west, field, east], axis=2)


def pick_all(table, edges):
    number = edges.shape[0]
    tile_hit = jnp.arange(number, dtype=jnp.int32) == table[..., 0:1]
    edge_hit = jnp.arange(2, dtype=jnp.int32) == table[..., 1:2]
    chosen = (tile_hit[..., :, None] & edge_hit[..., None, :]).astype(edges.dtype)
    got = jnp.einsum("...nf,nfrwc->...rwc", chosen, edges, preferred_element_type=jnp.float32)
    return got.astype(edges.dtype)


def doubling_gather(block, axis, radix=4):
    count = lax.axis_size(axis)
    if count & (count - 1):
        return lax.all_gather(block, axis, axis=0, tiled=True)
    me = lax.axis_index(axis)
    levels = []
    stride = 1
    while stride < count:
        r = min(radix, count // stride)
        levels.append((stride, r))
        stride *= r
    held = block
    for stride, r in reversed(levels):
        got = [held]
        for d in range(1, r):
            got.append(lax.ppermute(held, axis, [(i, i ^ (d * stride)) for i in range(count)]))
        digit = (me // stride) % r
        held = jnp.take(jnp.stack(got), digit ^ jnp.arange(r, dtype=jnp.int32), axis=0)
    depth = len(levels)
    held = jnp.transpose(held, tuple(reversed(range(depth))) + tuple(range(depth, held.ndim)))
    return held.reshape((count * block.shape[0],) + block.shape[1:])


def local(latents, norm_gain, metric, w_query, w_key, w_value, w_output, seam_table):
    own_tile = latents[0]
    channels = own_tile.shape[-1]
    seam_rows = seam_table[0]
    edges_raw = jnp.stack([own_tile[0], own_tile[-1]])
    got1 = normalize(doubling_gather(edges_raw[None], "blk"), norm_gain)
    sides = padded_2(own_tile[None], (("blk", 2),), 1)[0]
    normed = normalize(own_tile, norm_gain)
    widened = jnp.concatenate(
        [normalize(sides[:, :1], norm_gain), normed, normalize(sides[:, -1:], norm_gain)], axis=1
    )[None]
    got1 = widen_tiles(got1, 1)
    received = pick_all(seam_rows, got1[:, :, None])
    padded = place_rims(widened[0], received, seam_rows)
    smoothed = smooth(padded, metric[0])
    query = project(smoothed, w_query)
    field_wide = padded_2(smoothed[None], (("blk", 2),), RADIUS)
    rows3 = jnp.concatenate([smoothed[:RADIUS], smoothed[-RADIUS:]], axis=0)
    got3 = widen_tiles(doubling_gather(rows3[None], "blk"), RADIUS)
    edges3 = jnp.stack([got3[:, :RADIUS], got3[:, RADIUS:]], axis=1)
    field_got = pick_all(seam_rows, edges3)
    arrived = orient_rims(field_got, seam_rows)
    return attend_and_mix(query, field_wide[0], arrived, w_key, w_value, own_tile, w_output)[None]


def solution(mesh):
    return jax.shard_map(
        local,
        mesh=mesh,
        in_specs=(
            P(("group", "blk"), None, None, None),
            P(),
            P("blk", None, None, None),
            P(),
            P(),
            P(),
            P(),
            P("blk", None, None),
        ),
        out_specs=P(("group", "blk"), None, None, None),
        check_vma=False,
    )
```

```python
import jax
import jax.numpy as jnp
from jax import lax
from jax.sharding import PartitionSpec as P
from jax.experimental import pallas as pl
from jax.experimental.pallas import tpu as pltpu

HEADS = 8
RADIUS = 3


def padded_2(array, sides, width):
    for axis, dim in sides:
        count, length = (lax.axis_size(axis), array.shape[dim])
        up = [(i, (i + 1) % count) for i in range(count)]
        down = [(j, i) for i, j in up]
        last = lax.slice_in_dim(array, length - width, length, axis=dim)
        first = lax.slice_in_dim(array, 0, width, axis=dim)
        before = lax.ppermute(last, axis, up)
        after = lax.ppermute(first, axis, down)
        array = jnp.concatenate([before, array, after], axis=dim)
    return array


def normalize(latents, norm_gain):
    values = latents.astype(jnp.float32)
    factor = lax.rsqrt(jnp.mean(values * values, axis=-1, keepdims=True) + 1e-05)
    return (values * factor * norm_gain).astype(jnp.bfloat16)


def pick_rims(seam_rows, piece):
    number = piece.shape[0]
    tile_ids = jnp.arange(number, dtype=jnp.int32)
    tile_hit = tile_ids[None, :] == seam_rows[:, 0:1]
    edge_hit = jnp.arange(2, dtype=jnp.int32)[None, :] == seam_rows[:, 1:2]
    chosen = (tile_hit[:, :, None] & edge_hit[:, None, :]).astype(piece.dtype)
    return jnp.einsum("enf,nfrwc->erwc", chosen, piece, preferred_element_type=jnp.float32)


def edge_rows(widened, margin):
    return jnp.stack([widened[:, :margin], widened[:, -margin:]], axis=1)


def orient_rims(received, seam_pair):
    arrived = received.astype(jnp.bfloat16)
    orient = seam_pair[:, 2]
    flip_along = (orient % 2 == 1)[:, None, None, None]
    arrived = jnp.where(flip_along, arrived[:, :, ::-1], arrived)
    flip_across = (orient // 2 == 1)[:, None, None, None]
    return jnp.where(flip_across, arrived[:, ::-1], arrived)


def place_rims(widened, received, seam_pair):
    arrived = orient_rims(received, seam_pair)
    return jnp.concatenate([arrived[0], widened, arrived[1]], axis=0)


def smooth(padded, metric):
    rows, cols = (metric.shape[-2], metric.shape[-1])
    total = jnp.zeros((rows, cols, padded.shape[-1]), jnp.float32)
    for stencil in range(9):
        row_off = stencil // 3
        col_off = stencil % 3
        total = (
            total
            + metric[stencil, :, :, None]
            * padded[row_off : row_off + rows, col_off : col_off + cols, :]
        )
    return total.astype(jnp.bfloat16)


def project(values, weight):
    shape = values.shape
    flat = values.reshape(-1, shape[-1])
    return (
        jnp.dot(flat, weight, preferred_element_type=jnp.float32)
        .astype(jnp.bfloat16)
        .reshape(shape[:-1] + (weight.shape[1],))
    )


def attention_kernel(
    q_ref, kc_ref, kr_ref, vc_ref, vr_ref, lat_ref, wo_ref, out_ref, att_ref, k_ref, v_ref
):
    middle = kc_ref.shape[0]
    k_ref[pl.ds(0, middle)] = kc_ref[...]
    k_ref[pl.ds(middle, kr_ref.shape[0])] = kr_ref[...]
    v_ref[pl.ds(0, middle)] = vc_ref[...]
    v_ref[pl.ds(middle, vr_ref.shape[0])] = vr_ref[...]
    cells, channels = q_ref.shape
    positions = k_ref.shape[0]
    rows, cols = lat_ref.shape[0], lat_ref.shape[1]
    wide = cols + 2 * RADIUS
    span = 2 * RADIUS + 1
    head_size = channels // HEADS
    group = 128
    cell = lax.broadcasted_iota(jnp.int32, (cells, positions), 0)
    place = lax.broadcasted_iota(jnp.int32, (cells, positions), 1)
    rim_rows = RADIUS * wide
    rows_total = lat_ref.shape[0] + 2 * RADIUS
    key_row = jnp.where(
        place < middle,
        place // wide + RADIUS,
        jnp.where(
            place < middle + rim_rows,
            (place - middle) // wide,
            (place - middle - rim_rows) // wide + rows_total - RADIUS,
        ),
    )
    key_row = jnp.where(place < middle + 2 * rim_rows, key_row, rows_total + span)
    key_col = jnp.where(place < middle, place % wide, (place - middle) % wide)
    row_gap = key_row - cell // cols
    col_gap = key_col - cell % cols
    valid = (row_gap >= 0) & (row_gap < span) & (col_gap >= 0) & (col_gap < span)
    lane = lax.broadcasted_iota(jnp.int32, (cells, group), 1) // head_size
    for g in range(channels // group):
        lanes = slice(g * group, (g + 1) * group)
        q_g = q_ref[:, lanes]
        k_g = k_ref[:, lanes]
        v_g = v_ref[:, lanes]
        acc = jnp.zeros((cells, group), jnp.float32)
        for part in range(group // head_size):
            q_h = jnp.where(lane == part, q_g, jnp.zeros_like(q_g))
            s = lax.dot_general(
                q_h, k_g, (((1,), (1,)), ((), ())), preferred_element_type=jnp.float32
            )
            s = jnp.where(valid, s, -jnp.inf)
            top = jnp.max(s, axis=1, keepdims=True)
            e = jnp.exp(s - top)
            total = jnp.sum(e, axis=1, keepdims=True)
            w = (e / total).astype(jnp.bfloat16)
            o = jnp.dot(w, v_g, preferred_element_type=jnp.float32)
            acc = jnp.where(lane == part, o, acc)
        att_ref[:, lanes] = acc.astype(jnp.bfloat16)
    mixed = jnp.dot(att_ref[...], wo_ref[...], preferred_element_type=jnp.float32)
    lat = lat_ref[...].reshape(cells, channels)
    out_ref[...] = (lat.astype(jnp.float32) + mixed).astype(out_ref.dtype)


def attend_and_mix(query, center, rims, w_key, w_value, own_tile, w_output):
    rows, cols, channels = own_tile.shape
    cells = rows * cols
    center_flat = center.reshape(-1, channels)
    rim_flat = rims.reshape(-1, channels)
    count = center_flat.shape[0] + rim_flat.shape[0]
    positions = -(-count // 128) * 128
    rim_flat = jnp.pad(rim_flat, ((0, positions - count), (0, 0)))
    vmem = pl.BlockSpec(memory_space=pltpu.VMEM)
    out = pl.pallas_call(
        attention_kernel,
        out_shape=jax.ShapeDtypeStruct((cells, channels), own_tile.dtype),
        in_specs=[vmem] * 7,
        out_specs=vmem,
        scratch_shapes=[
            pltpu.VMEM((cells, channels), jnp.bfloat16),
            pltpu.VMEM((positions, channels), jnp.bfloat16),
            pltpu.VMEM((positions, channels), jnp.bfloat16),
        ],
    )(
        query.reshape(cells, channels) * jnp.asarray((channels // HEADS) ** (-0.5), query.dtype),
        project(center_flat, w_key),
        project(rim_flat, w_key),
        project(center_flat, w_value),
        project(rim_flat, w_value),
        own_tile,
        w_output,
    )
    return out.reshape(rows, cols, channels)


def widen_tiles(field, margin):
    west = jnp.roll(field, 1, axis=0)[:, :, -margin:]
    east = jnp.roll(field, -1, axis=0)[:, :, :margin]
    return jnp.concatenate([west, field, east], axis=2)


def pick_all(table, edges):
    number = edges.shape[0]
    tile_hit = jnp.arange(number, dtype=jnp.int32) == table[..., 0:1]
    edge_hit = jnp.arange(2, dtype=jnp.int32) == table[..., 1:2]
    chosen = (tile_hit[..., :, None] & edge_hit[..., None, :]).astype(edges.dtype)
    got = jnp.einsum("...nf,nfrwc->...rwc", chosen, edges, preferred_element_type=jnp.float32)
    return got.astype(edges.dtype)


def doubling_gather(block, axis, radix=4):
    count = lax.axis_size(axis)
    if count & (count - 1):
        return lax.all_gather(block, axis, axis=0, tiled=True)
    me = lax.axis_index(axis)
    levels = []
    stride = 1
    while stride < count:
        r = min(radix, count // stride)
        levels.append((stride, r))
        stride *= r
    held = block
    for stride, r in reversed(levels):
        got = [held]
        for d in range(1, r):
            got.append(lax.ppermute(held, axis, [(i, i ^ (d * stride)) for i in range(count)]))
        digit = (me // stride) % r
        held = jnp.take(jnp.stack(got), digit ^ jnp.arange(r, dtype=jnp.int32), axis=0)
    depth = len(levels)
    held = jnp.transpose(held, tuple(reversed(range(depth))) + tuple(range(depth, held.ndim)))
    return held.reshape((count * block.shape[0],) + block.shape[1:])


def local(latents, norm_gain, metric, w_query, w_key, w_value, w_output, seam_table):
    own_tile = latents[0]
    channels = own_tile.shape[-1]
    normed = normalize(own_tile, norm_gain)
    margin = 1
    seam_rows = seam_table[0]
    widened = padded_2(normed[None], (("blk", 2),), margin)
    rows1 = jnp.stack([normed[0], normed[-1]])
    got1 = widen_tiles(doubling_gather(rows1[None], "blk"), 1)
    received = pick_all(seam_rows, got1[:, :, None])
    padded = place_rims(widened[0], received, seam_rows)
    smoothed = smooth(padded, metric[0])
    query = project(smoothed, w_query)
    field_wide = padded_2(smoothed[None], (("blk", 2),), RADIUS)
    rows3 = jnp.concatenate([smoothed[:RADIUS], smoothed[-RADIUS:]], axis=0)
    got3 = widen_tiles(doubling_gather(rows3[None], "blk"), RADIUS)
    edges3 = jnp.stack([got3[:, :RADIUS], got3[:, RADIUS:]], axis=1)
    field_got = pick_all(seam_rows, edges3)
    arrived = orient_rims(field_got, seam_rows)
    return attend_and_mix(query, field_wide[0], arrived, w_key, w_value, own_tile, w_output)[None]


def solution(mesh):
    return jax.shard_map(
        local,
        mesh=mesh,
        in_specs=(
            P(("group", "blk"), None, None, None),
            P(),
            P("blk", None, None, None),
            P(),
            P(),
            P(),
            P(),
            P("blk", None, None),
        ),
        out_specs=P(("group", "blk"), None, None, None),
        check_vma=False,
    )
```

```python
import jax
import jax.numpy as jnp
from jax import lax
from jax.sharding import PartitionSpec as P
from jax.experimental import pallas as pl
from jax.experimental.pallas import tpu as pltpu

HEADS = 8
RADIUS = 3


def padded_2(array, sides, width):
    for axis, dim in sides:
        count, length = (lax.axis_size(axis), array.shape[dim])
        up = [(i, (i + 1) % count) for i in range(count)]
        down = [(j, i) for i, j in up]
        last = lax.slice_in_dim(array, length - width, length, axis=dim)
        first = lax.slice_in_dim(array, 0, width, axis=dim)
        before = lax.ppermute(last, axis, up)
        after = lax.ppermute(first, axis, down)
        array = jnp.concatenate([before, array, after], axis=dim)
    return array


def normalize(latents, norm_gain):
    values = latents.astype(jnp.float32)
    factor = lax.rsqrt(jnp.mean(values * values, axis=-1, keepdims=True) + 1e-05)
    return (values * factor * norm_gain).astype(jnp.bfloat16)


def pick_rims(seam_rows, piece):
    number = piece.shape[0]
    tile_ids = jnp.arange(number, dtype=jnp.int32)
    tile_hit = tile_ids[None, :] == seam_rows[:, 0:1]
    edge_hit = jnp.arange(2, dtype=jnp.int32)[None, :] == seam_rows[:, 1:2]
    chosen = (tile_hit[:, :, None] & edge_hit[:, None, :]).astype(piece.dtype)
    return jnp.einsum("enf,nfrwc->erwc", chosen, piece, preferred_element_type=jnp.float32)


def edge_rows(widened, margin):
    return jnp.stack([widened[:, :margin], widened[:, -margin:]], axis=1)


def orient_rims(received, seam_pair):
    arrived = received.astype(jnp.bfloat16)
    orient = seam_pair[:, 2]
    flip_along = (orient % 2 == 1)[:, None, None, None]
    arrived = jnp.where(flip_along, arrived[:, :, ::-1], arrived)
    flip_across = (orient // 2 == 1)[:, None, None, None]
    return jnp.where(flip_across, arrived[:, ::-1], arrived)


def place_rims(widened, received, seam_pair):
    arrived = orient_rims(received, seam_pair)
    return jnp.concatenate([arrived[0], widened, arrived[1]], axis=0)


def smooth(padded, metric):
    rows, cols = (metric.shape[-2], metric.shape[-1])
    total = jnp.zeros((rows, cols, padded.shape[-1]), jnp.float32)
    for stencil in range(9):
        row_off = stencil // 3
        col_off = stencil % 3
        total = (
            total
            + metric[stencil, :, :, None]
            * padded[row_off : row_off + rows, col_off : col_off + cols, :]
        )
    return total.astype(jnp.bfloat16)


def project(values, weight):
    shape = values.shape
    flat = values.reshape(-1, shape[-1])
    return (
        jnp.dot(flat, weight, preferred_element_type=jnp.float32)
        .astype(jnp.bfloat16)
        .reshape(shape[:-1] + (weight.shape[1],))
    )


def attention_kernel(
    q_ref, kc_ref, kr_ref, vc_ref, vr_ref, lat_ref, wo_ref, out_ref, att_ref, k_ref, v_ref
):
    middle = kc_ref.shape[0]
    k_ref[pl.ds(0, middle)] = kc_ref[...]
    k_ref[pl.ds(middle, kr_ref.shape[0])] = kr_ref[...]
    v_ref[pl.ds(0, middle)] = vc_ref[...]
    v_ref[pl.ds(middle, vr_ref.shape[0])] = vr_ref[...]
    cells, channels = q_ref.shape
    positions = k_ref.shape[0]
    rows, cols = lat_ref.shape[0], lat_ref.shape[1]
    wide = cols + 2 * RADIUS
    span = 2 * RADIUS + 1
    head_size = channels // HEADS
    group = 128
    cell = lax.broadcasted_iota(jnp.int32, (cells, positions), 0)
    place = lax.broadcasted_iota(jnp.int32, (cells, positions), 1)
    rim_rows = RADIUS * wide
    rows_total = lat_ref.shape[0] + 2 * RADIUS
    key_row = jnp.where(
        place < middle,
        place // wide + RADIUS,
        jnp.where(
            place < middle + rim_rows,
            (place - middle) // wide,
            (place - middle - rim_rows) // wide + rows_total - RADIUS,
        ),
    )
    key_row = jnp.where(place < middle + 2 * rim_rows, key_row, rows_total + span)
    key_col = jnp.where(place < middle, place % wide, (place - middle) % wide)
    row_gap = key_row - cell // cols
    col_gap = key_col - cell % cols
    valid = (row_gap >= 0) & (row_gap < span) & (col_gap >= 0) & (col_gap < span)
    lane = lax.broadcasted_iota(jnp.int32, (cells, group), 1) // head_size
    for g in range(channels // group):
        lanes = slice(g * group, (g + 1) * group)
        q_g = q_ref[:, lanes]
        k_g = k_ref[:, lanes]
        v_g = v_ref[:, lanes]
        acc = jnp.zeros((cells, group), jnp.float32)
        for part in range(group // head_size):
            q_h = jnp.where(lane == part, q_g, jnp.zeros_like(q_g))
            s = lax.dot_general(
                q_h, k_g, (((1,), (1,)), ((), ())), preferred_element_type=jnp.float32
            )
            s = jnp.where(valid, s, -jnp.inf)
            top = jnp.max(s, axis=1, keepdims=True)
            e = jnp.exp(s - top)
            total = jnp.sum(e, axis=1, keepdims=True)
            w = (e / total).astype(jnp.bfloat16)
            o = jnp.dot(w, v_g, preferred_element_type=jnp.float32)
            acc = jnp.where(lane == part, o, acc)
        att_ref[:, lanes] = acc.astype(jnp.bfloat16)
    mixed = jnp.dot(att_ref[...], wo_ref[...], preferred_element_type=jnp.float32)
    lat = lat_ref[...].reshape(cells, channels)
    out_ref[...] = (lat.astype(jnp.float32) + mixed).astype(out_ref.dtype)


def attend_and_mix(query, center, rims, w_key, w_value, own_tile, w_output):
    rows, cols, channels = own_tile.shape
    cells = rows * cols
    center_flat = center.reshape(-1, channels)
    rim_flat = rims.reshape(-1, channels)
    count = center_flat.shape[0] + rim_flat.shape[0]
    positions = -(-count // 128) * 128
    rim_flat = jnp.pad(rim_flat, ((0, positions - count), (0, 0)))
    vmem = pl.BlockSpec(memory_space=pltpu.VMEM)
    out = pl.pallas_call(
        attention_kernel,
        out_shape=jax.ShapeDtypeStruct((cells, channels), own_tile.dtype),
        in_specs=[vmem] * 7,
        out_specs=vmem,
        scratch_shapes=[
            pltpu.VMEM((cells, channels), jnp.bfloat16),
            pltpu.VMEM((positions, channels), jnp.bfloat16),
            pltpu.VMEM((positions, channels), jnp.bfloat16),
        ],
    )(
        query.reshape(cells, channels) * jnp.asarray((channels // HEADS) ** (-0.5), query.dtype),
        project(center_flat, w_key),
        project(rim_flat, w_key),
        project(center_flat, w_value),
        project(rim_flat, w_value),
        own_tile,
        w_output,
    )
    return out.reshape(rows, cols, channels)


def widen_tiles(field, margin):
    west = jnp.roll(field, 1, axis=0)[:, :, -margin:]
    east = jnp.roll(field, -1, axis=0)[:, :, :margin]
    return jnp.concatenate([west, field, east], axis=2)


def pick_all(table, edges):
    number = edges.shape[0]
    tile_hit = jnp.arange(number, dtype=jnp.int32) == table[..., 0:1]
    edge_hit = jnp.arange(2, dtype=jnp.int32) == table[..., 1:2]
    chosen = (tile_hit[..., :, None] & edge_hit[..., None, :]).astype(edges.dtype)
    got = jnp.einsum("...nf,nfrwc->...rwc", chosen, edges, preferred_element_type=jnp.float32)
    return got.astype(edges.dtype)


def doubling_gather(block, axis, radix=4):
    count = lax.axis_size(axis)
    if count & (count - 1):
        return lax.all_gather(block, axis, axis=0, tiled=True)
    me = lax.axis_index(axis)
    levels = []
    stride = 1
    while stride < count:
        r = min(radix, count // stride)
        levels.append((stride, r))
        stride *= r
    held = block
    for stride, r in reversed(levels):
        got = [held]
        for d in range(1, r):
            got.append(lax.ppermute(held, axis, [(i, i ^ (d * stride)) for i in range(count)]))
        digit = (me // stride) % r
        held = jnp.take(jnp.stack(got), digit ^ jnp.arange(r, dtype=jnp.int32), axis=0)
    depth = len(levels)
    held = jnp.transpose(held, tuple(reversed(range(depth))) + tuple(range(depth, held.ndim)))
    return held.reshape((count * block.shape[0],) + block.shape[1:])


def local(latents, norm_gain, metric, w_query, w_key, w_value, w_output, seam_table):
    own_tile = latents[0]
    channels = own_tile.shape[-1]
    normed = normalize(own_tile, norm_gain)
    margin = 1
    seam_rows = seam_table[0]
    widened = padded_2(normed[None], (("blk", 2),), margin)
    rows1 = jnp.stack([normed[0], normed[-1]])
    got1 = widen_tiles(doubling_gather(rows1[None], "blk"), 1)
    received = pick_all(seam_rows, got1[:, :, None])
    padded = place_rims(widened[0], received, seam_rows)
    smoothed = smooth(padded, metric[0])
    query = project(smoothed, w_query)
    field_wide = padded_2(smoothed[None], (("blk", 2),), RADIUS)
    rows3 = jnp.concatenate([smoothed[:RADIUS], smoothed[-RADIUS:]], axis=0)
    got3 = doubling_gather(rows3[None], "blk")
    count = got3.shape[0]
    edges3 = got3.reshape((count, 2, RADIUS) + got3.shape[2:])
    near = jnp.stack(
        [seam_rows.at[:, 0].set((seam_rows[:, 0] + count + k) % count) for k in (-1, 0, 1)], axis=1
    )
    picked = pick_all(near, edges3)
    field_got = jnp.concatenate(
        [picked[:, 0, :, -RADIUS:], picked[:, 1], picked[:, 2, :, :RADIUS]], axis=2
    )
    arrived = orient_rims(field_got, seam_rows)
    return attend_and_mix(query, field_wide[0], arrived, w_key, w_value, own_tile, w_output)[None]


def solution(mesh):
    return jax.shard_map(
        local,
        mesh=mesh,
        in_specs=(
            P(("group", "blk"), None, None, None),
            P(),
            P("blk", None, None, None),
            P(),
            P(),
            P(),
            P(),
            P("blk", None, None),
        ),
        out_specs=P(("group", "blk"), None, None, None),
        check_vma=False,
    )
```

```python
import jax
import jax.numpy as jnp
from jax import lax
from jax.sharding import PartitionSpec as P
from jax.experimental import pallas as pl
from jax.experimental.pallas import tpu as pltpu

HEADS = 8
RADIUS = 3


def padded_2(array, sides, width):
    for axis, dim in sides:
        count, length = (lax.axis_size(axis), array.shape[dim])
        up = [(i, (i + 1) % count) for i in range(count)]
        down = [(j, i) for i, j in up]
        last = lax.slice_in_dim(array, length - width, length, axis=dim)
        first = lax.slice_in_dim(array, 0, width, axis=dim)
        before = lax.ppermute(last, axis, up)
        after = lax.ppermute(first, axis, down)
        array = jnp.concatenate([before, array, after], axis=dim)
    return array


def normalize(latents, norm_gain):
    values = latents.astype(jnp.float32)
    factor = lax.rsqrt(jnp.mean(values * values, axis=-1, keepdims=True) + 1e-05)
    return (values * factor * norm_gain).astype(jnp.bfloat16)


def pick_rims(seam_rows, piece):
    number = piece.shape[0]
    tile_ids = jnp.arange(number, dtype=jnp.int32)
    tile_hit = tile_ids[None, :] == seam_rows[:, 0:1]
    edge_hit = jnp.arange(2, dtype=jnp.int32)[None, :] == seam_rows[:, 1:2]
    chosen = (tile_hit[:, :, None] & edge_hit[:, None, :]).astype(piece.dtype)
    return jnp.einsum("enf,nfrwc->erwc", chosen, piece, preferred_element_type=jnp.float32)


def edge_rows(widened, margin):
    return jnp.stack([widened[:, :margin], widened[:, -margin:]], axis=1)


def orient_rims(received, seam_pair):
    arrived = received.astype(jnp.bfloat16)
    orient = seam_pair[:, 2]
    flip_along = (orient % 2 == 1)[:, None, None, None]
    arrived = jnp.where(flip_along, arrived[:, :, ::-1], arrived)
    flip_across = (orient // 2 == 1)[:, None, None, None]
    return jnp.where(flip_across, arrived[:, ::-1], arrived)


def place_rims(widened, received, seam_pair):
    arrived = orient_rims(received, seam_pair)
    return jnp.concatenate([arrived[0], widened, arrived[1]], axis=0)


def smooth(padded, metric):
    rows, cols = (metric.shape[-2], metric.shape[-1])
    total = jnp.zeros((rows, cols, padded.shape[-1]), jnp.float32)
    for stencil in range(9):
        row_off = stencil // 3
        col_off = stencil % 3
        total = (
            total
            + metric[stencil, :, :, None]
            * padded[row_off : row_off + rows, col_off : col_off + cols, :]
        )
    return total.astype(jnp.bfloat16)


def project(values, weight):
    shape = values.shape
    flat = values.reshape(-1, shape[-1])
    return (
        jnp.dot(flat, weight, preferred_element_type=jnp.float32)
        .astype(jnp.bfloat16)
        .reshape(shape[:-1] + (weight.shape[1],))
    )


def attention_kernel(
    q_ref, kc_ref, kr_ref, vc_ref, vr_ref, lat_ref, wo_ref, out_ref, att_ref, k_ref, v_ref
):
    middle = kc_ref.shape[0]
    k_ref[pl.ds(0, middle)] = kc_ref[...]
    k_ref[pl.ds(middle, kr_ref.shape[0])] = kr_ref[...]
    v_ref[pl.ds(0, middle)] = vc_ref[...]
    v_ref[pl.ds(middle, vr_ref.shape[0])] = vr_ref[...]
    cells, channels = q_ref.shape
    positions = k_ref.shape[0]
    rows, cols = lat_ref.shape[0], lat_ref.shape[1]
    wide = cols + 2 * RADIUS
    span = 2 * RADIUS + 1
    head_size = channels // HEADS
    group = 128
    cell = lax.broadcasted_iota(jnp.int32, (cells, positions), 0)
    place = lax.broadcasted_iota(jnp.int32, (cells, positions), 1)
    rim_rows = RADIUS * wide
    rows_total = lat_ref.shape[0] + 2 * RADIUS
    key_row = jnp.where(
        place < middle,
        place // wide + RADIUS,
        jnp.where(
            place < middle + rim_rows,
            (place - middle) // wide,
            (place - middle - rim_rows) // wide + rows_total - RADIUS,
        ),
    )
    key_row = jnp.where(place < middle + 2 * rim_rows, key_row, rows_total + span)
    key_col = jnp.where(place < middle, place % wide, (place - middle) % wide)
    row_gap = key_row - cell // cols
    col_gap = key_col - cell % cols
    valid = (row_gap >= 0) & (row_gap < span) & (col_gap >= 0) & (col_gap < span)
    lane = lax.broadcasted_iota(jnp.int32, (cells, group), 1) // head_size
    for g in range(channels // group):
        lanes = slice(g * group, (g + 1) * group)
        q_g = q_ref[:, lanes]
        k_g = k_ref[:, lanes]
        v_g = v_ref[:, lanes]
        acc = jnp.zeros((cells, group), jnp.float32)
        for part in range(group // head_size):
            q_h = jnp.where(lane == part, q_g, jnp.zeros_like(q_g))
            s = lax.dot_general(
                q_h, k_g, (((1,), (1,)), ((), ())), preferred_element_type=jnp.float32
            )
            s = jnp.where(valid, s, -jnp.inf)
            top = jnp.max(s, axis=1, keepdims=True)
            e = jnp.exp(s - top)
            total = jnp.sum(e, axis=1, keepdims=True)
            w = (e / total).astype(jnp.bfloat16)
            o = jnp.dot(w, v_g, preferred_element_type=jnp.float32)
            acc = jnp.where(lane == part, o, acc)
        att_ref[:, lanes] = acc.astype(jnp.bfloat16)
    mixed = jnp.dot(att_ref[...], wo_ref[...], preferred_element_type=jnp.float32)
    lat = lat_ref[...].reshape(cells, channels)
    out_ref[...] = (lat.astype(jnp.float32) + mixed).astype(out_ref.dtype)


def attend_and_mix(query, center, rims, w_key, w_value, own_tile, w_output):
    rows, cols, channels = own_tile.shape
    cells = rows * cols
    center_flat = center.reshape(-1, channels)
    rim_flat = rims.reshape(-1, channels)
    count = center_flat.shape[0] + rim_flat.shape[0]
    positions = -(-count // 128) * 128
    rim_flat = jnp.pad(rim_flat, ((0, positions - count), (0, 0)))
    vmem = pl.BlockSpec(memory_space=pltpu.VMEM)
    out = pl.pallas_call(
        attention_kernel,
        out_shape=jax.ShapeDtypeStruct((cells, channels), own_tile.dtype),
        in_specs=[vmem] * 7,
        out_specs=vmem,
        scratch_shapes=[
            pltpu.VMEM((cells, channels), jnp.bfloat16),
            pltpu.VMEM((positions, channels), jnp.bfloat16),
            pltpu.VMEM((positions, channels), jnp.bfloat16),
        ],
    )(
        query.reshape(cells, channels) * jnp.asarray((channels // HEADS) ** (-0.5), query.dtype),
        project(center_flat, w_key),
        project(rim_flat, w_key),
        project(center_flat, w_value),
        project(rim_flat, w_value),
        own_tile,
        w_output,
    )
    return out.reshape(rows, cols, channels)


def widen_tiles(field, margin):
    west = jnp.roll(field, 1, axis=0)[:, :, -margin:]
    east = jnp.roll(field, -1, axis=0)[:, :, :margin]
    return jnp.concatenate([west, field, east], axis=2)


def pick_all(table, edges):
    number = edges.shape[0]
    tile_hit = jnp.arange(number, dtype=jnp.int32) == table[..., 0:1]
    edge_hit = jnp.arange(2, dtype=jnp.int32) == table[..., 1:2]
    chosen = (tile_hit[..., :, None] & edge_hit[..., None, :]).astype(edges.dtype)
    got = jnp.einsum("...nf,nfrwc->...rwc", chosen, edges, preferred_element_type=jnp.float32)
    return got.astype(edges.dtype)


def doubling_gather(block, axis, radix=4):
    count = lax.axis_size(axis)
    if count & (count - 1):
        return lax.all_gather(block, axis, axis=0, tiled=True)
    me = lax.axis_index(axis)
    levels = []
    stride = 1
    while stride < count:
        r = min(radix, count // stride)
        levels.append((stride, r))
        stride *= r
    held = block
    for stride, r in reversed(levels):
        got = [held]
        for d in range(1, r):
            got.append(lax.ppermute(held, axis, [(i, i ^ (d * stride)) for i in range(count)]))
        digit = (me // stride) % r
        held = jnp.take(jnp.stack(got), digit ^ jnp.arange(r, dtype=jnp.int32), axis=0)
    depth = len(levels)
    held = jnp.transpose(held, tuple(reversed(range(depth))) + tuple(range(depth, held.ndim)))
    return held.reshape((count * block.shape[0],) + block.shape[1:])


def local(latents, norm_gain, metric, w_query, w_key, w_value, w_output, seam_table):
    own_tile = latents[0]
    channels = own_tile.shape[-1]
    normed = normalize(own_tile, norm_gain)
    margin = 1
    seam_rows = seam_table[0]
    widened = padded_2(normed[None], (("blk", 2),), margin)
    rows1 = jnp.stack([normed[0], normed[-1]])
    got1 = doubling_gather(rows1[None], "blk")
    count = got1.shape[0]
    near1 = jnp.stack(
        [seam_rows.at[:, 0].set((seam_rows[:, 0] + count + k) % count) for k in (-1, 0, 1)], axis=1
    )
    picked1 = pick_all(near1, got1[:, :, None])
    received = jnp.concatenate(
        [picked1[:, 0, :, -1:], picked1[:, 1], picked1[:, 2, :, :1]], axis=2
    )
    padded = place_rims(widened[0], received, seam_rows)
    smoothed = smooth(padded, metric[0])
    query = project(smoothed, w_query)
    field_wide = padded_2(smoothed[None], (("blk", 2),), RADIUS)
    rows3 = jnp.concatenate([smoothed[:RADIUS], smoothed[-RADIUS:]], axis=0)
    got3 = doubling_gather(rows3[None], "blk")
    count = got3.shape[0]
    edges3 = got3.reshape((count, 2, RADIUS) + got3.shape[2:])
    near = jnp.stack(
        [seam_rows.at[:, 0].set((seam_rows[:, 0] + count + k) % count) for k in (-1, 0, 1)], axis=1
    )
    picked = pick_all(near, edges3)
    field_got = jnp.concatenate(
        [picked[:, 0, :, -RADIUS:], picked[:, 1], picked[:, 2, :, :RADIUS]], axis=2
    )
    arrived = orient_rims(field_got, seam_rows)
    return attend_and_mix(query, field_wide[0], arrived, w_key, w_value, own_tile, w_output)[None]


def solution(mesh):
    return jax.shard_map(
        local,
        mesh=mesh,
        in_specs=(
            P(("group", "blk"), None, None, None),
            P(),
            P("blk", None, None, None),
            P(),
            P(),
            P(),
            P(),
            P("blk", None, None),
        ),
        out_specs=P(("group", "blk"), None, None, None),
        check_vma=False,
    )
```

```python
import jax
import jax.numpy as jnp
from jax import lax
from jax.sharding import PartitionSpec as P
from jax.experimental import pallas as pl
from jax.experimental.pallas import tpu as pltpu

HEADS = 8
RADIUS = 3


def padded_2(array, sides, width):
    for axis, dim in sides:
        count, length = (lax.axis_size(axis), array.shape[dim])
        up = [(i, (i + 1) % count) for i in range(count)]
        down = [(j, i) for i, j in up]
        last = lax.slice_in_dim(array, length - width, length, axis=dim)
        first = lax.slice_in_dim(array, 0, width, axis=dim)
        before = lax.ppermute(last, axis, up)
        after = lax.ppermute(first, axis, down)
        array = jnp.concatenate([before, array, after], axis=dim)
    return array


def normalize(latents, norm_gain):
    values = latents.astype(jnp.float32)
    factor = lax.rsqrt(jnp.mean(values * values, axis=-1, keepdims=True) + 1e-05)
    return (values * factor * norm_gain).astype(jnp.bfloat16)


def pick_rims(seam_rows, piece):
    number = piece.shape[0]
    tile_ids = jnp.arange(number, dtype=jnp.int32)
    tile_hit = tile_ids[None, :] == seam_rows[:, 0:1]
    edge_hit = jnp.arange(2, dtype=jnp.int32)[None, :] == seam_rows[:, 1:2]
    chosen = (tile_hit[:, :, None] & edge_hit[:, None, :]).astype(piece.dtype)
    return jnp.einsum("enf,nfrwc->erwc", chosen, piece, preferred_element_type=jnp.float32)


def edge_rows(widened, margin):
    return jnp.stack([widened[:, :margin], widened[:, -margin:]], axis=1)


def orient_rims(received, seam_pair):
    arrived = received.astype(jnp.bfloat16)
    orient = seam_pair[:, 2]
    flip_along = (orient % 2 == 1)[:, None, None, None]
    arrived = jnp.where(flip_along, arrived[:, :, ::-1], arrived)
    flip_across = (orient // 2 == 1)[:, None, None, None]
    return jnp.where(flip_across, arrived[:, ::-1], arrived)


def place_rims(widened, received, seam_pair):
    arrived = orient_rims(received, seam_pair)
    return jnp.concatenate([arrived[0], widened, arrived[1]], axis=0)


def smooth(padded, metric):
    rows, cols = (metric.shape[-2], metric.shape[-1])
    total = jnp.zeros((rows, cols, padded.shape[-1]), jnp.float32)
    for stencil in range(9):
        row_off = stencil // 3
        col_off = stencil % 3
        total = (
            total
            + metric[stencil, :, :, None]
            * padded[row_off : row_off + rows, col_off : col_off + cols, :]
        )
    return total.astype(jnp.bfloat16)


def project(values, weight):
    shape = values.shape
    flat = values.reshape(-1, shape[-1])
    return (
        jnp.dot(flat, weight, preferred_element_type=jnp.float32)
        .astype(jnp.bfloat16)
        .reshape(shape[:-1] + (weight.shape[1],))
    )


def attention_kernel(
    q_ref, kc_ref, kr_ref, vc_ref, vr_ref, lat_ref, wo_ref, out_ref, att_ref, k_ref, v_ref
):
    middle = kc_ref.shape[0]
    k_ref[pl.ds(0, middle)] = kc_ref[...]
    k_ref[pl.ds(middle, kr_ref.shape[0])] = kr_ref[...]
    v_ref[pl.ds(0, middle)] = vc_ref[...]
    v_ref[pl.ds(middle, vr_ref.shape[0])] = vr_ref[...]
    cells, channels = q_ref.shape
    positions = k_ref.shape[0]
    rows, cols = lat_ref.shape[0], lat_ref.shape[1]
    wide = cols + 2 * RADIUS
    span = 2 * RADIUS + 1
    head_size = channels // HEADS
    group = 128
    cell = lax.broadcasted_iota(jnp.int32, (cells, positions), 0)
    place = lax.broadcasted_iota(jnp.int32, (cells, positions), 1)
    rim_rows = RADIUS * wide
    rows_total = lat_ref.shape[0] + 2 * RADIUS
    key_row = jnp.where(
        place < middle,
        place // wide + RADIUS,
        jnp.where(
            place < middle + rim_rows,
            (place - middle) // wide,
            (place - middle - rim_rows) // wide + rows_total - RADIUS,
        ),
    )
    key_row = jnp.where(place < middle + 2 * rim_rows, key_row, rows_total + span)
    key_col = jnp.where(place < middle, place % wide, (place - middle) % wide)
    row_gap = key_row - cell // cols
    col_gap = key_col - cell % cols
    valid = (row_gap >= 0) & (row_gap < span) & (col_gap >= 0) & (col_gap < span)
    lane = lax.broadcasted_iota(jnp.int32, (cells, group), 1) // head_size
    for g in range(channels // group):
        lanes = slice(g * group, (g + 1) * group)
        q_g = q_ref[:, lanes]
        k_g = k_ref[:, lanes]
        v_g = v_ref[:, lanes]
        acc = jnp.zeros((cells, group), jnp.float32)
        for part in range(group // head_size):
            q_h = jnp.where(lane == part, q_g, jnp.zeros_like(q_g))
            s = lax.dot_general(
                q_h, k_g, (((1,), (1,)), ((), ())), preferred_element_type=jnp.float32
            )
            s = jnp.where(valid, s, -jnp.inf)
            top = jnp.max(s, axis=1, keepdims=True)
            e = jnp.exp(s - top)
            total = jnp.sum(e, axis=1, keepdims=True)
            w = (e / total).astype(jnp.bfloat16)
            o = jnp.dot(w, v_g, preferred_element_type=jnp.float32)
            acc = jnp.where(lane == part, o, acc)
        att_ref[:, lanes] = acc.astype(jnp.bfloat16)
    mixed = jnp.dot(att_ref[...], wo_ref[...], preferred_element_type=jnp.float32)
    lat = lat_ref[...].reshape(cells, channels)
    out_ref[...] = (lat.astype(jnp.float32) + mixed).astype(out_ref.dtype)


def attend_and_mix(query, center, rims, w_key, w_value, own_tile, w_output):
    rows, cols, channels = own_tile.shape
    cells = rows * cols
    center_flat = center.reshape(-1, channels)
    rim_flat = rims.reshape(-1, channels)
    count = center_flat.shape[0] + rim_flat.shape[0]
    positions = -(-count // 128) * 128
    rim_flat = jnp.pad(rim_flat, ((0, positions - count), (0, 0)))
    vmem = pl.BlockSpec(memory_space=pltpu.VMEM)
    out = pl.pallas_call(
        attention_kernel,
        out_shape=jax.ShapeDtypeStruct((cells, channels), own_tile.dtype),
        in_specs=[vmem] * 7,
        out_specs=vmem,
        scratch_shapes=[
            pltpu.VMEM((cells, channels), jnp.bfloat16),
            pltpu.VMEM((positions, channels), jnp.bfloat16),
            pltpu.VMEM((positions, channels), jnp.bfloat16),
        ],
    )(
        query.reshape(cells, channels) * jnp.asarray((channels // HEADS) ** (-0.5), query.dtype),
        project(center_flat, w_key),
        project(rim_flat, w_key),
        project(center_flat, w_value),
        project(rim_flat, w_value),
        own_tile,
        w_output,
    )
    return out.reshape(rows, cols, channels)


def widen_tiles(field, margin):
    west = jnp.roll(field, 1, axis=0)[:, :, -margin:]
    east = jnp.roll(field, -1, axis=0)[:, :, :margin]
    return jnp.concatenate([west, field, east], axis=2)


def pick_all(table, edges):
    number = edges.shape[0]
    tile_hit = jnp.arange(number, dtype=jnp.int32) == table[..., 0:1]
    edge_hit = jnp.arange(2, dtype=jnp.int32) == table[..., 1:2]
    chosen = (tile_hit[..., :, None] & edge_hit[..., None, :]).astype(edges.dtype)
    got = jnp.einsum("...nf,nfrwc->...rwc", chosen, edges, preferred_element_type=jnp.float32)
    return got.astype(edges.dtype)


def doubling_gather(block, axis, radix=4):
    count = lax.axis_size(axis)
    if count & (count - 1):
        return lax.all_gather(block, axis, axis=0, tiled=True)
    me = lax.axis_index(axis)
    levels = []
    stride = 1
    while stride < count:
        r = min(radix, count // stride)
        levels.append((stride, r))
        stride *= r
    held = block
    for stride, r in reversed(levels):
        got = [held]
        for d in range(1, r):
            got.append(lax.ppermute(held, axis, [(i, i ^ (d * stride)) for i in range(count)]))
        digit = (me // stride) % r
        held = jnp.take(jnp.stack(got), digit ^ jnp.arange(r, dtype=jnp.int32), axis=0)
    depth = len(levels)
    held = jnp.transpose(held, tuple(reversed(range(depth))) + tuple(range(depth, held.ndim)))
    return held.reshape((count * block.shape[0],) + block.shape[1:])


def local(latents, norm_gain, metric, w_query, w_key, w_value, w_output, seam_table):
    own_tile = latents[0]
    channels = own_tile.shape[-1]
    normed = normalize(own_tile, norm_gain)
    margin = 1
    seam_rows = seam_table[0]
    widened = padded_2(normed[None], (("blk", 2),), margin)
    rows1 = jnp.stack([normed[0], normed[-1]])
    got1 = doubling_gather(rows1[None], "blk", radix=2)
    count = got1.shape[0]
    near1 = jnp.stack(
        [seam_rows.at[:, 0].set((seam_rows[:, 0] + count + k) % count) for k in (-1, 0, 1)], axis=1
    )
    picked1 = pick_all(near1, got1[:, :, None])
    received = jnp.concatenate(
        [picked1[:, 0, :, -1:], picked1[:, 1], picked1[:, 2, :, :1]], axis=2
    )
    padded = place_rims(widened[0], received, seam_rows)
    smoothed = smooth(padded, metric[0])
    query = project(smoothed, w_query)
    field_wide = padded_2(smoothed[None], (("blk", 2),), RADIUS)
    rows3 = jnp.concatenate([smoothed[:RADIUS], smoothed[-RADIUS:]], axis=0)
    got3 = doubling_gather(rows3[None], "blk")
    count = got3.shape[0]
    edges3 = got3.reshape((count, 2, RADIUS) + got3.shape[2:])
    near = jnp.stack(
        [seam_rows.at[:, 0].set((seam_rows[:, 0] + count + k) % count) for k in (-1, 0, 1)], axis=1
    )
    picked = pick_all(near, edges3)
    field_got = jnp.concatenate(
        [picked[:, 0, :, -RADIUS:], picked[:, 1], picked[:, 2, :, :RADIUS]], axis=2
    )
    arrived = orient_rims(field_got, seam_rows)
    return attend_and_mix(query, field_wide[0], arrived, w_key, w_value, own_tile, w_output)[None]


def solution(mesh):
    return jax.shard_map(
        local,
        mesh=mesh,
        in_specs=(
            P(("group", "blk"), None, None, None),
            P(),
            P("blk", None, None, None),
            P(),
            P(),
            P(),
            P(),
            P("blk", None, None),
        ),
        out_specs=P(("group", "blk"), None, None, None),
        check_vma=False,
    )
```

```python
import jax
import jax.numpy as jnp
from jax import lax
from jax.sharding import PartitionSpec as P
from jax.experimental import pallas as pl
from jax.experimental.pallas import tpu as pltpu

HEADS = 8
RADIUS = 3


def padded_2(array, sides, width):
    for axis, dim in sides:
        count, length = (lax.axis_size(axis), array.shape[dim])
        up = [(i, (i + 1) % count) for i in range(count)]
        down = [(j, i) for i, j in up]
        last = lax.slice_in_dim(array, length - width, length, axis=dim)
        first = lax.slice_in_dim(array, 0, width, axis=dim)
        before = lax.ppermute(last, axis, up)
        after = lax.ppermute(first, axis, down)
        array = jnp.concatenate([before, array, after], axis=dim)
    return array


def normalize(latents, norm_gain):
    values = latents.astype(jnp.float32)
    factor = lax.rsqrt(jnp.mean(values * values, axis=-1, keepdims=True) + 1e-05)
    return (values * factor * norm_gain).astype(jnp.bfloat16)


def pick_rims(seam_rows, piece):
    number = piece.shape[0]
    tile_ids = jnp.arange(number, dtype=jnp.int32)
    tile_hit = tile_ids[None, :] == seam_rows[:, 0:1]
    edge_hit = jnp.arange(2, dtype=jnp.int32)[None, :] == seam_rows[:, 1:2]
    chosen = (tile_hit[:, :, None] & edge_hit[:, None, :]).astype(piece.dtype)
    return jnp.einsum("enf,nfrwc->erwc", chosen, piece, preferred_element_type=jnp.float32)


def edge_rows(widened, margin):
    return jnp.stack([widened[:, :margin], widened[:, -margin:]], axis=1)


def orient_rims(received, seam_pair):
    arrived = received.astype(jnp.bfloat16)
    orient = seam_pair[:, 2]
    flip_along = (orient % 2 == 1)[:, None, None, None]
    arrived = jnp.where(flip_along, arrived[:, :, ::-1], arrived)
    flip_across = (orient // 2 == 1)[:, None, None, None]
    return jnp.where(flip_across, arrived[:, ::-1], arrived)


def place_rims(widened, received, seam_pair):
    arrived = orient_rims(received, seam_pair)
    return jnp.concatenate([arrived[0], widened, arrived[1]], axis=0)


def smooth(padded, metric):
    rows, cols = (metric.shape[-2], metric.shape[-1])
    total = jnp.zeros((rows, cols, padded.shape[-1]), jnp.float32)
    for stencil in range(9):
        row_off = stencil // 3
        col_off = stencil % 3
        total = (
            total
            + metric[stencil, :, :, None]
            * padded[row_off : row_off + rows, col_off : col_off + cols, :]
        )
    return total.astype(jnp.bfloat16)


def project(values, weight):
    shape = values.shape
    flat = values.reshape(-1, shape[-1])
    return (
        jnp.dot(flat, weight, preferred_element_type=jnp.float32)
        .astype(jnp.bfloat16)
        .reshape(shape[:-1] + (weight.shape[1],))
    )


def attention_kernel(
    q_ref, kc_ref, kr_ref, vc_ref, vr_ref, lat_hbm, wo_hbm, out_ref, att_ref, k_ref, v_ref,
    lat_ref, wo_ref, sems,
):
    lat_copy = pltpu.make_async_copy(lat_hbm, lat_ref, sems.at[0])
    wo_copy = pltpu.make_async_copy(wo_hbm, wo_ref, sems.at[1])
    lat_copy.start()
    wo_copy.start()
    middle = kc_ref.shape[0]
    k_ref[pl.ds(0, middle)] = kc_ref[...]
    k_ref[pl.ds(middle, kr_ref.shape[0])] = kr_ref[...]
    v_ref[pl.ds(0, middle)] = vc_ref[...]
    v_ref[pl.ds(middle, vr_ref.shape[0])] = vr_ref[...]
    cells, channels = q_ref.shape
    positions = k_ref.shape[0]
    rows, cols = lat_ref.shape[0], lat_ref.shape[1]
    wide = cols + 2 * RADIUS
    span = 2 * RADIUS + 1
    head_size = channels // HEADS
    group = 128
    cell = lax.broadcasted_iota(jnp.int32, (cells, positions), 0)
    place = lax.broadcasted_iota(jnp.int32, (cells, positions), 1)
    rim_rows = RADIUS * wide
    rows_total = lat_ref.shape[0] + 2 * RADIUS
    key_row = jnp.where(
        place < middle,
        place // wide + RADIUS,
        jnp.where(
            place < middle + rim_rows,
            (place - middle) // wide,
            (place - middle - rim_rows) // wide + rows_total - RADIUS,
        ),
    )
    key_row = jnp.where(place < middle + 2 * rim_rows, key_row, rows_total + span)
    key_col = jnp.where(place < middle, place % wide, (place - middle) % wide)
    row_gap = key_row - cell // cols
    col_gap = key_col - cell % cols
    valid = (row_gap >= 0) & (row_gap < span) & (col_gap >= 0) & (col_gap < span)
    lane = lax.broadcasted_iota(jnp.int32, (cells, group), 1) // head_size
    for g in range(channels // group):
        lanes = slice(g * group, (g + 1) * group)
        q_g = q_ref[:, lanes]
        k_g = k_ref[:, lanes]
        v_g = v_ref[:, lanes]
        acc = jnp.zeros((cells, group), jnp.float32)
        for part in range(group // head_size):
            q_h = jnp.where(lane == part, q_g, jnp.zeros_like(q_g))
            s = lax.dot_general(
                q_h, k_g, (((1,), (1,)), ((), ())), preferred_element_type=jnp.float32
            )
            s = jnp.where(valid, s, -jnp.inf)
            top = jnp.max(s, axis=1, keepdims=True)
            e = jnp.exp(s - top)
            total = jnp.sum(e, axis=1, keepdims=True)
            w = (e / total).astype(jnp.bfloat16)
            o = jnp.dot(w, v_g, preferred_element_type=jnp.float32)
            acc = jnp.where(lane == part, o, acc)
        att_ref[:, lanes] = acc.astype(jnp.bfloat16)
    wo_copy.wait()
    lat_copy.wait()
    mixed = jnp.dot(att_ref[...], wo_ref[...], preferred_element_type=jnp.float32)
    lat = lat_ref[...].reshape(cells, channels)
    out_ref[...] = (lat.astype(jnp.float32) + mixed).astype(out_ref.dtype)


def attend_and_mix(query, center, rims, w_key, w_value, own_tile, w_output):
    rows, cols, channels = own_tile.shape
    cells = rows * cols
    center_flat = center.reshape(-1, channels)
    rim_flat = rims.reshape(-1, channels)
    count = center_flat.shape[0] + rim_flat.shape[0]
    positions = -(-count // 128) * 128
    rim_flat = jnp.pad(rim_flat, ((0, positions - count), (0, 0)))
    vmem = pl.BlockSpec(memory_space=pltpu.VMEM)
    out = pl.pallas_call(
        attention_kernel,
        out_shape=jax.ShapeDtypeStruct((cells, channels), own_tile.dtype),
        in_specs=[vmem] * 5 + [pl.BlockSpec(memory_space=pl.ANY)] * 2,
        out_specs=vmem,
        scratch_shapes=[
            pltpu.VMEM((cells, channels), jnp.bfloat16),
            pltpu.VMEM((positions, channels), jnp.bfloat16),
            pltpu.VMEM((positions, channels), jnp.bfloat16),
            pltpu.VMEM(own_tile.shape, own_tile.dtype),
            pltpu.VMEM(w_output.shape, w_output.dtype),
            pltpu.SemaphoreType.DMA((2,)),
        ],
    )(
        query.reshape(cells, channels) * jnp.asarray((channels // HEADS) ** (-0.5), query.dtype),
        project(center_flat, w_key),
        project(rim_flat, w_key),
        project(center_flat, w_value),
        project(rim_flat, w_value),
        own_tile,
        w_output,
    )
    return out.reshape(rows, cols, channels)


def widen_tiles(field, margin):
    west = jnp.roll(field, 1, axis=0)[:, :, -margin:]
    east = jnp.roll(field, -1, axis=0)[:, :, :margin]
    return jnp.concatenate([west, field, east], axis=2)


def pick_all(table, edges):
    number = edges.shape[0]
    tile_hit = jnp.arange(number, dtype=jnp.int32) == table[..., 0:1]
    edge_hit = jnp.arange(2, dtype=jnp.int32) == table[..., 1:2]
    chosen = (tile_hit[..., :, None] & edge_hit[..., None, :]).astype(edges.dtype)
    got = jnp.einsum("...nf,nfrwc->...rwc", chosen, edges, preferred_element_type=jnp.float32)
    return got.astype(edges.dtype)


def doubling_gather(block, axis, radix=4):
    count = lax.axis_size(axis)
    if count & (count - 1):
        return lax.all_gather(block, axis, axis=0, tiled=True)
    me = lax.axis_index(axis)
    levels = []
    stride = 1
    while stride < count:
        r = min(radix, count // stride)
        levels.append((stride, r))
        stride *= r
    held = block
    for stride, r in reversed(levels):
        got = [held]
        for d in range(1, r):
            got.append(lax.ppermute(held, axis, [(i, i ^ (d * stride)) for i in range(count)]))
        digit = (me // stride) % r
        held = jnp.take(jnp.stack(got), digit ^ jnp.arange(r, dtype=jnp.int32), axis=0)
    depth = len(levels)
    held = jnp.transpose(held, tuple(reversed(range(depth))) + tuple(range(depth, held.ndim)))
    return held.reshape((count * block.shape[0],) + block.shape[1:])


def local(latents, norm_gain, metric, w_query, w_key, w_value, w_output, seam_table):
    own_tile = latents[0]
    channels = own_tile.shape[-1]
    normed = normalize(own_tile, norm_gain)
    margin = 1
    seam_rows = seam_table[0]
    widened = padded_2(normed[None], (("blk", 2),), margin)
    rows1 = jnp.stack([normed[0], normed[-1]])
    got1 = doubling_gather(rows1[None], "blk")
    count = got1.shape[0]
    near1 = jnp.stack(
        [seam_rows.at[:, 0].set((seam_rows[:, 0] + count + k) % count) for k in (-1, 0, 1)], axis=1
    )
    picked1 = pick_all(near1, got1[:, :, None])
    received = jnp.concatenate(
        [picked1[:, 0, :, -1:], picked1[:, 1], picked1[:, 2, :, :1]], axis=2
    )
    padded = place_rims(widened[0], received, seam_rows)
    smoothed = smooth(padded, metric[0])
    query = project(smoothed, w_query)
    field_wide = padded_2(smoothed[None], (("blk", 2),), RADIUS)
    rows3 = jnp.concatenate([smoothed[:RADIUS], smoothed[-RADIUS:]], axis=0)
    got3 = doubling_gather(rows3[None], "blk")
    count = got3.shape[0]
    edges3 = got3.reshape((count, 2, RADIUS) + got3.shape[2:])
    near = jnp.stack(
        [seam_rows.at[:, 0].set((seam_rows[:, 0] + count + k) % count) for k in (-1, 0, 1)], axis=1
    )
    picked = pick_all(near, edges3)
    field_got = jnp.concatenate(
        [picked[:, 0, :, -RADIUS:], picked[:, 1], picked[:, 2, :, :RADIUS]], axis=2
    )
    arrived = orient_rims(field_got, seam_rows)
    return attend_and_mix(query, field_wide[0], arrived, w_key, w_value, own_tile, w_output)[None]


def solution(mesh):
    return jax.shard_map(
        local,
        mesh=mesh,
        in_specs=(
            P(("group", "blk"), None, None, None),
            P(),
            P("blk", None, None, None),
            P(),
            P(),
            P(),
            P(),
            P("blk", None, None),
        ),
        out_specs=P(("group", "blk"), None, None, None),
        check_vma=False,
    )
```

```python
import jax
import jax.numpy as jnp
from jax import lax
from jax.sharding import PartitionSpec as P
from jax.experimental import pallas as pl
from jax.experimental.pallas import tpu as pltpu

HEADS = 8
RADIUS = 3


def padded_2(array, sides, width):
    for axis, dim in sides:
        count, length = (lax.axis_size(axis), array.shape[dim])
        up = [(i, (i + 1) % count) for i in range(count)]
        down = [(j, i) for i, j in up]
        last = lax.slice_in_dim(array, length - width, length, axis=dim)
        first = lax.slice_in_dim(array, 0, width, axis=dim)
        before = lax.ppermute(last, axis, up)
        after = lax.ppermute(first, axis, down)
        array = jnp.concatenate([before, array, after], axis=dim)
    return array


def normalize(latents, norm_gain):
    values = latents.astype(jnp.float32)
    factor = lax.rsqrt(jnp.mean(values * values, axis=-1, keepdims=True) + 1e-05)
    return (values * factor * norm_gain).astype(jnp.bfloat16)


def pick_rims(seam_rows, piece):
    number = piece.shape[0]
    tile_ids = jnp.arange(number, dtype=jnp.int32)
    tile_hit = tile_ids[None, :] == seam_rows[:, 0:1]
    edge_hit = jnp.arange(2, dtype=jnp.int32)[None, :] == seam_rows[:, 1:2]
    chosen = (tile_hit[:, :, None] & edge_hit[:, None, :]).astype(piece.dtype)
    return jnp.einsum("enf,nfrwc->erwc", chosen, piece, preferred_element_type=jnp.float32)


def edge_rows(widened, margin):
    return jnp.stack([widened[:, :margin], widened[:, -margin:]], axis=1)


def orient_rims(received, seam_pair):
    arrived = received.astype(jnp.bfloat16)
    orient = seam_pair[:, 2]
    flip_along = (orient % 2 == 1)[:, None, None, None]
    arrived = jnp.where(flip_along, arrived[:, :, ::-1], arrived)
    flip_across = (orient // 2 == 1)[:, None, None, None]
    return jnp.where(flip_across, arrived[:, ::-1], arrived)


def place_rims(widened, received, seam_pair):
    arrived = orient_rims(received, seam_pair)
    return jnp.concatenate([arrived[0], widened, arrived[1]], axis=0)


def smooth(padded, metric):
    rows, cols = (metric.shape[-2], metric.shape[-1])
    total = jnp.zeros((rows, cols, padded.shape[-1]), jnp.float32)
    for stencil in range(9):
        row_off = stencil // 3
        col_off = stencil % 3
        total = (
            total
            + metric[stencil, :, :, None]
            * padded[row_off : row_off + rows, col_off : col_off + cols, :]
        )
    return total.astype(jnp.bfloat16)


def project(values, weight):
    shape = values.shape
    flat = values.reshape(-1, shape[-1])
    return (
        jnp.dot(flat, weight, preferred_element_type=jnp.float32)
        .astype(jnp.bfloat16)
        .reshape(shape[:-1] + (weight.shape[1],))
    )


def attention_kernel(
    q_ref, kc_ref, kr_ref, vc_ref, vr_ref, lat_ref, wo_ref, out_ref, att_ref, k_ref, v_ref
):
    middle = kc_ref.shape[0]
    k_ref[pl.ds(0, middle)] = kc_ref[...]
    k_ref[pl.ds(middle, kr_ref.shape[0])] = kr_ref[...]
    v_ref[pl.ds(0, middle)] = vc_ref[...]
    v_ref[pl.ds(middle, vr_ref.shape[0])] = vr_ref[...]
    cells, channels = q_ref.shape
    positions = k_ref.shape[0]
    rows, cols = lat_ref.shape[0], lat_ref.shape[1]
    wide = cols + 2 * RADIUS
    span = 2 * RADIUS + 1
    head_size = channels // HEADS
    group = 128
    cell = lax.broadcasted_iota(jnp.int32, (cells, positions), 0)
    place = lax.broadcasted_iota(jnp.int32, (cells, positions), 1)
    rim_rows = RADIUS * wide
    rows_total = lat_ref.shape[0] + 2 * RADIUS
    key_row = jnp.where(
        place < middle,
        place // wide + RADIUS,
        jnp.where(
            place < middle + rim_rows,
            (place - middle) // wide,
            (place - middle - rim_rows) // wide + rows_total - RADIUS,
        ),
    )
    key_row = jnp.where(place < middle + 2 * rim_rows, key_row, rows_total + span)
    key_col = jnp.where(place < middle, place % wide, (place - middle) % wide)
    row_gap = key_row - cell // cols
    col_gap = key_col - cell % cols
    valid = (row_gap >= 0) & (row_gap < span) & (col_gap >= 0) & (col_gap < span)
    lane = lax.broadcasted_iota(jnp.int32, (cells, group), 1) // head_size
    for g in range(channels // group):
        lanes = slice(g * group, (g + 1) * group)
        q_g = q_ref[:, lanes]
        k_g = k_ref[:, lanes]
        v_g = v_ref[:, lanes]
        acc = jnp.zeros((cells, group), jnp.float32)
        for part in range(group // head_size):
            q_h = jnp.where(lane == part, q_g, jnp.zeros_like(q_g))
            s = lax.dot_general(
                q_h, k_g, (((1,), (1,)), ((), ())), preferred_element_type=jnp.float32
            )
            s = jnp.where(valid, s, -jnp.inf)
            top = jnp.max(s, axis=1, keepdims=True)
            e = jnp.exp(s - top)
            total = jnp.sum(e, axis=1, keepdims=True)
            w = (e / total).astype(jnp.bfloat16)
            o = jnp.dot(w, v_g, preferred_element_type=jnp.float32)
            acc = jnp.where(lane == part, o, acc)
        att_ref[:, lanes] = acc.astype(jnp.bfloat16)
    mixed = jnp.dot(att_ref[...], wo_ref[...], preferred_element_type=jnp.float32)
    lat = lat_ref[...].reshape(cells, channels)
    out_ref[...] = (lat.astype(jnp.float32) + mixed).astype(out_ref.dtype)


def attend_and_mix(query, center, rims, w_key, w_value, own_tile, w_output):
    rows, cols, channels = own_tile.shape
    cells = rows * cols
    center_flat = center.reshape(-1, channels)
    rim_flat = rims.reshape(-1, channels)
    count = center_flat.shape[0] + rim_flat.shape[0]
    positions = -(-count // 128) * 128
    rim_flat = jnp.pad(rim_flat, ((0, positions - count), (0, 0)))
    vmem = pl.BlockSpec(memory_space=pltpu.VMEM)
    out = pl.pallas_call(
        attention_kernel,
        out_shape=jax.ShapeDtypeStruct((cells, channels), own_tile.dtype),
        in_specs=[vmem] * 7,
        out_specs=vmem,
        scratch_shapes=[
            pltpu.VMEM((cells, channels), jnp.bfloat16),
            pltpu.VMEM((positions, channels), jnp.bfloat16),
            pltpu.VMEM((positions, channels), jnp.bfloat16),
        ],
    )(
        query.reshape(cells, channels) * jnp.asarray((channels // HEADS) ** (-0.5), query.dtype),
        project(center_flat, w_key),
        project(rim_flat, w_key),
        project(center_flat, w_value),
        project(rim_flat, w_value),
        own_tile,
        w_output,
    )
    return out.reshape(rows, cols, channels)


def widen_tiles(field, margin):
    west = jnp.roll(field, 1, axis=0)[:, :, -margin:]
    east = jnp.roll(field, -1, axis=0)[:, :, :margin]
    return jnp.concatenate([west, field, east], axis=2)


def pick_all(table, edges):
    number = edges.shape[0]
    tile_hit = jnp.arange(number, dtype=jnp.int32) == table[..., 0:1]
    edge_hit = jnp.arange(2, dtype=jnp.int32) == table[..., 1:2]
    chosen = (tile_hit[..., :, None] & edge_hit[..., None, :]).astype(edges.dtype)
    got = jnp.einsum("...nf,nfrwc->...rwc", chosen, edges, preferred_element_type=jnp.float32)
    return got.astype(edges.dtype)


def doubling_gather(block, axis, radix=4):
    count = lax.axis_size(axis)
    if count & (count - 1):
        return lax.all_gather(block, axis, axis=0, tiled=True)
    me = lax.axis_index(axis)
    levels = []
    stride = 1
    while stride < count:
        r = min(radix, count // stride)
        levels.append((stride, r))
        stride *= r
    held = block
    for stride, r in reversed(levels):
        got = [held]
        for d in range(1, r):
            got.append(lax.ppermute(held, axis, [(i, i ^ (d * stride)) for i in range(count)]))
        digit = (me // stride) % r
        held = jnp.take(jnp.stack(got), digit ^ jnp.arange(r, dtype=jnp.int32), axis=0)
    depth = len(levels)
    held = jnp.transpose(held, tuple(reversed(range(depth))) + tuple(range(depth, held.ndim)))
    return held.reshape((count * block.shape[0],) + block.shape[1:])


def raw_gather(block, axis, radix=4):
    count = lax.axis_size(axis)
    me = lax.axis_index(axis)
    if count & (count - 1):
        return lax.all_gather(block[None], axis, axis=0, tiled=True), (lambda j: j)
    levels = []
    stride = 1
    while stride < count:
        r = min(radix, count // stride)
        levels.append((stride, r))
        stride *= r
    held = block
    for stride, r in reversed(levels):
        got = [held]
        for d in range(1, r):
            got.append(lax.ppermute(held, axis, [(i, i ^ (d * stride)) for i in range(count)]))
        held = jnp.stack(got)

    def locate(j):
        gap = j ^ me
        flat = 0
        for stride, r in levels:
            flat = flat * r + (gap // stride) % r
        return flat

    return held.reshape((count,) + block.shape), locate


def local(latents, norm_gain, metric, w_query, w_key, w_value, w_output, seam_table):
    own_tile = latents[0]
    channels = own_tile.shape[-1]
    normed = normalize(own_tile, norm_gain)
    margin = 1
    seam_rows = seam_table[0]
    widened = padded_2(normed[None], (("blk", 2),), margin)
    rows1 = jnp.stack([normed[0], normed[-1]])
    got1 = doubling_gather(rows1[None], "blk")
    count = got1.shape[0]
    near1 = jnp.stack(
        [seam_rows.at[:, 0].set((seam_rows[:, 0] + count + k) % count) for k in (-1, 0, 1)], axis=1
    )
    picked1 = pick_all(near1, got1[:, :, None])
    received = jnp.concatenate(
        [picked1[:, 0, :, -1:], picked1[:, 1], picked1[:, 2, :, :1]], axis=2
    )
    padded = place_rims(widened[0], received, seam_rows)
    smoothed = smooth(padded, metric[0])
    query = project(smoothed, w_query)
    field_wide = padded_2(smoothed[None], (("blk", 2),), RADIUS)
    rows3 = jnp.concatenate([smoothed[:RADIUS], smoothed[-RADIUS:]], axis=0)
    got3, locate3 = raw_gather(rows3, "blk")
    count = got3.shape[0]
    edges3 = got3.reshape((count, 2, RADIUS) + got3.shape[2:])
    near = jnp.stack(
        [seam_rows.at[:, 0].set(locate3((seam_rows[:, 0] + count + k) % count)) for k in (-1, 0, 1)],
        axis=1,
    )
    picked = pick_all(near, edges3)
    field_got = jnp.concatenate(
        [picked[:, 0, :, -RADIUS:], picked[:, 1], picked[:, 2, :, :RADIUS]], axis=2
    )
    arrived = orient_rims(field_got, seam_rows)
    return attend_and_mix(query, field_wide[0], arrived, w_key, w_value, own_tile, w_output)[None]


def solution(mesh):
    return jax.shard_map(
        local,
        mesh=mesh,
        in_specs=(
            P(("group", "blk"), None, None, None),
            P(),
            P("blk", None, None, None),
            P(),
            P(),
            P(),
            P(),
            P("blk", None, None),
        ),
        out_specs=P(("group", "blk"), None, None, None),
        check_vma=False,
    )
```

```python
import jax
import jax.numpy as jnp
from jax import lax
from jax.sharding import PartitionSpec as P
from jax.experimental import pallas as pl
from jax.experimental.pallas import tpu as pltpu

HEADS = 8
RADIUS = 3


def padded_2(array, sides, width):
    for axis, dim in sides:
        count, length = (lax.axis_size(axis), array.shape[dim])
        up = [(i, (i + 1) % count) for i in range(count)]
        down = [(j, i) for i, j in up]
        last = lax.slice_in_dim(array, length - width, length, axis=dim)
        first = lax.slice_in_dim(array, 0, width, axis=dim)
        before = lax.ppermute(last, axis, up)
        after = lax.ppermute(first, axis, down)
        array = jnp.concatenate([before, array, after], axis=dim)
    return array


def normalize(latents, norm_gain):
    values = latents.astype(jnp.float32)
    factor = lax.rsqrt(jnp.mean(values * values, axis=-1, keepdims=True) + 1e-05)
    return (values * factor * norm_gain).astype(jnp.bfloat16)


def pick_rims(seam_rows, piece):
    number = piece.shape[0]
    tile_ids = jnp.arange(number, dtype=jnp.int32)
    tile_hit = tile_ids[None, :] == seam_rows[:, 0:1]
    edge_hit = jnp.arange(2, dtype=jnp.int32)[None, :] == seam_rows[:, 1:2]
    chosen = (tile_hit[:, :, None] & edge_hit[:, None, :]).astype(piece.dtype)
    return jnp.einsum("enf,nfrwc->erwc", chosen, piece, preferred_element_type=jnp.float32)


def edge_rows(widened, margin):
    return jnp.stack([widened[:, :margin], widened[:, -margin:]], axis=1)


def orient_rims(received, seam_pair):
    arrived = received.astype(jnp.bfloat16)
    orient = seam_pair[:, 2]
    flip_along = (orient % 2 == 1)[:, None, None, None]
    arrived = jnp.where(flip_along, arrived[:, :, ::-1], arrived)
    flip_across = (orient // 2 == 1)[:, None, None, None]
    return jnp.where(flip_across, arrived[:, ::-1], arrived)


def place_rims(widened, received, seam_pair):
    arrived = orient_rims(received, seam_pair)
    return jnp.concatenate([arrived[0], widened, arrived[1]], axis=0)


def smooth(padded, metric):
    rows, cols = (metric.shape[-2], metric.shape[-1])
    total = jnp.zeros((rows, cols, padded.shape[-1]), jnp.float32)
    for stencil in range(9):
        row_off = stencil // 3
        col_off = stencil % 3
        total = (
            total
            + metric[stencil, :, :, None]
            * padded[row_off : row_off + rows, col_off : col_off + cols, :]
        )
    return total.astype(jnp.bfloat16)


def project(values, weight):
    shape = values.shape
    flat = values.reshape(-1, shape[-1])
    return (
        jnp.dot(flat, weight, preferred_element_type=jnp.float32)
        .astype(jnp.bfloat16)
        .reshape(shape[:-1] + (weight.shape[1],))
    )


def attention_kernel(
    q_ref, kc_ref, kr_ref, vc_ref, vr_ref, lat_ref, wo_ref, out_ref, att_ref, k_ref, v_ref
):
    middle = kc_ref.shape[0]
    k_ref[pl.ds(0, middle)] = kc_ref[...]
    k_ref[pl.ds(middle, kr_ref.shape[0])] = kr_ref[...]
    v_ref[pl.ds(0, middle)] = vc_ref[...]
    v_ref[pl.ds(middle, vr_ref.shape[0])] = vr_ref[...]
    cells, channels = q_ref.shape
    positions = k_ref.shape[0]
    rows, cols = lat_ref.shape[0], lat_ref.shape[1]
    wide = cols + 2 * RADIUS
    span = 2 * RADIUS + 1
    head_size = channels // HEADS
    group = 128
    cell = lax.broadcasted_iota(jnp.int32, (cells, positions), 0)
    place = lax.broadcasted_iota(jnp.int32, (cells, positions), 1)
    rim_rows = RADIUS * wide
    rows_total = lat_ref.shape[0] + 2 * RADIUS
    key_row = jnp.where(
        place < middle,
        place // wide + RADIUS,
        jnp.where(
            place < middle + rim_rows,
            (place - middle) // wide,
            (place - middle - rim_rows) // wide + rows_total - RADIUS,
        ),
    )
    key_row = jnp.where(place < middle + 2 * rim_rows, key_row, rows_total + span)
    key_col = jnp.where(place < middle, place % wide, (place - middle) % wide)
    row_gap = key_row - cell // cols
    col_gap = key_col - cell % cols
    valid = (row_gap >= 0) & (row_gap < span) & (col_gap >= 0) & (col_gap < span)
    lane = lax.broadcasted_iota(jnp.int32, (cells, group), 1) // head_size
    for g in range(channels // group):
        lanes = slice(g * group, (g + 1) * group)
        q_g = q_ref[:, lanes]
        k_g = k_ref[:, lanes]
        v_g = v_ref[:, lanes]
        acc = jnp.zeros((cells, group), jnp.float32)
        for part in range(group // head_size):
            q_h = jnp.where(lane == part, q_g, jnp.zeros_like(q_g))
            s = lax.dot_general(
                q_h, k_g, (((1,), (1,)), ((), ())), preferred_element_type=jnp.float32
            )
            s = jnp.where(valid, s, -jnp.inf)
            top = jnp.max(s, axis=1, keepdims=True)
            e = jnp.exp(s - top)
            total = jnp.sum(e, axis=1, keepdims=True)
            w = (e / total).astype(jnp.bfloat16)
            o = jnp.dot(w, v_g, preferred_element_type=jnp.float32)
            acc = jnp.where(lane == part, o, acc)
        att_ref[:, lanes] = acc.astype(jnp.bfloat16)
    mixed = jnp.dot(att_ref[...], wo_ref[...], preferred_element_type=jnp.float32)
    lat = lat_ref[...].reshape(cells, channels)
    out_ref[...] = (lat.astype(jnp.float32) + mixed).astype(out_ref.dtype)


def attend_and_mix(query, center, rims, w_key, w_value, own_tile, w_output):
    rows, cols, channels = own_tile.shape
    cells = rows * cols
    center_flat = center.reshape(-1, channels)
    rim_flat = rims.reshape(-1, channels)
    count = center_flat.shape[0] + rim_flat.shape[0]
    positions = -(-count // 128) * 128
    rim_flat = jnp.pad(rim_flat, ((0, positions - count), (0, 0)))
    vmem = pl.BlockSpec(memory_space=pltpu.VMEM)
    out = pl.pallas_call(
        attention_kernel,
        out_shape=jax.ShapeDtypeStruct((cells, channels), own_tile.dtype),
        in_specs=[vmem] * 7,
        out_specs=vmem,
        scratch_shapes=[
            pltpu.VMEM((cells, channels), jnp.bfloat16),
            pltpu.VMEM((positions, channels), jnp.bfloat16),
            pltpu.VMEM((positions, channels), jnp.bfloat16),
        ],
    )(
        query.reshape(cells, channels) * jnp.asarray((channels // HEADS) ** (-0.5), query.dtype),
        project(center_flat, w_key),
        project(rim_flat, w_key),
        project(center_flat, w_value),
        project(rim_flat, w_value),
        own_tile,
        w_output,
    )
    return out.reshape(rows, cols, channels)


def widen_tiles(field, margin):
    west = jnp.roll(field, 1, axis=0)[:, :, -margin:]
    east = jnp.roll(field, -1, axis=0)[:, :, :margin]
    return jnp.concatenate([west, field, east], axis=2)


def pick_all(table, edges):
    number = edges.shape[0]
    tile_hit = jnp.arange(number, dtype=jnp.int32) == table[..., 0:1]
    edge_hit = jnp.arange(2, dtype=jnp.int32) == table[..., 1:2]
    chosen = (tile_hit[..., :, None] & edge_hit[..., None, :]).astype(edges.dtype)
    got = jnp.einsum("...nf,nfrwc->...rwc", chosen, edges, preferred_element_type=jnp.float32)
    return got.astype(edges.dtype)


def doubling_gather(block, axis, radix=4):
    count = lax.axis_size(axis)
    if count & (count - 1):
        return lax.all_gather(block, axis, axis=0, tiled=True)
    me = lax.axis_index(axis)
    levels = []
    stride = 1
    while stride < count:
        r = min(radix, count // stride)
        levels.append((stride, r))
        stride *= r
    held = block
    for stride, r in reversed(levels):
        got = [held]
        for d in range(1, r):
            got.append(lax.ppermute(held, axis, [(i, i ^ (d * stride)) for i in range(count)]))
        digit = (me // stride) % r
        held = jnp.take(jnp.stack(got), digit ^ jnp.arange(r, dtype=jnp.int32), axis=0)
    depth = len(levels)
    held = jnp.transpose(held, tuple(reversed(range(depth))) + tuple(range(depth, held.ndim)))
    return held.reshape((count * block.shape[0],) + block.shape[1:])


def raw_gather(block, axis, radix=4):
    count = lax.axis_size(axis)
    me = lax.axis_index(axis)
    if count & (count - 1):
        return lax.all_gather(block[None], axis, axis=0, tiled=True), (lambda j: j)
    levels = []
    stride = 1
    while stride < count:
        r = min(radix, count // stride)
        levels.append((stride, r))
        stride *= r
    held = block
    for stride, r in reversed(levels):
        got = [held]
        for d in range(1, r):
            got.append(lax.ppermute(held, axis, [(i, i ^ (d * stride)) for i in range(count)]))
        held = jnp.stack(got)

    def locate(j):
        gap = j ^ me
        flat = 0
        for stride, r in levels:
            flat = flat * r + (gap // stride) % r
        return flat

    return held.reshape((count,) + block.shape), locate


def local(latents, norm_gain, metric, w_query, w_key, w_value, w_output, seam_table):
    own_tile = latents[0]
    channels = own_tile.shape[-1]
    normed = normalize(own_tile, norm_gain)
    margin = 1
    seam_rows = seam_table[0]
    widened = padded_2(normed[None], (("blk", 2),), margin)
    rows1 = jnp.stack([normed[0], normed[-1]])
    got1, locate1 = raw_gather(rows1, "blk")
    count = got1.shape[0]
    near1 = jnp.stack(
        [seam_rows.at[:, 0].set(locate1((seam_rows[:, 0] + count + k) % count)) for k in (-1, 0, 1)],
        axis=1,
    )
    picked1 = pick_all(near1, got1[:, :, None])
    received = jnp.concatenate(
        [picked1[:, 0, :, -1:], picked1[:, 1], picked1[:, 2, :, :1]], axis=2
    )
    padded = place_rims(widened[0], received, seam_rows)
    smoothed = smooth(padded, metric[0])
    query = project(smoothed, w_query)
    field_wide = padded_2(smoothed[None], (("blk", 2),), RADIUS)
    rows3 = jnp.concatenate([smoothed[:RADIUS], smoothed[-RADIUS:]], axis=0)
    got3, locate3 = raw_gather(rows3, "blk")
    count = got3.shape[0]
    edges3 = got3.reshape((count, 2, RADIUS) + got3.shape[2:])
    near = jnp.stack(
        [seam_rows.at[:, 0].set(locate3((seam_rows[:, 0] + count + k) % count)) for k in (-1, 0, 1)],
        axis=1,
    )
    picked = pick_all(near, edges3)
    field_got = jnp.concatenate(
        [picked[:, 0, :, -RADIUS:], picked[:, 1], picked[:, 2, :, :RADIUS]], axis=2
    )
    arrived = orient_rims(field_got, seam_rows)
    return attend_and_mix(query, field_wide[0], arrived, w_key, w_value, own_tile, w_output)[None]


def solution(mesh):
    return jax.shard_map(
        local,
        mesh=mesh,
        in_specs=(
            P(("group", "blk"), None, None, None),
            P(),
            P("blk", None, None, None),
            P(),
            P(),
            P(),
            P(),
            P("blk", None, None),
        ),
        out_specs=P(("group", "blk"), None, None, None),
        check_vma=False,
    )
```
